128 devices in a mesh: bx: 8 (over z, core), by: 16 (over x, y).
Axes of the slice: x: 4, y: 4, z: 4, core: 2. Of those that a mesh axis runs over, the one named last changes fastest.
Arguments:
- adjoint_source: float32 [5, 32, 64, 512], P(None, 'bx', 'by'), may hold values from -5 to 5
- initial: float32 [5, 32, 64, 512], P(None, 'bx', 'by'), may hold values from -6 to 6
- inverses: float32 [5, 5, 32, 64, 512], P(None, None, 'bx', 'by'), may hold values from -0.23 to 0.48
- couplings: bfloat16 [6, 5, 5, 32, 64, 512], P(None, None, None, 'bx', 'by'), may hold values from -3.7 to 1.3
- interface_tiles: float32 [128, 5, 5, 256], P(('bx', 'by')), may hold values from -2.5 to 2.5
- source_cells: int32 [128, 256], P(('bx', 'by')), may hold values from 0 to 8191
- target_cells: int32 [128, 256], P(('bx', 'by')), may hold values from 0 to 8191
- tile_counts: int32 [128, 128], P(('bx', 'by')), may hold values from 1 to 2, as said below
Outputs:
- adjoint: float32 [5, 32, 64, 512], P(None, 'bx', 'by')
The draws below stay inside these ranges and needn't reach their ends.
Inputs may be any that keep to these rules, and one draw needn't show every extreme that they name: Slots k of the group of receiving block d with k < tile_counts[o, d] hold tiles; the others are padding. In every draw one receiving block gets 2 tiles from every block.
All inputs are finite; a program needn't handle non-finite values.
Results may differ from the reference program's by a relative error of at most 0.0003.
Values sent between devices are 32-bit elements; how exact they have to be, the bound alone decides.
No kernel may reach another device: no remote copies, remote signals or barrier semaphores. Data moves between devices by JAX's collectives and lax.ppermute only.
A program may use at most 64 MiB of HBM per device.

```python
import jax
import jax.numpy as jnp
import numpy as np
from jax import lax

VARS = 5
CX = 4
CY = 4
CZ = 512
ITERS = 2
CAP = 2
BLOCKS = 128
SLOTS = 256
NX = 32
NY = 64
NZ = 512
N_BX = 8
N_BY = 16


def draw_adjoint_source(key, part):
    values = jax.random.normal(key, (VARS, NX, NY, NZ), jnp.float32)
    return jnp.clip(values, -5.0, 5.0)


def draw_inverses(key, part):
    noise = jnp.clip(jax.random.normal(key, (VARS, VARS, NX, NY, NZ), jnp.float32), -4.0, 4.0)
    identity = jnp.eye(VARS, dtype=jnp.float32)[:, :, None, None, None]
    return 0.25 * (identity + 0.22 * noise)


def draw_couplings(key, part):
    key_rate, key_noise = jax.random.split(key)
    rates = jax.random.uniform(key_rate, (6, 1, 1, NX, NY, NZ), jnp.float32, 0.29, 0.58)
    strong = [1.0, 1.0, 1.0, 0.06, 0.06]
    weak = [0.06, 0.06, 0.06, 1.0, 1.0]
    table = np.array([strong, weak, strong, weak, [0.2] * 5, [0.2] * 5], dtype=np.float32)
    diagonal = jnp.asarray(table)[:, :, None] * jnp.eye(VARS, dtype=jnp.float32)[None]
    noise = jnp.clip(jax.random.normal(key_noise, (6, VARS, VARS, NX, NY, NZ), jnp.float32), -4.0, 4.0)
    return (-4.0 * (rates * diagonal[:, :, :, None, None, None] + 0.08 * noise)).astype(jnp.bfloat16)


def draw_tile_counts(key, part):
    key_main, key_full = jax.random.split(key)
    counts = jax.random.randint(key_main, (BLOCKS, BLOCKS), 1, CAP + 1, dtype=jnp.int32)
    chosen = jax.random.randint(key_full, (), 0, BLOCKS, dtype=jnp.int32)
    column = jnp.arange(BLOCKS, dtype=jnp.int32)[None, :]
    counts = jnp.where(column == chosen, CAP, counts)
    counts = jnp.where(column == (chosen + 1) % BLOCKS, 1, counts)
    return counts


def set_ends(entries, key, least, top_value):
    spot = [jax.random.randint(jax.random.fold_in(key, axis), (), 0, length) for axis, length in enumerate(entries.shape)]
    main_axis = entries.shape.index(max(entries.shape))
    next_to = spot[:main_axis] + [(spot[main_axis] + 1) % entries.shape[main_axis]] + spot[main_axis + 1:]
    return entries.at[tuple(spot)].set(least).at[tuple(next_to)].set(top_value)


def block_levels(own_key, shape, cuts, least, largest):
    factor_of, own = 1.0, jax.random.fold_in(own_key, 6)
    for position, parts in cuts:
        steps = jnp.exp(jax.random.uniform(jax.random.fold_in(own, position), (parts,), jnp.float32, least / len(cuts), largest / len(cuts)))
        factor_of = factor_of * jnp.repeat(steps, shape[position] // parts).reshape([-1 if axis == position else 1 for axis in range(len(shape))])
    return factor_of


def centred(own_key, dims, spread, bound, cuts=(), kind=jnp.bfloat16):
    entries = spread * jax.random.normal(own_key, dims, jnp.float32)
    if cuts:
        entries = entries * block_levels(own_key, dims, cuts, -0.22, 0.18)
    return jnp.clip(entries, -bound, bound).astype(kind)


def setup_inputs(seed: int = 0) -> dict:
    keys = jax.random.split(jax.random.key(seed), 9)
    return {
        "adjoint_source": draw_adjoint_source(jax.random.fold_in(keys[8], 71), 0),
        "initial": centred(keys[1], (VARS, NX, NY, NZ), 1.0, 6.0, ((1, 8), (2, 16)), jnp.float32),
        "inverses": draw_inverses(jax.random.fold_in(keys[8], 71), 0),
        "couplings": draw_couplings(jax.random.fold_in(keys[8], 71), 0),
        "interface_tiles": centred(keys[4], (BLOCKS, VARS, VARS, SLOTS), VARS ** -0.5, 2.5, ((0, 128),), jnp.float32),
        "source_cells": set_ends(jax.random.randint(keys[5], (BLOCKS, SLOTS), 0, CX * CY * CZ), jax.random.fold_in(keys[5], 1), 0, (CX * CY * CZ) - 1).astype(jnp.int32),
        "target_cells": set_ends(jax.random.randint(keys[6], (BLOCKS, SLOTS), 0, CX * CY * CZ), jax.random.fold_in(keys[6], 1), 0, (CX * CY * CZ) - 1).astype(jnp.int32),
        "tile_counts": draw_tile_counts(jax.random.fold_in(keys[8], 71), 0),
    }


def matvec(matrix, vector):
    return jnp.sum(matrix.astype(jnp.float32) * vector[None], axis=1)


def neighbour(values, axis_at, offset):
    length = values.shape[axis_at]
    border = jnp.zeros_like(lax.slice_in_dim(values, 0, 1, axis=axis_at))
    if offset > 0:
        return jnp.concatenate([lax.slice_in_dim(values, 1, length, axis=axis_at), border], axis=axis_at)
    return jnp.concatenate([border, lax.slice_in_dim(values, 0, length - 1, axis=axis_at)], axis=axis_at)


def sweep_blocks(fixed, inverses, along_x, along_y, reverse):
    def plane_step(prev_plane, planes):
        fix_plane, inv_plane, kx_plane, ky_plane = planes

        def column(prev_column, columns):
            fix_col, inv_col, kx_col, ky_col, from_x = columns
            right = fix_col - matvec(kx_col, from_x) - matvec(ky_col, prev_column)
            fresh = matvec(inv_col, right)
            return fresh, fresh

        columns = (jnp.moveaxis(fix_plane, 1, 0), jnp.moveaxis(inv_plane, 2, 0),
                   jnp.moveaxis(kx_plane, 2, 0), jnp.moveaxis(ky_plane, 2, 0),
                   jnp.moveaxis(prev_plane, 1, 0))
        last_col, stacked = lax.scan(column, jnp.zeros((VARS, NZ), jnp.float32), columns, reverse=reverse)
        fresh_plane = jnp.moveaxis(stacked, 0, 1)
        return fresh_plane, fresh_plane

    planes = (jnp.moveaxis(fixed, 1, 0), jnp.moveaxis(inverses, 2, 0),
              jnp.moveaxis(along_x, 2, 0), jnp.moveaxis(along_y, 2, 0))
    last_plane, stacked = lax.scan(plane_step, jnp.zeros((VARS, NY, NZ), jnp.float32), planes, reverse=reverse)
    return jnp.moveaxis(stacked, 0, 1)


def to_blocks(values):
    shaped = values.reshape(VARS, N_BX, CX, N_BY, CY, CZ)
    shaped = jnp.transpose(shaped, (1, 3, 0, 2, 4, 5))
    return shaped.reshape(N_BX * N_BY, VARS, CX * CY * CZ)


def from_blocks(blocks):
    shaped = blocks.reshape(N_BX, N_BY, VARS, CX, CY, CZ)
    shaped = jnp.transpose(shaped, (2, 0, 3, 1, 4, 5))
    return shaped.reshape(VARS, NX, NY, NZ)


def interface(values, interface_tiles, source_cells, target_cells, tile_counts):
    blocks = to_blocks(values)
    index_all = jnp.broadcast_to(source_cells[:, None, :], (BLOCKS, VARS, SLOTS))
    picked = jnp.take_along_axis(blocks, index_all, axis=2)
    products = jnp.sum(interface_tiles * picked[:, None, :, :], axis=2)
    slot_ids = jnp.arange(SLOTS, dtype=jnp.int32)
    limits = jnp.repeat(tile_counts, CAP, axis=1)
    products = jnp.where((slot_ids % CAP)[None, None, :] < limits[:, None, :], products, 0.0)
    arrived = products.reshape(BLOCKS, VARS, BLOCKS, CAP).transpose(2, 1, 0, 3).reshape(BLOCKS, VARS, SLOTS)

    def place_sums(incoming, targets):
        return jnp.zeros((VARS, CX * CY * CZ), jnp.float32).at[:, targets].add(incoming)

    return from_blocks(jax.vmap(place_sums)(arrived, target_cells))


def reference(adjoint_source, initial, inverses, couplings, interface_tiles, source_cells, target_cells, tile_counts):
    iterate = initial
    for number in range(ITERS):
        inter = interface(iterate, interface_tiles, source_cells, target_cells, tile_counts)
        base = adjoint_source - inter
        lower_terms = (base - matvec(couplings[1], neighbour(iterate, 1, 1))
                       - matvec(couplings[3], neighbour(iterate, 2, 1))
                       - matvec(couplings[4], neighbour(iterate, 3, -1))
                       - matvec(couplings[5], neighbour(iterate, 3, 1)))
        half = sweep_blocks(lower_terms, inverses, couplings[0], couplings[2], False)
        upper_terms = (base - matvec(couplings[0], neighbour(half, 1, -1))
                       - matvec(couplings[2], neighbour(half, 2, -1))
                       - matvec(couplings[4], neighbour(half, 3, -1))
                       - matvec(couplings[5], neighbour(half, 3, 1)))
        iterate = sweep_blocks(upper_terms, inverses, couplings[1], couplings[3], True)
    return iterate
```

```python
import functools

import jax
import jax.numpy as jnp
from jax import lax
from jax.experimental import pallas as pl
from jax.experimental.pallas import tpu as pltpu
from jax.sharding import PartitionSpec as P

ITERS = 2
AXES = ("bx", "by")
ROWS = 8


def interface(iterate, interface_tiles, source_cells, target_cells, tile_counts):
    var_count = iterate.shape[0]
    flat_cells = iterate.reshape(var_count, -1)
    block_count = lax.axis_size("bx") * lax.axis_size("by")
    slot_count = source_cells.shape[1]
    per_pair = slot_count // block_count
    picked = jnp.take(flat_cells, source_cells[0], axis=1)
    products = jnp.sum(interface_tiles[0] * picked[None], axis=1)
    slot_ids = jnp.arange(slot_count, dtype=jnp.int32)
    limits = jnp.repeat(tile_counts[0], per_pair)
    products = jnp.where((slot_ids % per_pair)[None] < limits[None], products, 0.0)
    arrived = lax.all_to_all(products, AXES, split_axis=1, concat_axis=1, tiled=True)
    summed = jnp.zeros_like(flat_cells).at[:, target_cells[0]].add(arrived)
    return summed.reshape(iterate.shape)


def to_slices(values, devices):
    count, ca, cb, nz = values.shape
    shaped = jnp.transpose(values, (3, 1, 2, 0))
    return shaped.reshape(devices, (nz // devices) * ca * cb, count)


def gather_grid(received, n_bx, n_by, ca, cb, width):
    count = received.shape[2]
    shaped = received.reshape(n_bx, n_by, width, ca, cb, count)
    shaped = jnp.transpose(shaped, (1, 4, 5, 2, 0, 3))
    return shaped.reshape(n_by * cb, count, width * n_bx * ca)


def scatter_grid(grid, n_bx, n_by, ca, cb, width):
    ny, count, lanes = grid.shape
    shaped = grid.reshape(n_by, cb, count, width, n_bx, ca)
    shaped = jnp.transpose(shaped, (4, 0, 3, 5, 1, 2))
    return shaped.reshape(n_bx * n_by, width * ca * cb, count)


def from_slices(received, ca, cb):
    src, rows, count = received.shape
    width = rows // (ca * cb)
    shaped = received.reshape(src * width, ca, cb, count)
    return jnp.transpose(shaped, (3, 1, 2, 0))


def lane_x(shape, nx):
    return lax.broadcasted_iota(jnp.int32, shape, len(shape) - 1) % nx


def skew(grid, steps, nx):
    ny = grid.shape[0]
    values = jnp.pad(grid, ((0, steps - ny), (0, 0), (0, 0)))
    x = lane_x(values.shape, nx)
    bit = 1
    while bit < nx:
        values = lax.optimization_barrier(values)
        moved = jnp.concatenate([jnp.zeros_like(values[:bit]), values[:-bit]], axis=0)
        values = jnp.where((x & bit) != 0, moved, values)
        bit *= 2
    return values


def unskew(values, ny, nx):
    x = lane_x(values.shape, nx)
    bit = 1
    while bit < nx:
        values = lax.optimization_barrier(values)
        moved = jnp.concatenate([values[bit:], jnp.zeros_like(values[:bit])], axis=0)
        values = jnp.where((x & bit) != 0, moved, values)
        bit *= 2
    return values[:ny]


def as_vectors(rows):
    return jnp.pad(rows, ((0, 0), (0, ROWS - rows.shape[1]), (0, 0)))


def as_matrices(rows, count):
    steps, _, lanes = rows.shape
    shaped = rows.reshape(steps, count, count, lanes)
    return jnp.pad(shaped, ((0, 0), (0, 0), (0, ROWS - count), (0, 0)))


def matvec(matrix, vector):
    count = matrix.shape[1]
    return jnp.sum(matrix * vector[:, :count, None, :], axis=1)


def shift_t(values, offset):
    zero = jnp.zeros_like(values[:1])
    if offset > 0:
        return jnp.concatenate([values[1:], zero], axis=0)
    return jnp.concatenate([zero, values[:-1]], axis=0)


def shift_x(values, offset, nx):
    x = lane_x(values.shape, nx)
    zero = jnp.zeros_like(values[..., :1])
    if offset > 0:
        moved = jnp.concatenate([values[..., 1:], zero], axis=-1)
        return jnp.where(x == nx - 1, 0.0, moved)
    moved = jnp.concatenate([zero, values[..., :-1]], axis=-1)
    return jnp.where(x == 0, 0.0, moved)


def shift_z(values, offset, nx, devices, count):
    rows = values.shape[1]
    if offset > 0:
        halo = lax.ppermute(values[:, :count, :nx], AXES, [(i + 1, i) for i in range(devices - 1)])
        halo = jnp.pad(halo, ((0, 0), (0, rows - count), (0, 0)))
        return jnp.concatenate([values[..., nx:], halo], axis=-1)
    halo = lax.ppermute(values[:, :count, -nx:], AXES, [(i, i + 1) for i in range(devices - 1)])
    halo = jnp.pad(halo, ((0, 0), (0, rows - count), (0, 0)))
    return jnp.concatenate([halo, values[..., :-nx]], axis=-1)


def sweep_kernel(rhs_ref, kx_ref, ky_ref, inv_ref, out_ref, *, forward, nx, count):
    steps = rhs_ref.shape[0]
    lanes = rhs_ref.shape[2]
    x = lax.broadcasted_iota(jnp.int32, (ROWS, lanes), 1) % nx
    if forward:
        keep = x > 0
        shift = 1
    else:
        keep = x < nx - 1
        shift = lanes - 1

    def step(s, fresh):
        t = s if forward else steps - 1 - s
        from_x = jnp.where(keep, pltpu.roll(fresh, shift, 1), 0.0)
        right = rhs_ref[t]
        for j in range(count):
            right = right - kx_ref[t, j] * from_x[j : j + 1, :] - ky_ref[t, j] * fresh[j : j + 1, :]
        result = inv_ref[t, 0] * right[0:1, :]
        for j in range(1, count):
            result = result + inv_ref[t, j] * right[j : j + 1, :]
        out_ref[t] = result
        return result

    lax.fori_loop(0, steps, step, jnp.zeros((ROWS, lanes), jnp.float32), unroll=2)


def sweep(rhs, along_x, along_y, inverses, forward, nx):
    count = along_x.shape[1]
    kernel = functools.partial(sweep_kernel, forward=forward, nx=nx, count=count)
    return pl.pallas_call(
        kernel,
        out_shape=jax.ShapeDtypeStruct(rhs.shape, jnp.float32),
    )(rhs, along_x, along_y, inverses)


def per_device(
    adjoint_source,
    initial,
    inverses,
    couplings,
    interface_tiles,
    source_cells,
    target_cells,
    tile_counts,
):
    n_bx = lax.axis_size("bx")
    n_by = lax.axis_size("by")
    devices = n_bx * n_by
    count, ca, cb, nz = adjoint_source.shape
    nx, ny = n_bx * ca, n_by * cb
    width = nz // devices
    steps = nx + ny
    tables = (interface_tiles, source_cells, target_cells, tile_counts)

    def to_z(values):
        vcount = values.shape[0]
        received = lax.all_to_all(to_slices(values, devices), AXES, 0, 0, tiled=True)
        return skew(gather_grid(received, n_bx, n_by, ca, cb, width), steps, nx)

    def to_xy(skewed):
        grid = unskew(skewed[:, :count], ny, nx)
        received = lax.all_to_all(scatter_grid(grid, n_bx, n_by, ca, cb, width), AXES, 0, 0, tiled=True)
        return from_slices(received, ca, cb)

    base = adjoint_source - interface(initial, *tables)
    packed = jnp.concatenate(
        [
            jnp.swapaxes(inverses, 0, 1).reshape(count * count, ca, cb, nz),
            jnp.swapaxes(couplings, 1, 2).astype(jnp.float32).reshape(6 * count * count, ca, cb, nz),
            base,
            initial,
        ],
        axis=0,
    )
    rows = to_z(packed)
    span = count * count
    inv = as_matrices(rows[:, :span], count)
    ks = [as_matrices(rows[:, span * (k + 1) : span * (k + 2)], count) for k in range(6)]
    base_z = as_vectors(rows[:, 7 * span : 7 * span + count])
    iterate = as_vectors(rows[:, 7 * span + count : 7 * span + 2 * count])

    for number in range(ITERS):
        if number > 0:
            inter = interface(to_xy(iterate), *tables)
            base_z = as_vectors(to_z(adjoint_source - inter))
        lower_terms = (
            base_z
            - matvec(ks[1], shift_x(shift_t(iterate, 1), 1, nx))
            - matvec(ks[3], shift_t(iterate, 1))
            - matvec(ks[4], shift_z(iterate, -1, nx, devices, count))
            - matvec(ks[5], shift_z(iterate, 1, nx, devices, count))
        )
        half = sweep(lower_terms, ks[0], ks[2], inv, True, nx)
        upper_terms = (
            base_z
            - matvec(ks[0], shift_x(shift_t(half, -1), -1, nx))
            - matvec(ks[2], shift_t(half, -1))
            - matvec(ks[4], shift_z(half, -1, nx, devices, count))
            - matvec(ks[5], shift_z(half, 1, nx, devices, count))
        )
        iterate = sweep(upper_terms, ks[1], ks[3], inv, False, nx)
    return to_xy(iterate)


def solution(mesh):
    return jax.shard_map(
        per_device,
        mesh=mesh,
        in_specs=(
            P(None, "bx", "by", None),
            P(None, "bx", "by", None),
            P(None, None, "bx", "by", None),
            P(None, None, None, "bx", "by", None),
            P(AXES, None, None, None),
            P(AXES, None),
            P(AXES, None),
            P(AXES, None),
        ),
        out_specs=P(None, "bx", "by", None),
        check_vma=False,
    )
```

```python
import functools

import jax
import jax.numpy as jnp
from jax import lax
from jax.experimental import pallas as pl
from jax.experimental.pallas import tpu as pltpu
from jax.sharding import PartitionSpec as P

ITERS = 2
AXES = ("bx", "by")
ROWS = 8


def interface(iterate, interface_tiles, source_cells, target_cells, tile_counts):
    var_count = iterate.shape[0]
    flat_cells = iterate.reshape(var_count, -1)
    block_count = lax.axis_size("bx") * lax.axis_size("by")
    slot_count = source_cells.shape[1]
    per_pair = slot_count // block_count
    picked = jnp.take(flat_cells, source_cells[0], axis=1)
    products = jnp.sum(interface_tiles[0] * picked[None], axis=1)
    slot_ids = jnp.arange(slot_count, dtype=jnp.int32)
    limits = jnp.repeat(tile_counts[0], per_pair)
    products = jnp.where((slot_ids % per_pair)[None] < limits[None], products, 0.0)
    arrived = lax.all_to_all(products, AXES, split_axis=1, concat_axis=1, tiled=True)
    summed = jnp.zeros_like(flat_cells).at[:, target_cells[0]].add(arrived)
    return summed.reshape(iterate.shape)


def to_slices(values, devices):
    count, ca, cb, nz = values.shape
    shaped = jnp.transpose(values, (3, 1, 2, 0))
    return shaped.reshape(devices, (nz // devices) * ca * cb, count)


def gather_grid(received, n_bx, n_by, ca, cb, width):
    count = received.shape[2]
    shaped = received.reshape(n_bx, n_by, width, ca, cb, count)
    shaped = jnp.transpose(shaped, (1, 4, 5, 2, 0, 3))
    return shaped.reshape(n_by * cb, count, width * n_bx * ca)


def scatter_grid(grid, n_bx, n_by, ca, cb, width):
    ny, count, lanes = grid.shape
    shaped = grid.reshape(n_by, cb, count, width, n_bx, ca)
    shaped = jnp.transpose(shaped, (4, 0, 3, 5, 1, 2))
    return shaped.reshape(n_bx * n_by, width * ca * cb, count)


def from_slices(received, ca, cb):
    src, rows, count = received.shape
    width = rows // (ca * cb)
    shaped = received.reshape(src * width, ca, cb, count)
    return jnp.transpose(shaped, (3, 1, 2, 0))


def lane_x(shape, nx):
    return lax.broadcasted_iota(jnp.int32, shape, len(shape) - 1) % nx


def skew(grid, steps, nx):
    ny = grid.shape[0]
    values = jnp.pad(grid, ((0, steps - ny), (0, 0), (0, 0)))
    x = lane_x(values.shape, nx)
    bit = 1
    while bit < nx:
        values = lax.optimization_barrier(values)
        moved = jnp.concatenate([jnp.zeros_like(values[:bit]), values[:-bit]], axis=0)
        values = jnp.where((x & bit) != 0, moved, values)
        bit *= 2
    return values


def skew_kernel(grid_ref, out_ref, *, nx):
    ny = grid_ref.shape[0]
    steps = out_ref.shape[0]
    out_ref[:ny] = grid_ref[...]
    out_ref[ny:] = jnp.zeros((steps - ny,) + out_ref.shape[1:], jnp.float32)
    x = lax.broadcasted_iota(jnp.int32, out_ref.shape[1:], 1) % nx
    bit = 1
    while bit < nx:
        moves = (x & bit) != 0

        def body(i, carry, bit=bit, moves=moves):
            t = steps - 1 - i
            out_ref[t] = jnp.where(moves, out_ref[t - bit], out_ref[t])
            return carry

        lax.fori_loop(0, steps - bit, body, 0)
        for t in range(bit):
            out_ref[t] = jnp.where(moves, 0.0, out_ref[t])
        bit *= 2


def skew_big(grid, steps, nx):
    ny, count, lanes = grid.shape
    return pl.pallas_call(
        functools.partial(skew_kernel, nx=nx),
        out_shape=jax.ShapeDtypeStruct((steps, count, lanes), jnp.float32),
    )(grid)


def unskew(values, ny, nx):
    x = lane_x(values.shape, nx)
    bit = 1
    while bit < nx:
        values = lax.optimization_barrier(values)
        moved = jnp.concatenate([values[bit:], jnp.zeros_like(values[:bit])], axis=0)
        values = jnp.where((x & bit) != 0, moved, values)
        bit *= 2
    return values[:ny]


def as_vectors(rows):
    return jnp.pad(rows, ((0, 0), (0, ROWS - rows.shape[1]), (0, 0)))


def as_matrices(rows, count):
    steps, _, lanes = rows.shape
    shaped = rows.reshape(steps, count, count, lanes)
    return jnp.pad(shaped, ((0, 0), (0, 0), (0, ROWS - count), (0, 0)))


def matvec(matrix, vector):
    count = matrix.shape[1]
    return jnp.sum(matrix * vector[:, :count, None, :], axis=1)


def shift_t(values, offset):
    zero = jnp.zeros_like(values[:1])
    if offset > 0:
        return jnp.concatenate([values[1:], zero], axis=0)
    return jnp.concatenate([zero, values[:-1]], axis=0)


def shift_x(values, offset, nx):
    x = lane_x(values.shape, nx)
    zero = jnp.zeros_like(values[..., :1])
    if offset > 0:
        moved = jnp.concatenate([values[..., 1:], zero], axis=-1)
        return jnp.where(x == nx - 1, 0.0, moved)
    moved = jnp.concatenate([zero, values[..., :-1]], axis=-1)
    return jnp.where(x == 0, 0.0, moved)


def shift_z(values, offset, nx, devices, count):
    rows = values.shape[1]
    if offset > 0:
        halo = lax.ppermute(values[:, :count, :nx], AXES, [(i + 1, i) for i in range(devices - 1)])
        halo = jnp.pad(halo, ((0, 0), (0, rows - count), (0, 0)))
        return jnp.concatenate([values[..., nx:], halo], axis=-1)
    halo = lax.ppermute(values[:, :count, -nx:], AXES, [(i, i + 1) for i in range(devices - 1)])
    halo = jnp.pad(halo, ((0, 0), (0, rows - count), (0, 0)))
    return jnp.concatenate([halo, values[..., :-nx]], axis=-1)


def sweep_kernel(rhs_ref, kx_ref, ky_ref, inv_ref, out_ref, *, forward, nx, count):
    steps = rhs_ref.shape[0]
    lanes = rhs_ref.shape[2]
    x = lax.broadcasted_iota(jnp.int32, (ROWS, lanes), 1) % nx
    if forward:
        keep = x > 0
        shift = 1
    else:
        keep = x < nx - 1
        shift = lanes - 1

    def step(s, fresh):
        t = s if forward else steps - 1 - s
        from_x = jnp.where(keep, pltpu.roll(fresh, shift, 1), 0.0)
        right = rhs_ref[t]
        for j in range(count):
            right = right - kx_ref[t, j] * from_x[j : j + 1, :] - ky_ref[t, j] * fresh[j : j + 1, :]
        result = inv_ref[t, 0] * right[0:1, :]
        for j in range(1, count):
            result = result + inv_ref[t, j] * right[j : j + 1, :]
        out_ref[t] = result
        return result

    lax.fori_loop(0, steps, step, jnp.zeros((ROWS, lanes), jnp.float32), unroll=2)


def sweep(rhs, along_x, along_y, inverses, forward, nx):
    count = along_x.shape[1]
    kernel = functools.partial(sweep_kernel, forward=forward, nx=nx, count=count)
    return pl.pallas_call(
        kernel,
        out_shape=jax.ShapeDtypeStruct(rhs.shape, jnp.float32),
    )(rhs, along_x, along_y, inverses)


def per_device(
    adjoint_source,
    initial,
    inverses,
    couplings,
    interface_tiles,
    source_cells,
    target_cells,
    tile_counts,
):
    n_bx = lax.axis_size("bx")
    n_by = lax.axis_size("by")
    devices = n_bx * n_by
    count, ca, cb, nz = adjoint_source.shape
    nx, ny = n_bx * ca, n_by * cb
    width = nz // devices
    steps = nx + ny
    tables = (interface_tiles, source_cells, target_cells, tile_counts)

    def to_z(values, skewer=skew):
        received = lax.all_to_all(to_slices(values, devices), AXES, 0, 0, tiled=True)
        return skewer(gather_grid(received, n_bx, n_by, ca, cb, width), steps, nx)

    def to_xy(skewed):
        grid = unskew(skewed[:, :count], ny, nx)
        received = lax.all_to_all(scatter_grid(grid, n_bx, n_by, ca, cb, width), AXES, 0, 0, tiled=True)
        return from_slices(received, ca, cb)

    base = adjoint_source - interface(initial, *tables)
    packed = jnp.concatenate(
        [
            jnp.swapaxes(inverses, 0, 1).reshape(count * count, ca, cb, nz),
            jnp.swapaxes(couplings, 1, 2).astype(jnp.float32).reshape(6 * count * count, ca, cb, nz),
            base,
            initial,
        ],
        axis=0,
    )
    rows = to_z(packed, skew_big)
    span = count * count
    inv = as_matrices(rows[:, :span], count)
    ks = [as_matrices(rows[:, span * (k + 1) : span * (k + 2)], count) for k in range(6)]
    base_z = as_vectors(rows[:, 7 * span : 7 * span + count])
    iterate = as_vectors(rows[:, 7 * span + count : 7 * span + 2 * count])

    for number in range(ITERS):
        if number > 0:
            inter = interface(to_xy(iterate), *tables)
            base_z = as_vectors(to_z(adjoint_source - inter))
        lower_terms = (
            base_z
            - matvec(ks[1], shift_x(shift_t(iterate, 1), 1, nx))
            - matvec(ks[3], shift_t(iterate, 1))
            - matvec(ks[4], shift_z(iterate, -1, nx, devices, count))
            - matvec(ks[5], shift_z(iterate, 1, nx, devices, count))
        )
        half = sweep(lower_terms, ks[0], ks[2], inv, True, nx)
        upper_terms = (
            base_z
            - matvec(ks[0], shift_x(shift_t(half, -1), -1, nx))
            - matvec(ks[2], shift_t(half, -1))
            - matvec(ks[4], shift_z(half, -1, nx, devices, count))
            - matvec(ks[5], shift_z(half, 1, nx, devices, count))
        )
        iterate = sweep(upper_terms, ks[1], ks[3], inv, False, nx)
    return to_xy(iterate)


def solution(mesh):
    return jax.shard_map(
        per_device,
        mesh=mesh,
        in_specs=(
            P(None, "bx", "by", None),
            P(None, "bx", "by", None),
            P(None, None, "bx", "by", None),
            P(None, None, None, "bx", "by", None),
            P(AXES, None, None, None),
            P(AXES, None),
            P(AXES, None),
            P(AXES, None),
        ),
        out_specs=P(None, "bx", "by", None),
        check_vma=False,
    )
```

```python
import functools

import jax
import jax.numpy as jnp
from jax import lax
from jax.experimental import pallas as pl
from jax.experimental.pallas import tpu as pltpu
from jax.sharding import PartitionSpec as P

ITERS = 2
AXES = ("bx", "by")
ROWS = 8


def interface(iterate, interface_tiles, source_cells, target_cells, tile_counts):
    var_count = iterate.shape[0]
    flat_cells = iterate.reshape(var_count, -1)
    block_count = lax.axis_size("bx") * lax.axis_size("by")
    slot_count = source_cells.shape[1]
    per_pair = slot_count // block_count
    picked = jnp.take(flat_cells, source_cells[0], axis=1)
    products = jnp.sum(interface_tiles[0] * picked[None], axis=1)
    slot_ids = jnp.arange(slot_count, dtype=jnp.int32)
    limits = jnp.repeat(tile_counts[0], per_pair)
    products = jnp.where((slot_ids % per_pair)[None] < limits[None], products, 0.0)
    arrived = lax.all_to_all(products, AXES, split_axis=1, concat_axis=1, tiled=True)
    summed = jnp.zeros_like(flat_cells).at[:, target_cells[0]].add(arrived)
    return summed.reshape(iterate.shape)


def to_slices(values, devices):
    count, ca, cb, nz = values.shape
    shaped = jnp.transpose(values, (3, 1, 2, 0))
    return shaped.reshape(devices, (nz // devices) * ca * cb, count)


def gather_grid(received, n_bx, n_by, ca, cb, width):
    count = received.shape[2]
    shaped = received.reshape(n_bx, n_by, width, ca, cb, count)
    shaped = jnp.transpose(shaped, (1, 4, 5, 2, 0, 3))
    return shaped.reshape(n_by * cb, count, width * n_bx * ca)


def scatter_grid(grid, n_bx, n_by, ca, cb, width):
    ny, count, lanes = grid.shape
    shaped = grid.reshape(n_by, cb, count, width, n_bx, ca)
    shaped = jnp.transpose(shaped, (4, 0, 3, 5, 1, 2))
    return shaped.reshape(n_bx * n_by, width * ca * cb, count)


def from_slices(received, ca, cb):
    src, rows, count = received.shape
    width = rows // (ca * cb)
    shaped = received.reshape(src * width, ca, cb, count)
    return jnp.transpose(shaped, (3, 1, 2, 0))


def lane_x(shape, nx):
    return lax.broadcasted_iota(jnp.int32, shape, len(shape) - 1) % nx


def skew(grid, steps, nx):
    ny = grid.shape[0]
    values = jnp.pad(grid, ((0, steps - ny), (0, 0), (0, 0)))
    x = lane_x(values.shape, nx)
    bit = 1
    while bit < nx:
        values = lax.optimization_barrier(values)
        moved = jnp.concatenate([jnp.zeros_like(values[:bit]), values[:-bit]], axis=0)
        values = jnp.where((x & bit) != 0, moved, values)
        bit *= 2
    return values


def skew_kernel(grid_ref, out_ref, *, nx):
    ny = grid_ref.shape[0]
    steps = out_ref.shape[0]
    out_ref[:ny] = grid_ref[...]
    out_ref[ny:] = jnp.zeros((steps - ny,) + out_ref.shape[1:], jnp.float32)
    x = lax.broadcasted_iota(jnp.int32, out_ref.shape[1:], 1) % nx
    bit = 1
    while bit < nx:
        moves = (x & bit) != 0

        def body(i, carry, bit=bit, moves=moves):
            t = steps - 1 - i
            out_ref[t] = jnp.where(moves, out_ref[t - bit], out_ref[t])
            return carry

        lax.fori_loop(0, steps - bit, body, 0)
        for t in range(bit):
            out_ref[t] = jnp.where(moves, 0.0, out_ref[t])
        bit *= 2


def skew_big(grid, steps, nx):
    ny, count, lanes = grid.shape
    return pl.pallas_call(
        functools.partial(skew_kernel, nx=nx),
        out_shape=jax.ShapeDtypeStruct((steps, count, lanes), jnp.float32),
    )(grid)


def unskew(values, ny, nx):
    x = lane_x(values.shape, nx)
    bit = 1
    while bit < nx:
        values = lax.optimization_barrier(values)
        moved = jnp.concatenate([values[bit:], jnp.zeros_like(values[:bit])], axis=0)
        values = jnp.where((x & bit) != 0, moved, values)
        bit *= 2
    return values[:ny]


def as_vectors(rows):
    return jnp.pad(rows, ((0, 0), (0, ROWS - rows.shape[1]), (0, 0)))


def as_matrices(rows, count):
    steps, _, lanes = rows.shape
    shaped = rows.reshape(steps, count, count, lanes)
    return jnp.pad(shaped, ((0, 0), (0, 0), (0, ROWS - count), (0, 0)))


def matvec(matrix, vector):
    count = matrix.shape[1]
    return jnp.sum(matrix * vector[:, :count, None, :], axis=1)


def shift_t(values, offset):
    zero = jnp.zeros_like(values[:1])
    if offset > 0:
        return jnp.concatenate([values[1:], zero], axis=0)
    return jnp.concatenate([zero, values[:-1]], axis=0)


def shift_x(values, offset, nx):
    x = lane_x(values.shape, nx)
    zero = jnp.zeros_like(values[..., :1])
    if offset > 0:
        moved = jnp.concatenate([values[..., 1:], zero], axis=-1)
        return jnp.where(x == nx - 1, 0.0, moved)
    moved = jnp.concatenate([zero, values[..., :-1]], axis=-1)
    return jnp.where(x == 0, 0.0, moved)


def shift_z(values, offset, nx, devices, count):
    rows = values.shape[1]
    if offset > 0:
        halo = lax.ppermute(values[:, :count, :nx], AXES, [(i + 1, i) for i in range(devices - 1)])
        halo = jnp.pad(halo, ((0, 0), (0, rows - count), (0, 0)))
        return jnp.concatenate([values[..., nx:], halo], axis=-1)
    halo = lax.ppermute(values[:, :count, -nx:], AXES, [(i, i + 1) for i in range(devices - 1)])
    halo = jnp.pad(halo, ((0, 0), (0, rows - count), (0, 0)))
    return jnp.concatenate([halo, values[..., :-nx]], axis=-1)


def sweep_kernel(rhs_ref, kx_ref, ky_ref, inv_ref, out_ref, *, forward, nx, count):
    steps = rhs_ref.shape[0]
    lanes = rhs_ref.shape[2]
    x = lax.broadcasted_iota(jnp.int32, (ROWS, lanes), 1) % nx
    if forward:
        keep = x > 0
        shift = 1
    else:
        keep = x < nx - 1
        shift = lanes - 1

    def step(s, fresh):
        t = s if forward else steps - 1 - s
        from_x = jnp.where(keep, pltpu.roll(fresh, shift, 1), 0.0)
        right = rhs_ref[t]
        for j in range(count):
            right = right - kx_ref[t, j] * from_x[j : j + 1, :] - ky_ref[t, j] * fresh[j : j + 1, :]
        result = inv_ref[t, 0] * right[0:1, :]
        for j in range(1, count):
            result = result + inv_ref[t, j] * right[j : j + 1, :]
        out_ref[t] = result
        return result

    lax.fori_loop(0, steps, step, jnp.zeros((ROWS, lanes), jnp.float32), unroll=2)


def sweep(rhs, along_x, along_y, inverses, forward, nx):
    count = along_x.shape[1]
    kernel = functools.partial(sweep_kernel, forward=forward, nx=nx, count=count)
    return pl.pallas_call(
        kernel,
        out_shape=jax.ShapeDtypeStruct(rhs.shape, jnp.float32),
    )(rhs, along_x, along_y, inverses)


def per_device(
    adjoint_source,
    initial,
    inverses,
    couplings,
    interface_tiles,
    source_cells,
    target_cells,
    tile_counts,
):
    n_bx = lax.axis_size("bx")
    n_by = lax.axis_size("by")
    devices = n_bx * n_by
    count, ca, cb, nz = adjoint_source.shape
    nx, ny = n_bx * ca, n_by * cb
    width = nz // devices
    steps = nx + ny
    tables = (interface_tiles, source_cells, target_cells, tile_counts)

    def to_z(values, skewer=skew):
        received = lax.all_to_all(to_slices(values, devices), AXES, 0, 0, tiled=True)
        return skewer(gather_grid(received, n_bx, n_by, ca, cb, width), steps, nx)

    def to_xy(skewed):
        grid = unskew(skewed[:, :count], ny, nx)
        received = lax.all_to_all(scatter_grid(grid, n_bx, n_by, ca, cb, width), AXES, 0, 0, tiled=True)
        return from_slices(received, ca, cb)

    span = count * count
    sweep_rows = to_z(
        jnp.concatenate(
            [
                jnp.swapaxes(inverses, 0, 1).reshape(span, ca, cb, nz),
                jnp.swapaxes(couplings[0::2][:2], 1, 2).astype(jnp.float32).reshape(2 * span, ca, cb, nz),
            ],
            axis=0,
        ),
        skew_big,
    )
    base = adjoint_source - interface(initial, *tables)
    other_rows = to_z(
        jnp.concatenate(
            [
                jnp.swapaxes(couplings[jnp.array([1, 3, 4, 5])], 1, 2).astype(jnp.float32).reshape(4 * span, ca, cb, nz),
                base,
                initial,
            ],
            axis=0,
        ),
        skew_big,
    )
    inv = as_matrices(sweep_rows[:, :span], count)
    ks = [None] * 6
    ks[0] = as_matrices(sweep_rows[:, span : 2 * span], count)
    ks[2] = as_matrices(sweep_rows[:, 2 * span : 3 * span], count)
    for place, k in enumerate((1, 3, 4, 5)):
        ks[k] = as_matrices(other_rows[:, span * place : span * (place + 1)], count)
    base_z = as_vectors(other_rows[:, 4 * span : 4 * span + count])
    iterate = as_vectors(other_rows[:, 4 * span + count : 4 * span + 2 * count])

    for number in range(ITERS):
        if number > 0:
            inter = interface(to_xy(iterate), *tables)
            base_z = as_vectors(to_z(adjoint_source - inter))
        lower_terms = (
            base_z
            - matvec(ks[1], shift_x(shift_t(iterate, 1), 1, nx))
            - matvec(ks[3], shift_t(iterate, 1))
            - matvec(ks[4], shift_z(iterate, -1, nx, devices, count))
            - matvec(ks[5], shift_z(iterate, 1, nx, devices, count))
        )
        half = sweep(lower_terms, ks[0], ks[2], inv, True, nx)
        upper_terms = (
            base_z
            - matvec(ks[0], shift_x(shift_t(half, -1), -1, nx))
            - matvec(ks[2], shift_t(half, -1))
            - matvec(ks[4], shift_z(half, -1, nx, devices, count))
            - matvec(ks[5], shift_z(half, 1, nx, devices, count))
        )
        iterate = sweep(upper_terms, ks[1], ks[3], inv, False, nx)
    return to_xy(iterate)


def solution(mesh):
    return jax.shard_map(
        per_device,
        mesh=mesh,
        in_specs=(
            P(None, "bx", "by", None),
            P(None, "bx", "by", None),
            P(None, None, "bx", "by", None),
            P(None, None, None, "bx", "by", None),
            P(AXES, None, None, None),
            P(AXES, None),
            P(AXES, None),
            P(AXES, None),
        ),
        out_specs=P(None, "bx", "by", None),
        check_vma=False,
    )
```

```python
import functools

import jax
import jax.numpy as jnp
from jax import lax
from jax.experimental import pallas as pl
from jax.experimental.pallas import tpu as pltpu
from jax.sharding import PartitionSpec as P

ITERS = 2
AXES = ("bx", "by")
ROWS = 8


def interface(iterate, interface_tiles, source_cells, target_cells, tile_counts):
    var_count = iterate.shape[0]
    flat_cells = iterate.reshape(var_count, -1)
    block_count = lax.axis_size("bx") * lax.axis_size("by")
    slot_count = source_cells.shape[1]
    per_pair = slot_count // block_count
    picked = jnp.take(flat_cells, source_cells[0], axis=1)
    products = jnp.sum(interface_tiles[0] * picked[None], axis=1)
    slot_ids = jnp.arange(slot_count, dtype=jnp.int32)
    limits = jnp.repeat(tile_counts[0], per_pair)
    products = jnp.where((slot_ids % per_pair)[None] < limits[None], products, 0.0)
    arrived = lax.all_to_all(products, AXES, split_axis=1, concat_axis=1, tiled=True)
    summed = jnp.zeros_like(flat_cells).at[:, target_cells[0]].add(arrived)
    return summed.reshape(iterate.shape)


def to_slices(values, devices):
    count, ca, cb, nz = values.shape
    shaped = jnp.transpose(values, (3, 1, 2, 0))
    return shaped.reshape(devices, (nz // devices) * ca * cb, count)


def gather_grid(received, n_bx, n_by, ca, cb, width):
    count = received.shape[2]
    shaped = received.reshape(n_bx, n_by, width, ca, cb, count)
    shaped = jnp.transpose(shaped, (1, 4, 5, 2, 0, 3))
    return shaped.reshape(n_by * cb, count, width * n_bx * ca)


def scatter_grid(grid, n_bx, n_by, ca, cb, width):
    ny, count, lanes = grid.shape
    shaped = grid.reshape(n_by, cb, count, width, n_bx, ca)
    shaped = jnp.transpose(shaped, (4, 0, 3, 5, 1, 2))
    return shaped.reshape(n_bx * n_by, width * ca * cb, count)


def from_slices(received, ca, cb):
    src, rows, count = received.shape
    width = rows // (ca * cb)
    shaped = received.reshape(src * width, ca, cb, count)
    return jnp.transpose(shaped, (3, 1, 2, 0))


def lane_x(shape, nx):
    return lax.broadcasted_iota(jnp.int32, shape, len(shape) - 1) % nx


def skew(grid, steps, nx):
    ny = grid.shape[0]
    values = jnp.pad(grid, ((0, steps - ny), (0, 0), (0, 0)))
    x = lane_x(values.shape, nx)
    bit = 1
    while bit < nx:
        values = lax.optimization_barrier(values)
        moved = jnp.concatenate([jnp.zeros_like(values[:bit]), values[:-bit]], axis=0)
        values = jnp.where((x & bit) != 0, moved, values)
        bit *= 2
    return values


def skew_kernel(grid_ref, out_ref, *, nx):
    ny = grid_ref.shape[0]
    steps = out_ref.shape[0]
    out_ref[:ny] = grid_ref[...]
    out_ref[ny:] = jnp.zeros((steps - ny,) + out_ref.shape[1:], jnp.float32)
    x = lax.broadcasted_iota(jnp.int32, out_ref.shape[1:], 1) % nx
    bit = 1
    while bit < nx:
        moves = (x & bit) != 0

        def body(i, carry, bit=bit, moves=moves):
            t = steps - 1 - i
            out_ref[t] = jnp.where(moves, out_ref[t - bit], out_ref[t])
            return carry

        lax.fori_loop(0, steps - bit, body, 0)
        for t in range(bit):
            out_ref[t] = jnp.where(moves, 0.0, out_ref[t])
        bit *= 2


def skew_big(grid, steps, nx):
    ny, count, lanes = grid.shape
    return pl.pallas_call(
        functools.partial(skew_kernel, nx=nx),
        out_shape=jax.ShapeDtypeStruct((steps, count, lanes), jnp.float32),
    )(grid)


def unskew(values, ny, nx):
    x = lane_x(values.shape, nx)
    bit = 1
    while bit < nx:
        values = lax.optimization_barrier(values)
        moved = jnp.concatenate([values[bit:], jnp.zeros_like(values[:bit])], axis=0)
        values = jnp.where((x & bit) != 0, moved, values)
        bit *= 2
    return values[:ny]


def as_vectors(rows):
    return jnp.pad(rows, ((0, 0), (0, ROWS - rows.shape[1]), (0, 0)))


def as_matrices(rows, count):
    steps, _, lanes = rows.shape
    shaped = rows.reshape(steps, count, count, lanes)
    return jnp.pad(shaped, ((0, 0), (0, 0), (0, ROWS - count), (0, 0)))


def matvec(matrix, vector):
    count = matrix.shape[1]
    return jnp.sum(matrix * vector[:, :count, None, :], axis=1)


def shift_t(values, offset):
    zero = jnp.zeros_like(values[:1])
    if offset > 0:
        return jnp.concatenate([values[1:], zero], axis=0)
    return jnp.concatenate([zero, values[:-1]], axis=0)


def shift_x(values, offset, nx):
    x = lane_x(values.shape, nx)
    zero = jnp.zeros_like(values[..., :1])
    if offset > 0:
        moved = jnp.concatenate([values[..., 1:], zero], axis=-1)
        return jnp.where(x == nx - 1, 0.0, moved)
    moved = jnp.concatenate([zero, values[..., :-1]], axis=-1)
    return jnp.where(x == 0, 0.0, moved)


def shift_z(values, offset, nx, devices, count):
    rows = values.shape[1]
    if offset > 0:
        halo = lax.ppermute(values[:, :count, :nx], AXES, [(i + 1, i) for i in range(devices - 1)])
        halo = jnp.pad(halo, ((0, 0), (0, rows - count), (0, 0)))
        return jnp.concatenate([values[..., nx:], halo], axis=-1)
    halo = lax.ppermute(values[:, :count, -nx:], AXES, [(i, i + 1) for i in range(devices - 1)])
    halo = jnp.pad(halo, ((0, 0), (0, rows - count), (0, 0)))
    return jnp.concatenate([halo, values[..., :-nx]], axis=-1)


def tree_sum(terms):
    while len(terms) > 1:
        paired = [terms[i] + terms[i + 1] for i in range(0, len(terms) - 1, 2)]
        terms = paired + terms[len(paired) * 2 :]
    return terms[0]


def sweep_kernel(rhs_ref, kx_ref, ky_ref, inv_ref, out_ref, *, forward, nx, count):
    steps = rhs_ref.shape[0]
    lanes = rhs_ref.shape[2]
    x = lax.broadcasted_iota(jnp.int32, (ROWS, lanes), 1) % nx
    if forward:
        keep = x > 0
        shift = 1
    else:
        keep = x < nx - 1
        shift = lanes - 1

    def step(s, fresh):
        t = s if forward else steps - 1 - s
        from_x = jnp.where(keep, pltpu.roll(fresh, shift, 1), 0.0)
        terms = [kx_ref[t, j] * from_x[j : j + 1, :] for j in range(count)]
        terms += [ky_ref[t, j] * fresh[j : j + 1, :] for j in range(count)]
        right = rhs_ref[t] - tree_sum(terms)
        result = tree_sum([inv_ref[t, j] * right[j : j + 1, :] for j in range(count)])
        out_ref[t] = result
        return result

    lax.fori_loop(0, steps, step, jnp.zeros((ROWS, lanes), jnp.float32), unroll=2)


def sweep(rhs, along_x, along_y, inverses, forward, nx):
    count = along_x.shape[1]
    kernel = functools.partial(sweep_kernel, forward=forward, nx=nx, count=count)
    return pl.pallas_call(
        kernel,
        out_shape=jax.ShapeDtypeStruct(rhs.shape, jnp.float32),
    )(rhs, along_x, along_y, inverses)


def per_device(
    adjoint_source,
    initial,
    inverses,
    couplings,
    interface_tiles,
    source_cells,
    target_cells,
    tile_counts,
):
    n_bx = lax.axis_size("bx")
    n_by = lax.axis_size("by")
    devices = n_bx * n_by
    count, ca, cb, nz = adjoint_source.shape
    nx, ny = n_bx * ca, n_by * cb
    width = nz // devices
    steps = nx + ny
    tables = (interface_tiles, source_cells, target_cells, tile_counts)

    def to_z(values, skewer=skew):
        received = lax.all_to_all(to_slices(values, devices), AXES, 0, 0, tiled=True)
        return skewer(gather_grid(received, n_bx, n_by, ca, cb, width), steps, nx)

    def to_xy(skewed):
        grid = unskew(skewed[:, :count], ny, nx)
        received = lax.all_to_all(scatter_grid(grid, n_bx, n_by, ca, cb, width), AXES, 0, 0, tiled=True)
        return from_slices(received, ca, cb)

    span = count * count
    sweep_rows = to_z(
        jnp.concatenate(
            [
                jnp.swapaxes(inverses, 0, 1).reshape(span, ca, cb, nz),
                jnp.swapaxes(couplings[0::2][:2], 1, 2).astype(jnp.float32).reshape(2 * span, ca, cb, nz),
            ],
            axis=0,
        ),
        skew_big,
    )
    base = adjoint_source - interface(initial, *tables)
    other_rows = to_z(
        jnp.concatenate(
            [
                jnp.swapaxes(couplings[jnp.array([1, 3, 4, 5])], 1, 2).astype(jnp.float32).reshape(4 * span, ca, cb, nz),
                base,
                initial,
            ],
            axis=0,
        ),
        skew_big,
    )
    inv = as_matrices(sweep_rows[:, :span], count)
    ks = [None] * 6
    ks[0] = as_matrices(sweep_rows[:, span : 2 * span], count)
    ks[2] = as_matrices(sweep_rows[:, 2 * span : 3 * span], count)
    for place, k in enumerate((1, 3, 4, 5)):
        ks[k] = as_matrices(other_rows[:, span * place : span * (place + 1)], count)
    base_z = as_vectors(other_rows[:, 4 * span : 4 * span + count])
    iterate = as_vectors(other_rows[:, 4 * span + count : 4 * span + 2 * count])

    for number in range(ITERS):
        if number > 0:
            inter = interface(to_xy(iterate), *tables)
            base_z = as_vectors(to_z(adjoint_source - inter))
        lower_terms = (
            base_z
            - matvec(ks[1], shift_x(shift_t(iterate, 1), 1, nx))
            - matvec(ks[3], shift_t(iterate, 1))
            - matvec(ks[4], shift_z(iterate, -1, nx, devices, count))
            - matvec(ks[5], shift_z(iterate, 1, nx, devices, count))
        )
        half = sweep(lower_terms, ks[0], ks[2], inv, True, nx)
        upper_terms = (
            base_z
            - matvec(ks[0], shift_x(shift_t(half, -1), -1, nx))
            - matvec(ks[2], shift_t(half, -1))
            - matvec(ks[4], shift_z(half, -1, nx, devices, count))
            - matvec(ks[5], shift_z(half, 1, nx, devices, count))
        )
        iterate = sweep(upper_terms, ks[1], ks[3], inv, False, nx)
    return to_xy(iterate)


def solution(mesh):
    return jax.shard_map(
        per_device,
        mesh=mesh,
        in_specs=(
            P(None, "bx", "by", None),
            P(None, "bx", "by", None),
            P(None, None, "bx", "by", None),
            P(None, None, None, "bx", "by", None),
            P(AXES, None, None, None),
            P(AXES, None),
            P(AXES, None),
            P(AXES, None),
        ),
        out_specs=P(None, "bx", "by", None),
        check_vma=False,
    )
```

```python
import functools

import jax
import jax.numpy as jnp
from jax import lax
from jax.experimental import pallas as pl
from jax.experimental.pallas import tpu as pltpu
from jax.sharding import PartitionSpec as P

ITERS = 2
AXES = ("bx", "by")
ROWS = 8


def interface(iterate, interface_tiles, source_cells, target_cells, tile_counts):
    var_count = iterate.shape[0]
    flat_cells = iterate.reshape(var_count, -1)
    block_count = lax.axis_size("bx") * lax.axis_size("by")
    slot_count = source_cells.shape[1]
    per_pair = slot_count // block_count
    picked = jnp.take(flat_cells, source_cells[0], axis=1)
    products = jnp.sum(interface_tiles[0] * picked[None], axis=1)
    slot_ids = jnp.arange(slot_count, dtype=jnp.int32)
    limits = jnp.repeat(tile_counts[0], per_pair)
    products = jnp.where((slot_ids % per_pair)[None] < limits[None], products, 0.0)
    arrived = lax.all_to_all(products, AXES, split_axis=1, concat_axis=1, tiled=True)
    summed = jnp.zeros_like(flat_cells).at[:, target_cells[0]].add(arrived)
    return summed.reshape(iterate.shape)


def to_slices(values, devices):
    count, ca, cb, nz = values.shape
    shaped = jnp.transpose(values, (3, 1, 2, 0))
    return shaped.reshape(devices, (nz // devices) * ca * cb, count)


def gather_grid(received, n_bx, n_by, ca, cb, width):
    count = received.shape[2]
    shaped = received.reshape(n_bx, n_by, width, ca, cb, count)
    shaped = jnp.transpose(shaped, (1, 4, 5, 2, 0, 3))
    return shaped.reshape(n_by * cb, count, width * n_bx * ca)


def scatter_grid(grid, n_bx, n_by, ca, cb, width):
    ny, count, lanes = grid.shape
    shaped = grid.reshape(n_by, cb, count, width, n_bx, ca)
    shaped = jnp.transpose(shaped, (4, 0, 3, 5, 1, 2))
    return shaped.reshape(n_bx * n_by, width * ca * cb, count)


def from_slices(received, ca, cb):
    src, rows, count = received.shape
    width = rows // (ca * cb)
    shaped = received.reshape(src * width, ca, cb, count)
    return jnp.transpose(shaped, (3, 1, 2, 0))


def lane_x(shape, nx):
    return lax.broadcasted_iota(jnp.int32, shape, len(shape) - 1) % nx


def skew(grid, steps, nx):
    ny = grid.shape[0]
    values = jnp.pad(grid, ((0, steps - ny), (0, 0), (0, 0)))
    x = lane_x(values.shape, nx)
    bit = 1
    while bit < nx:
        values = lax.optimization_barrier(values)
        moved = jnp.concatenate([jnp.zeros_like(values[:bit]), values[:-bit]], axis=0)
        values = jnp.where((x & bit) != 0, moved, values)
        bit *= 2
    return values


def skew_kernel(grid_ref, out_ref, *, nx):
    ny = grid_ref.shape[0]
    steps = out_ref.shape[0]
    out_ref[:ny] = grid_ref[...]
    out_ref[ny:] = jnp.zeros((steps - ny,) + out_ref.shape[1:], jnp.float32)
    x = lax.broadcasted_iota(jnp.int32, out_ref.shape[1:], 1) % nx
    bit = 1
    while bit < nx:
        moves = (x & bit) != 0

        def body(i, carry, bit=bit, moves=moves):
            t = steps - 1 - i
            out_ref[t] = jnp.where(moves, out_ref[t - bit], out_ref[t])
            return carry

        lax.fori_loop(0, steps - bit, body, 0)
        for t in range(bit):
            out_ref[t] = jnp.where(moves, 0.0, out_ref[t])
        bit *= 2


def skew_big(grid, steps, nx):
    ny, count, lanes = grid.shape
    return pl.pallas_call(
        functools.partial(skew_kernel, nx=nx),
        out_shape=jax.ShapeDtypeStruct((steps, count, lanes), jnp.float32),
    )(grid)


def unskew(values, ny, nx):
    x = lane_x(values.shape, nx)
    bit = 1
    while bit < nx:
        values = lax.optimization_barrier(values)
        moved = jnp.concatenate([values[bit:], jnp.zeros_like(values[:bit])], axis=0)
        values = jnp.where((x & bit) != 0, moved, values)
        bit *= 2
    return values[:ny]


def as_vectors(rows):
    return jnp.pad(rows, ((0, 0), (0, ROWS - rows.shape[1]), (0, 0)))


def as_matrices(rows, count):
    steps, _, lanes = rows.shape
    shaped = rows.reshape(steps, count, count, lanes)
    return jnp.pad(shaped, ((0, 0), (0, 0), (0, ROWS - count), (0, 0)))


def matvec(matrix, vector):
    count = matrix.shape[1]
    return jnp.sum(matrix * vector[:, :count, None, :], axis=1)


def shift_t(values, offset):
    zero = jnp.zeros_like(values[:1])
    if offset > 0:
        return jnp.concatenate([values[1:], zero], axis=0)
    return jnp.concatenate([zero, values[:-1]], axis=0)


def shift_x(values, offset, nx):
    x = lane_x(values.shape, nx)
    zero = jnp.zeros_like(values[..., :1])
    if offset > 0:
        moved = jnp.concatenate([values[..., 1:], zero], axis=-1)
        return jnp.where(x == nx - 1, 0.0, moved)
    moved = jnp.concatenate([zero, values[..., :-1]], axis=-1)
    return jnp.where(x == 0, 0.0, moved)


def shift_z(values, offset, nx, devices, count):
    rows = values.shape[1]
    if offset > 0:
        halo = lax.ppermute(values[:, :count, :nx], AXES, [(i + 1, i) for i in range(devices - 1)])
        halo = jnp.pad(halo, ((0, 0), (0, rows - count), (0, 0)))
        return jnp.concatenate([values[..., nx:], halo], axis=-1)
    halo = lax.ppermute(values[:, :count, -nx:], AXES, [(i, i + 1) for i in range(devices - 1)])
    halo = jnp.pad(halo, ((0, 0), (0, rows - count), (0, 0)))
    return jnp.concatenate([halo, values[..., :-nx]], axis=-1)


def tree_sum(terms):
    while len(terms) > 1:
        paired = [terms[i] + terms[i + 1] for i in range(0, len(terms) - 1, 2)]
        terms = paired + terms[len(paired) * 2 :]
    return terms[0]


def sweep_kernel(rhs_ref, kx_ref, ky_ref, inv_ref, out_ref, *, forward, nx, count):
    steps = rhs_ref.shape[0]
    lanes = rhs_ref.shape[2]
    x = lax.broadcasted_iota(jnp.int32, (ROWS, lanes), 1) % nx
    if forward:
        keep = x > 0
        shift = 1
    else:
        keep = x < nx - 1
        shift = lanes - 1

    def step(s, fresh):
        t = s if forward else steps - 1 - s
        from_x = jnp.where(keep, pltpu.roll(fresh, shift, 1), 0.0)
        terms = [kx_ref[t, j] * from_x[j : j + 1, :] for j in range(count)]
        terms += [ky_ref[t, j] * fresh[j : j + 1, :] for j in range(count)]
        right = rhs_ref[t] - tree_sum(terms)
        result = tree_sum([inv_ref[t, j] * right[j : j + 1, :] for j in range(count)])
        out_ref[t] = result
        return result

    lax.fori_loop(0, steps, step, jnp.zeros((ROWS, lanes), jnp.float32), unroll=2)


def sweep(rhs, along_x, along_y, inverses, forward, nx):
    count = along_x.shape[1]
    kernel = functools.partial(sweep_kernel, forward=forward, nx=nx, count=count)
    return pl.pallas_call(
        kernel,
        out_shape=jax.ShapeDtypeStruct(rhs.shape, jnp.float32),
    )(rhs, along_x, along_y, inverses)


def per_device(
    adjoint_source,
    initial,
    inverses,
    couplings,
    interface_tiles,
    source_cells,
    target_cells,
    tile_counts,
):
    n_bx = lax.axis_size("bx")
    n_by = lax.axis_size("by")
    devices = n_bx * n_by
    count, ca, cb, nz = adjoint_source.shape
    nx, ny = n_bx * ca, n_by * cb
    width = nz // devices
    steps = nx + ny
    tables = (interface_tiles, source_cells, target_cells, tile_counts)

    def to_z(values, skewer=skew):
        received = lax.all_to_all(to_slices(values, devices), AXES, 0, 0, tiled=True)
        return skewer(gather_grid(received, n_bx, n_by, ca, cb, width), steps, nx)

    def to_xy(skewed):
        rows = skewed.shape[1]
        grid = unskew(skewed, ny, nx)
        lanes = grid.shape[2]
        chunks = grid.reshape(ny * rows, lanes).T
        chunks = chunks.reshape(width, n_bx, ca, n_by, cb * rows)
        chunks = jnp.transpose(chunks, (1, 3, 0, 2, 4)).reshape(devices, width * ca * cb * rows)
        received = lax.all_to_all(chunks, AXES, 0, 0, tiled=True)
        flat = received.reshape(devices * width, ca * cb * rows).T
        flat = flat.reshape(ca, cb, rows, nz)
        return jnp.transpose(flat, (2, 0, 1, 3))[:count]

    def small_to_z(values):
        padded = jnp.pad(values, ((0, ROWS - count), (0, 0), (0, 0), (0, 0)))
        flat = jnp.transpose(padded, (1, 2, 0, 3)).reshape(ca * cb * ROWS, nz)
        chunks = flat.T.reshape(devices, width * ca * cb * ROWS)
        received = lax.all_to_all(chunks, AXES, 0, 0, tiled=True)
        shaped = received.reshape(n_bx, n_by, width, ca, cb * ROWS)
        shaped = jnp.transpose(shaped, (2, 0, 3, 1, 4)).reshape(width * nx, ny * ROWS)
        return skew(shaped.T.reshape(ny, ROWS, width * nx), steps, nx)

    span = count * count
    sweep_rows = to_z(
        jnp.concatenate(
            [
                jnp.swapaxes(inverses, 0, 1).reshape(span, ca, cb, nz),
                jnp.swapaxes(couplings[0::2][:2], 1, 2).astype(jnp.float32).reshape(2 * span, ca, cb, nz),
            ],
            axis=0,
        ),
        skew_big,
    )
    base = adjoint_source - interface(initial, *tables)
    other_rows = to_z(
        jnp.concatenate(
            [
                jnp.swapaxes(couplings[jnp.array([1, 3, 4, 5])], 1, 2).astype(jnp.float32).reshape(4 * span, ca, cb, nz),
                base,
                initial,
            ],
            axis=0,
        ),
        skew_big,
    )
    inv = as_matrices(sweep_rows[:, :span], count)
    ks = [None] * 6
    ks[0] = as_matrices(sweep_rows[:, span : 2 * span], count)
    ks[2] = as_matrices(sweep_rows[:, 2 * span : 3 * span], count)
    for place, k in enumerate((1, 3, 4, 5)):
        ks[k] = as_matrices(other_rows[:, span * place : span * (place + 1)], count)
    base_z = as_vectors(other_rows[:, 4 * span : 4 * span + count])
    iterate = as_vectors(other_rows[:, 4 * span + count : 4 * span + 2 * count])

    for number in range(ITERS):
        if number > 0:
            inter = interface(to_xy(iterate), *tables)
            base_z = small_to_z(adjoint_source - inter)
        lower_terms = (
            base_z
            - matvec(ks[1], shift_x(shift_t(iterate, 1), 1, nx))
            - matvec(ks[3], shift_t(iterate, 1))
            - matvec(ks[4], shift_z(iterate, -1, nx, devices, count))
            - matvec(ks[5], shift_z(iterate, 1, nx, devices, count))
        )
        half = sweep(lower_terms, ks[0], ks[2], inv, True, nx)
        upper_terms = (
            base_z
            - matvec(ks[0], shift_x(shift_t(half, -1), -1, nx))
            - matvec(ks[2], shift_t(half, -1))
            - matvec(ks[4], shift_z(half, -1, nx, devices, count))
            - matvec(ks[5], shift_z(half, 1, nx, devices, count))
        )
        iterate = sweep(upper_terms, ks[1], ks[3], inv, False, nx)
    return to_xy(iterate)


def solution(mesh):
    return jax.shard_map(
        per_device,
        mesh=mesh,
        in_specs=(
            P(None, "bx", "by", None),
            P(None, "bx", "by", None),
            P(None, None, "bx", "by", None),
            P(None, None, None, "bx", "by", None),
            P(AXES, None, None, None),
            P(AXES, None),
            P(AXES, None),
            P(AXES, None),
        ),
        out_specs=P(None, "bx", "by", None),
        check_vma=False,
    )
```

```python
import functools

import jax
import jax.numpy as jnp
from jax import lax
from jax.experimental import pallas as pl
from jax.experimental.pallas import tpu as pltpu
from jax.sharding import PartitionSpec as P

ITERS = 2
AXES = ("bx", "by")
ROWS = 8


def interface(iterate, interface_tiles, source_cells, target_cells, tile_counts):
    var_count = iterate.shape[0]
    flat_cells = iterate.reshape(var_count, -1)
    block_count = lax.axis_size("bx") * lax.axis_size("by")
    slot_count = source_cells.shape[1]
    per_pair = slot_count // block_count
    picked = jnp.take(flat_cells, source_cells[0], axis=1)
    products = jnp.sum(interface_tiles[0] * picked[None], axis=1)
    slot_ids = jnp.arange(slot_count, dtype=jnp.int32)
    limits = jnp.repeat(tile_counts[0], per_pair)
    products = jnp.where((slot_ids % per_pair)[None] < limits[None], products, 0.0)
    arrived = lax.all_to_all(products, AXES, split_axis=1, concat_axis=1, tiled=True)
    summed = jnp.zeros_like(flat_cells).at[:, target_cells[0]].add(arrived)
    return summed.reshape(iterate.shape)


def to_slices(values, devices):
    count, ca, cb, nz = values.shape
    shaped = jnp.transpose(values, (3, 1, 2, 0))
    return shaped.reshape(devices, (nz // devices) * ca * cb, count)


def gather_grid(received, n_bx, n_by, ca, cb, width):
    count = received.shape[2]
    shaped = received.reshape(n_bx, n_by, width, ca, cb, count)
    shaped = jnp.transpose(shaped, (1, 4, 5, 2, 0, 3))
    return shaped.reshape(n_by * cb, count, width * n_bx * ca)


def scatter_grid(grid, n_bx, n_by, ca, cb, width):
    ny, count, lanes = grid.shape
    shaped = grid.reshape(n_by, cb, count, width, n_bx, ca)
    shaped = jnp.transpose(shaped, (4, 0, 3, 5, 1, 2))
    return shaped.reshape(n_bx * n_by, width * ca * cb, count)


def from_slices(received, ca, cb):
    src, rows, count = received.shape
    width = rows // (ca * cb)
    shaped = received.reshape(src * width, ca, cb, count)
    return jnp.transpose(shaped, (3, 1, 2, 0))


def lane_x(shape, nx):
    return lax.broadcasted_iota(jnp.int32, shape, len(shape) - 1) % nx


def skew(grid, steps, nx):
    ny = grid.shape[0]
    values = jnp.pad(grid, ((0, steps - ny), (0, 0), (0, 0)))
    x = lane_x(values.shape, nx)
    bit = 1
    while bit < nx:
        values = lax.optimization_barrier(values)
        moved = jnp.concatenate([jnp.zeros_like(values[:bit]), values[:-bit]], axis=0)
        values = jnp.where((x & bit) != 0, moved, values)
        bit *= 2
    return values


def skew_kernel(grid_ref, out_ref, *, nx):
    ny = grid_ref.shape[0]
    steps = out_ref.shape[0]
    out_ref[:ny] = grid_ref[...]
    out_ref[ny:] = jnp.zeros((steps - ny,) + out_ref.shape[1:], jnp.float32)
    x = lax.broadcasted_iota(jnp.int32, out_ref.shape[1:], 1) % nx
    bit = 1
    while bit < nx:
        moves = (x & bit) != 0

        def body(i, carry, bit=bit, moves=moves):
            t = steps - 1 - i
            out_ref[t] = jnp.where(moves, out_ref[t - bit], out_ref[t])
            return carry

        lax.fori_loop(0, steps - bit, body, 0)
        for t in range(bit):
            out_ref[t] = jnp.where(moves, 0.0, out_ref[t])
        bit *= 2


def skew_big(grid, steps, nx):
    ny, count, lanes = grid.shape
    return pl.pallas_call(
        functools.partial(skew_kernel, nx=nx),
        out_shape=jax.ShapeDtypeStruct((steps, count, lanes), jnp.float32),
    )(grid)


def unskew(values, ny, nx):
    x = lane_x(values.shape, nx)
    bit = 1
    while bit < nx:
        values = lax.optimization_barrier(values)
        moved = jnp.concatenate([values[bit:], jnp.zeros_like(values[:bit])], axis=0)
        values = jnp.where((x & bit) != 0, moved, values)
        bit *= 2
    return values[:ny]


def as_vectors(rows):
    return jnp.pad(rows, ((0, 0), (0, ROWS - rows.shape[1]), (0, 0)))


def as_matrices(rows, count):
    steps, _, lanes = rows.shape
    shaped = rows.reshape(steps, count, count, lanes)
    return jnp.pad(shaped, ((0, 0), (0, 0), (0, ROWS - count), (0, 0)))


def matvec(matrix, vector):
    count = matrix.shape[1]
    return jnp.sum(matrix * vector[:, :count, None, :], axis=1)


def shift_t(values, offset):
    zero = jnp.zeros_like(values[:1])
    if offset > 0:
        return jnp.concatenate([values[1:], zero], axis=0)
    return jnp.concatenate([zero, values[:-1]], axis=0)


def shift_x(values, offset, nx):
    x = lane_x(values.shape, nx)
    zero = jnp.zeros_like(values[..., :1])
    if offset > 0:
        moved = jnp.concatenate([values[..., 1:], zero], axis=-1)
        return jnp.where(x == nx - 1, 0.0, moved)
    moved = jnp.concatenate([zero, values[..., :-1]], axis=-1)
    return jnp.where(x == 0, 0.0, moved)


def shift_z(values, offset, nx, devices, count):
    rows = values.shape[1]
    if offset > 0:
        halo = lax.ppermute(values[:, :count, :nx], AXES, [(i + 1, i) for i in range(devices - 1)])
        halo = jnp.pad(halo, ((0, 0), (0, rows - count), (0, 0)))
        return jnp.concatenate([values[..., nx:], halo], axis=-1)
    halo = lax.ppermute(values[:, :count, -nx:], AXES, [(i, i + 1) for i in range(devices - 1)])
    halo = jnp.pad(halo, ((0, 0), (0, rows - count), (0, 0)))
    return jnp.concatenate([halo, values[..., :-nx]], axis=-1)


def tree_sum(terms):
    while len(terms) > 1:
        paired = [terms[i] + terms[i + 1] for i in range(0, len(terms) - 1, 2)]
        terms = paired + terms[len(paired) * 2 :]
    return terms[0]


def sweep_kernel(rhs_ref, kx_ref, ky_ref, inv_ref, out_ref, *, forward, nx, count):
    steps = rhs_ref.shape[0]
    lanes = rhs_ref.shape[2]
    x = lax.broadcasted_iota(jnp.int32, (ROWS, lanes), 1) % nx
    if forward:
        keep = x > 0
        shift = 1
    else:
        keep = x < nx - 1
        shift = lanes - 1

    def step(s, fresh):
        t = s if forward else steps - 1 - s
        from_x = jnp.where(keep, pltpu.roll(fresh, shift, 1), 0.0)
        terms = [kx_ref[t, j] * from_x[j : j + 1, :] for j in range(count)]
        terms += [ky_ref[t, j] * fresh[j : j + 1, :] for j in range(count)]
        right = rhs_ref[t] - tree_sum(terms)
        result = tree_sum([inv_ref[t, j] * right[j : j + 1, :] for j in range(count)])
        out_ref[t] = result
        return result

    lax.fori_loop(0, steps, step, jnp.zeros((ROWS, lanes), jnp.float32), unroll=2)


def sweep(rhs, along_x, along_y, inverses, forward, nx):
    count = along_x.shape[1]
    kernel = functools.partial(sweep_kernel, forward=forward, nx=nx, count=count)
    return pl.pallas_call(
        kernel,
        out_shape=jax.ShapeDtypeStruct(rhs.shape, jnp.float32),
    )(rhs, along_x, along_y, inverses)


def per_device(
    adjoint_source,
    initial,
    inverses,
    couplings,
    interface_tiles,
    source_cells,
    target_cells,
    tile_counts,
):
    n_bx = lax.axis_size("bx")
    n_by = lax.axis_size("by")
    devices = n_bx * n_by
    count, ca, cb, nz = adjoint_source.shape
    nx, ny = n_bx * ca, n_by * cb
    width = nz // devices
    steps = nx + ny
    tables = (interface_tiles, source_cells, target_cells, tile_counts)

    def to_z(values, skewer=skew):
        received = lax.all_to_all(to_slices(values, devices), AXES, 0, 0, tiled=True)
        return skewer(gather_grid(received, n_bx, n_by, ca, cb, width), steps, nx)

    def to_xy(skewed):
        rows = skewed.shape[1]
        grid = unskew(skewed, ny, nx)
        lanes = grid.shape[2]
        chunks = grid.reshape(ny * rows, lanes).T
        chunks = chunks.reshape(width, n_bx, ca, n_by, cb * rows)
        chunks = jnp.transpose(chunks, (1, 3, 0, 2, 4)).reshape(devices, width * ca * cb * rows)
        received = lax.all_to_all(chunks, AXES, 0, 0, tiled=True)
        flat = received.reshape(devices * width, ca * cb * rows).T
        flat = flat.reshape(ca, cb, rows, nz)
        return jnp.transpose(flat, (2, 0, 1, 3))[:count]

    def small_to_z(values):
        padded = jnp.pad(values, ((0, ROWS - count), (0, 0), (0, 0), (0, 0)))
        flat = jnp.transpose(padded, (1, 2, 0, 3)).reshape(ca * cb * ROWS, nz)
        chunks = flat.T.reshape(devices, width * ca * cb * ROWS)
        received = lax.all_to_all(chunks, AXES, 0, 0, tiled=True)
        shaped = received.reshape(n_bx, n_by, width, ca, cb * ROWS)
        shaped = jnp.transpose(shaped, (2, 0, 3, 1, 4)).reshape(width * nx, ny * ROWS)
        return skew(shaped.T.reshape(ny, ROWS, width * nx), steps, nx)

    span = count * count
    sweep_rows = to_z(
        jnp.concatenate(
            [
                jnp.swapaxes(inverses, 0, 1).reshape(span, ca, cb, nz),
                jnp.swapaxes(couplings[0::2][:2], 1, 2).astype(jnp.float32).reshape(2 * span, ca, cb, nz),
            ],
            axis=0,
        ),
        skew_big,
    )
    base = adjoint_source - interface(initial, *tables)
    other_rows = to_z(
        jnp.concatenate(
            [
                jnp.swapaxes(couplings[jnp.array([1, 3, 4, 5])], 1, 2).astype(jnp.float32).reshape(4 * span, ca, cb, nz),
                initial,
            ],
            axis=0,
        ),
        skew_big,
    )
    inv = as_matrices(sweep_rows[:, :span], count)
    ks = [None] * 6
    ks[0] = as_matrices(sweep_rows[:, span : 2 * span], count)
    ks[2] = as_matrices(sweep_rows[:, 2 * span : 3 * span], count)
    for place, k in enumerate((1, 3, 4, 5)):
        ks[k] = as_matrices(other_rows[:, span * place : span * (place + 1)], count)
    iterate = as_vectors(other_rows[:, 4 * span : 4 * span + count])
    base_z = small_to_z(base)

    for number in range(ITERS):
        if number > 0:
            inter = interface(to_xy(iterate), *tables)
            base_z = small_to_z(adjoint_source - inter)
        lower_terms = (
            base_z
            - matvec(ks[1], shift_x(shift_t(iterate, 1), 1, nx))
            - matvec(ks[3], shift_t(iterate, 1))
            - matvec(ks[4], shift_z(iterate, -1, nx, devices, count))
            - matvec(ks[5], shift_z(iterate, 1, nx, devices, count))
        )
        half = sweep(lower_terms, ks[0], ks[2], inv, True, nx)
        upper_terms = (
            base_z
            - matvec(ks[0], shift_x(shift_t(half, -1), -1, nx))
            - matvec(ks[2], shift_t(half, -1))
            - matvec(ks[4], shift_z(half, -1, nx, devices, count))
            - matvec(ks[5], shift_z(half, 1, nx, devices, count))
        )
        iterate = sweep(upper_terms, ks[1], ks[3], inv, False, nx)
    return to_xy(iterate)


def solution(mesh):
    return jax.shard_map(
        per_device,
        mesh=mesh,
        in_specs=(
            P(None, "bx", "by", None),
            P(None, "bx", "by", None),
            P(None, None, "bx", "by", None),
            P(None, None, None, "bx", "by", None),
            P(AXES, None, None, None),
            P(AXES, None),
            P(AXES, None),
            P(AXES, None),
        ),
        out_specs=P(None, "bx", "by", None),
        check_vma=False,
    )
```

```python
import functools

import jax
import jax.numpy as jnp
from jax import lax
from jax.experimental import pallas as pl
from jax.experimental.pallas import tpu as pltpu
from jax.sharding import PartitionSpec as P

ITERS = 2
AXES = ("bx", "by")
ROWS = 8


def interface(iterate, interface_tiles, source_cells, target_cells, tile_counts):
    var_count = iterate.shape[0]
    flat_cells = iterate.reshape(var_count, -1)
    block_count = lax.axis_size("bx") * lax.axis_size("by")
    slot_count = source_cells.shape[1]
    per_pair = slot_count // block_count
    picked = jnp.take(flat_cells, source_cells[0], axis=1)
    products = jnp.sum(interface_tiles[0] * picked[None], axis=1)
    slot_ids = jnp.arange(slot_count, dtype=jnp.int32)
    limits = jnp.repeat(tile_counts[0], per_pair)
    products = jnp.where((slot_ids % per_pair)[None] < limits[None], products, 0.0)
    arrived = lax.all_to_all(products, AXES, split_axis=1, concat_axis=1, tiled=True)
    summed = jnp.zeros_like(flat_cells).at[:, target_cells[0]].add(arrived)
    return summed.reshape(iterate.shape)


def to_slices(values, devices):
    count, ca, cb, nz = values.shape
    shaped = jnp.transpose(values, (3, 1, 2, 0))
    return shaped.reshape(devices, (nz // devices) * ca * cb, count)


def gather_grid(received, n_bx, n_by, ca, cb, width):
    count = received.shape[2]
    shaped = received.reshape(n_bx, n_by, width, ca, cb, count)
    shaped = jnp.transpose(shaped, (1, 4, 5, 2, 0, 3))
    return shaped.reshape(n_by * cb, count, width * n_bx * ca)


def scatter_grid(grid, n_bx, n_by, ca, cb, width):
    ny, count, lanes = grid.shape
    shaped = grid.reshape(n_by, cb, count, width, n_bx, ca)
    shaped = jnp.transpose(shaped, (4, 0, 3, 5, 1, 2))
    return shaped.reshape(n_bx * n_by, width * ca * cb, count)


def from_slices(received, ca, cb):
    src, rows, count = received.shape
    width = rows // (ca * cb)
    shaped = received.reshape(src * width, ca, cb, count)
    return jnp.transpose(shaped, (3, 1, 2, 0))


def lane_x(shape, nx):
    return lax.broadcasted_iota(jnp.int32, shape, len(shape) - 1) % nx


def skew(grid, steps, nx):
    ny = grid.shape[0]
    values = jnp.pad(grid, ((0, steps - ny), (0, 0), (0, 0)))
    x = lane_x(values.shape, nx)
    bit = 1
    while bit < nx:
        values = lax.optimization_barrier(values)
        moved = jnp.concatenate([jnp.zeros_like(values[:bit]), values[:-bit]], axis=0)
        values = jnp.where((x & bit) != 0, moved, values)
        bit *= 2
    return values


def skew_kernel(grid_ref, out_ref, *, nx):
    ny = grid_ref.shape[0]
    steps = out_ref.shape[0]
    out_ref[:ny] = grid_ref[...]
    out_ref[ny:] = jnp.zeros((steps - ny,) + out_ref.shape[1:], jnp.float32)
    x = lax.broadcasted_iota(jnp.int32, out_ref.shape[1:], 1) % nx
    bit = 1
    while bit < nx:
        moves = (x & bit) != 0

        def body(i, carry, bit=bit, moves=moves):
            t = steps - 1 - i
            out_ref[t] = jnp.where(moves, out_ref[t - bit], out_ref[t])
            return carry

        lax.fori_loop(0, steps - bit, body, 0)
        for t in range(bit):
            out_ref[t] = jnp.where(moves, 0.0, out_ref[t])
        bit *= 2


def skew_big(grid, steps, nx):
    ny, count, lanes = grid.shape
    return pl.pallas_call(
        functools.partial(skew_kernel, nx=nx),
        out_shape=jax.ShapeDtypeStruct((steps, count, lanes), jnp.float32),
    )(grid)


def unskew(values, ny, nx):
    x = lane_x(values.shape, nx)
    bit = 1
    while bit < nx:
        values = lax.optimization_barrier(values)
        moved = jnp.concatenate([values[bit:], jnp.zeros_like(values[:bit])], axis=0)
        values = jnp.where((x & bit) != 0, moved, values)
        bit *= 2
    return values[:ny]


def as_vectors(rows):
    return jnp.pad(rows, ((0, 0), (0, ROWS - rows.shape[1]), (0, 0)))


def as_matrices(rows, count):
    steps, _, lanes = rows.shape
    shaped = rows.reshape(steps, count, count, lanes)
    return jnp.pad(shaped, ((0, 0), (0, 0), (0, ROWS - count), (0, 0)))


def matvec(source, off, vector):
    count = vector.shape[1]
    return tree_sum([source[:, off + count * j : off + count * (j + 1), :] * vector[:, j : j + 1, :] for j in range(count)])


def shift_t(values, offset):
    zero = jnp.zeros_like(values[:1])
    if offset > 0:
        return jnp.concatenate([values[1:], zero], axis=0)
    return jnp.concatenate([zero, values[:-1]], axis=0)


def shift_x(values, offset, nx):
    x = lane_x(values.shape, nx)
    zero = jnp.zeros_like(values[..., :1])
    if offset > 0:
        moved = jnp.concatenate([values[..., 1:], zero], axis=-1)
        return jnp.where(x == nx - 1, 0.0, moved)
    moved = jnp.concatenate([zero, values[..., :-1]], axis=-1)
    return jnp.where(x == 0, 0.0, moved)


def shift_z(values, offset, nx, devices, count):
    rows = values.shape[1]
    if offset > 0:
        halo = lax.ppermute(values[:, :count, :nx], AXES, [(i + 1, i) for i in range(devices - 1)])
        halo = jnp.pad(halo, ((0, 0), (0, rows - count), (0, 0)))
        return jnp.concatenate([values[..., nx:], halo], axis=-1)
    halo = lax.ppermute(values[:, :count, -nx:], AXES, [(i, i + 1) for i in range(devices - 1)])
    halo = jnp.pad(halo, ((0, 0), (0, rows - count), (0, 0)))
    return jnp.concatenate([halo, values[..., :-nx]], axis=-1)


def tree_sum(terms):
    while len(terms) > 1:
        paired = [terms[i] + terms[i + 1] for i in range(0, len(terms) - 1, 2)]
        terms = paired + terms[len(paired) * 2 :]
    return terms[0]


def sweep_kernel(rhs_ref, *refs, forward, nx, count, places):
    out_ref = refs[-1]
    steps = rhs_ref.shape[0]
    lanes = rhs_ref.shape[2]
    x = lax.broadcasted_iota(jnp.int32, (count, lanes), 1) % nx
    if forward:
        keep = x > 0
        shift = 1
    else:
        keep = x < nx - 1
        shift = lanes - 1
    (kx_at, kx_off), (ky_at, ky_off), (inv_at, inv_off) = places

    def column(at, off, t, j):
        return refs[at][t, pl.ds(off + count * j, count), :]

    def step(s, fresh):
        t = s if forward else steps - 1 - s
        from_x = jnp.where(keep, pltpu.roll(fresh, shift, 1), 0.0)
        terms = [column(kx_at, kx_off, t, j) * from_x[j : j + 1, :] for j in range(count)]
        terms += [column(ky_at, ky_off, t, j) * fresh[j : j + 1, :] for j in range(count)]
        right = rhs_ref[t] - tree_sum(terms)
        result = tree_sum([column(inv_at, inv_off, t, j) * right[j : j + 1, :] for j in range(count)])
        out_ref[t] = result
        return result

    lax.fori_loop(0, steps, step, jnp.zeros((count, lanes), jnp.float32), unroll=2)


def sweep(rhs, sources, places, forward, nx):
    count = rhs.shape[1]
    kernel = functools.partial(sweep_kernel, forward=forward, nx=nx, count=count, places=places)
    specs = [pl.BlockSpec(rhs.shape, lambda i: (0, 0, 0))]
    for source in sources:
        needed = max(off + count * count for at, off in places if sources[at] is source)
        rows = min(source.shape[1], -(-needed // ROWS) * ROWS)
        specs.append(pl.BlockSpec((source.shape[0], rows, source.shape[2]), lambda i: (0, 0, 0)))
    return pl.pallas_call(
        kernel,
        grid=(1,),
        in_specs=specs,
        out_specs=pl.BlockSpec(rhs.shape, lambda i: (0, 0, 0)),
        out_shape=jax.ShapeDtypeStruct(rhs.shape, jnp.float32),
    )(rhs, *sources)


def per_device(
    adjoint_source,
    initial,
    inverses,
    couplings,
    interface_tiles,
    source_cells,
    target_cells,
    tile_counts,
):
    n_bx = lax.axis_size("bx")
    n_by = lax.axis_size("by")
    devices = n_bx * n_by
    count, ca, cb, nz = adjoint_source.shape
    nx, ny = n_bx * ca, n_by * cb
    width = nz // devices
    steps = nx + ny
    tables = (interface_tiles, source_cells, target_cells, tile_counts)

    def to_z(values, skewer=skew):
        received = lax.all_to_all(to_slices(values, devices), AXES, 0, 0, tiled=True)
        return skewer(gather_grid(received, n_bx, n_by, ca, cb, width), steps, nx)

    def to_xy(skewed):
        rows = ROWS
        grid = unskew(jnp.pad(skewed, ((0, 0), (0, rows - skewed.shape[1]), (0, 0))), ny, nx)
        lanes = grid.shape[2]
        chunks = grid.reshape(ny * rows, lanes).T
        chunks = chunks.reshape(width, n_bx, ca, n_by, cb * rows)
        chunks = jnp.transpose(chunks, (1, 3, 0, 2, 4)).reshape(devices, width * ca * cb * rows)
        received = lax.all_to_all(chunks, AXES, 0, 0, tiled=True)
        flat = received.reshape(devices * width, ca * cb * rows).T
        flat = flat.reshape(ca, cb, rows, nz)
        return jnp.transpose(flat, (2, 0, 1, 3))[:count]

    def small_to_z(values):
        padded = jnp.pad(values, ((0, ROWS - count), (0, 0), (0, 0), (0, 0)))
        flat = jnp.transpose(padded, (1, 2, 0, 3)).reshape(ca * cb * ROWS, nz)
        chunks = flat.T.reshape(devices, width * ca * cb * ROWS)
        received = lax.all_to_all(chunks, AXES, 0, 0, tiled=True)
        shaped = received.reshape(n_bx, n_by, width, ca, cb * ROWS)
        shaped = jnp.transpose(shaped, (2, 0, 3, 1, 4)).reshape(width * nx, ny * ROWS)
        return skew(shaped.T.reshape(ny, ROWS, width * nx), steps, nx)

    span = count * count
    sweep_rows = to_z(
        jnp.concatenate(
            [
                jnp.swapaxes(inverses, 0, 1).reshape(span, ca, cb, nz),
                jnp.swapaxes(couplings[0::2][:2], 1, 2).astype(jnp.float32).reshape(2 * span, ca, cb, nz),
            ],
            axis=0,
        ),
        skew_big,
    )
    base = adjoint_source - interface(initial, *tables)
    other_rows = to_z(
        jnp.concatenate(
            [
                jnp.swapaxes(couplings[jnp.array([1, 3, 4, 5])], 1, 2).astype(jnp.float32).reshape(4 * span, ca, cb, nz),
                base,
                initial,
            ],
            axis=0,
        ),
        skew_big,
    )
    base_z = other_rows[:, 4 * span : 4 * span + count]
    iterate = other_rows[:, 4 * span + count : 4 * span + 2 * count]
    forward_places = ((0, span), (0, 2 * span), (0, 0))
    backward_places = ((0, 0), (0, span), (1, 0))

    for number in range(ITERS):
        if number > 0:
            inter = interface(to_xy(iterate), *tables)
            base_z = small_to_z(adjoint_source - inter)[:, :count]
        lower_terms = base_z - (
            matvec(other_rows, 0, shift_x(shift_t(iterate, 1), 1, nx))
            + matvec(other_rows, span, shift_t(iterate, 1))
            + matvec(other_rows, 2 * span, shift_z(iterate, -1, nx, devices, count))
            + matvec(other_rows, 3 * span, shift_z(iterate, 1, nx, devices, count))
        )
        half = sweep(lower_terms, (sweep_rows,), forward_places, True, nx)
        upper_terms = base_z - (
            matvec(sweep_rows, span, shift_x(shift_t(half, -1), -1, nx))
            + matvec(sweep_rows, 2 * span, shift_t(half, -1))
            + matvec(other_rows, 2 * span, shift_z(half, -1, nx, devices, count))
            + matvec(other_rows, 3 * span, shift_z(half, 1, nx, devices, count))
        )
        iterate = sweep(upper_terms, (other_rows, sweep_rows), backward_places, False, nx)
    return to_xy(iterate)


def solution(mesh):
    return jax.shard_map(
        per_device,
        mesh=mesh,
        in_specs=(
            P(None, "bx", "by", None),
            P(None, "bx", "by", None),
            P(None, None, "bx", "by", None),
            P(None, None, None, "bx", "by", None),
            P(AXES, None, None, None),
            P(AXES, None),
            P(AXES, None),
            P(AXES, None),
        ),
        out_specs=P(None, "bx", "by", None),
        check_vma=False,
    )
```

```python
import functools

import jax
import jax.numpy as jnp
from jax import lax
from jax.experimental import pallas as pl
from jax.experimental.pallas import tpu as pltpu
from jax.sharding import PartitionSpec as P

ITERS = 2
AXES = ("bx", "by")
ROWS = 8


def interface(iterate, interface_tiles, source_cells, target_cells, tile_counts):
    var_count = iterate.shape[0]
    flat_cells = iterate.reshape(var_count, -1)
    block_count = lax.axis_size("bx") * lax.axis_size("by")
    slot_count = source_cells.shape[1]
    per_pair = slot_count // block_count
    picked = jnp.take(flat_cells, source_cells[0], axis=1)
    products = jnp.sum(interface_tiles[0] * picked[None], axis=1)
    slot_ids = jnp.arange(slot_count, dtype=jnp.int32)
    limits = jnp.repeat(tile_counts[0], per_pair)
    products = jnp.where((slot_ids % per_pair)[None] < limits[None], products, 0.0)
    arrived = lax.all_to_all(products, AXES, split_axis=1, concat_axis=1, tiled=True)
    summed = jnp.zeros_like(flat_cells).at[:, target_cells[0]].add(arrived)
    return summed.reshape(iterate.shape)


def to_slices(values, devices):
    count, ca, cb, nz = values.shape
    shaped = jnp.transpose(values, (3, 1, 2, 0))
    return shaped.reshape(devices, (nz // devices) * ca * cb, count)


def gather_grid(received, n_bx, n_by, ca, cb, width):
    count = received.shape[2]
    shaped = received.reshape(n_bx, n_by, width, ca, cb, count)
    shaped = jnp.transpose(shaped, (1, 4, 5, 2, 0, 3))
    return shaped.reshape(n_by * cb, count, width * n_bx * ca)


def scatter_grid(grid, n_bx, n_by, ca, cb, width):
    ny, count, lanes = grid.shape
    shaped = grid.reshape(n_by, cb, count, width, n_bx, ca)
    shaped = jnp.transpose(shaped, (4, 0, 3, 5, 1, 2))
    return shaped.reshape(n_bx * n_by, width * ca * cb, count)


def from_slices(received, ca, cb):
    src, rows, count = received.shape
    width = rows // (ca * cb)
    shaped = received.reshape(src * width, ca, cb, count)
    return jnp.transpose(shaped, (3, 1, 2, 0))


def lane_x(shape, nx):
    return lax.broadcasted_iota(jnp.int32, shape, len(shape) - 1) % nx


def skew(grid, steps, nx):
    ny = grid.shape[0]
    values = jnp.pad(grid, ((0, steps - ny), (0, 0), (0, 0)))
    x = lane_x(values.shape, nx)
    bit = 1
    while bit < nx:
        values = lax.optimization_barrier(values)
        moved = jnp.concatenate([jnp.zeros_like(values[:bit]), values[:-bit]], axis=0)
        values = jnp.where((x & bit) != 0, moved, values)
        bit *= 2
    return values


def skew_kernel(grid_ref, out_ref, *, nx):
    ny = grid_ref.shape[0]
    steps = out_ref.shape[0]
    out_ref[:ny] = grid_ref[...]
    out_ref[ny:] = jnp.zeros((steps - ny,) + out_ref.shape[1:], jnp.float32)
    x = lax.broadcasted_iota(jnp.int32, out_ref.shape[1:], 1) % nx
    bit = 1
    while bit < nx:
        moves = (x & bit) != 0

        def body(i, carry, bit=bit, moves=moves):
            t = steps - 1 - i
            out_ref[t] = jnp.where(moves, out_ref[t - bit], out_ref[t])
            return carry

        lax.fori_loop(0, steps - bit, body, 0)
        for t in range(bit):
            out_ref[t] = jnp.where(moves, 0.0, out_ref[t])
        bit *= 2


def skew_big(grid, steps, nx):
    ny, count, lanes = grid.shape
    return pl.pallas_call(
        functools.partial(skew_kernel, nx=nx),
        out_shape=jax.ShapeDtypeStruct((steps, count, lanes), jnp.float32),
    )(grid)


def unskew(values, ny, nx):
    x = lane_x(values.shape, nx)
    bit = 1
    while bit < nx:
        values = lax.optimization_barrier(values)
        moved = jnp.concatenate([values[bit:], jnp.zeros_like(values[:bit])], axis=0)
        values = jnp.where((x & bit) != 0, moved, values)
        bit *= 2
    return values[:ny]


def as_vectors(rows):
    return jnp.pad(rows, ((0, 0), (0, ROWS - rows.shape[1]), (0, 0)))


def as_matrices(rows, count):
    steps, _, lanes = rows.shape
    shaped = rows.reshape(steps, count, count, lanes)
    return jnp.pad(shaped, ((0, 0), (0, 0), (0, ROWS - count), (0, 0)))


def matvec(source, off, vector):
    count = vector.shape[1]
    return tree_sum([source[:, off + count * j : off + count * (j + 1), :] * vector[:, j : j + 1, :] for j in range(count)])


def shift_t(values, offset):
    zero = jnp.zeros_like(values[:1])
    if offset > 0:
        return jnp.concatenate([values[1:], zero], axis=0)
    return jnp.concatenate([zero, values[:-1]], axis=0)


def shift_x(values, offset, nx):
    x = lane_x(values.shape, nx)
    zero = jnp.zeros_like(values[..., :1])
    if offset > 0:
        moved = jnp.concatenate([values[..., 1:], zero], axis=-1)
        return jnp.where(x == nx - 1, 0.0, moved)
    moved = jnp.concatenate([zero, values[..., :-1]], axis=-1)
    return jnp.where(x == 0, 0.0, moved)


def shift_z(values, offset, nx, devices, count):
    rows = values.shape[1]
    if offset > 0:
        halo = lax.ppermute(values[:, :count, :nx], AXES, [(i + 1, i) for i in range(devices - 1)])
        halo = jnp.pad(halo, ((0, 0), (0, rows - count), (0, 0)))
        return jnp.concatenate([values[..., nx:], halo], axis=-1)
    halo = lax.ppermute(values[:, :count, -nx:], AXES, [(i, i + 1) for i in range(devices - 1)])
    halo = jnp.pad(halo, ((0, 0), (0, rows - count), (0, 0)))
    return jnp.concatenate([halo, values[..., :-nx]], axis=-1)


def tree_sum(terms):
    while len(terms) > 1:
        paired = [terms[i] + terms[i + 1] for i in range(0, len(terms) - 1, 2)]
        terms = paired + terms[len(paired) * 2 :]
    return terms[0]


def sweep_kernel(rhs_ref, *refs, forward, nx, count, places):
    out_ref = refs[-1]
    steps = rhs_ref.shape[0]
    lanes = rhs_ref.shape[2]
    x = lax.broadcasted_iota(jnp.int32, (count, lanes), 1) % nx
    if forward:
        keep = x > 0
        shift = 1
    else:
        keep = x < nx - 1
        shift = lanes - 1
    (kx_at, kx_off), (ky_at, ky_off), (inv_at, inv_off) = places

    def column(at, off, t, j):
        return refs[at][t, pl.ds(off + count * j, count), :]

    def step(s, fresh):
        t = s if forward else steps - 1 - s
        from_x = jnp.where(keep, pltpu.roll(fresh, shift, 1), 0.0)
        terms = [column(kx_at, kx_off, t, j) * from_x[j : j + 1, :] for j in range(count)]
        terms += [column(ky_at, ky_off, t, j) * fresh[j : j + 1, :] for j in range(count)]
        right = rhs_ref[t] - tree_sum(terms)
        result = tree_sum([column(inv_at, inv_off, t, j) * right[j : j + 1, :] for j in range(count)])
        out_ref[t] = result
        return result

    lax.fori_loop(0, steps, step, jnp.zeros((count, lanes), jnp.float32), unroll=2)


def sweep(rhs, sources, places, forward, nx):
    count = rhs.shape[1]
    kernel = functools.partial(sweep_kernel, forward=forward, nx=nx, count=count, places=places)
    specs = [pl.BlockSpec(rhs.shape, lambda i: (0, 0, 0))]
    for source in sources:
        needed = max(off + count * count for at, off in places if sources[at] is source)
        rows = min(source.shape[1], -(-needed // ROWS) * ROWS)
        specs.append(pl.BlockSpec((source.shape[0], rows, source.shape[2]), lambda i: (0, 0, 0)))
    return pl.pallas_call(
        kernel,
        grid=(1,),
        in_specs=specs,
        out_specs=pl.BlockSpec(rhs.shape, lambda i: (0, 0, 0)),
        out_shape=jax.ShapeDtypeStruct(rhs.shape, jnp.float32),
    )(rhs, *sources)


def per_device(
    adjoint_source,
    initial,
    inverses,
    couplings,
    interface_tiles,
    source_cells,
    target_cells,
    tile_counts,
):
    n_bx = lax.axis_size("bx")
    n_by = lax.axis_size("by")
    devices = n_bx * n_by
    count, ca, cb, nz = adjoint_source.shape
    nx, ny = n_bx * ca, n_by * cb
    width = nz // devices
    steps = nx + ny
    tables = (interface_tiles, source_cells, target_cells, tile_counts)

    def to_z(values, skewer=skew):
        received = lax.all_to_all(to_slices(values, devices), AXES, 0, 0, tiled=True)
        return skewer(gather_grid(received, n_bx, n_by, ca, cb, width), steps, nx)

    def to_xy(skewed):
        rows = ROWS
        grid = unskew(jnp.pad(skewed, ((0, 0), (0, rows - skewed.shape[1]), (0, 0))), ny, nx)
        lanes = grid.shape[2]
        chunks = grid.reshape(ny * rows, lanes).T
        chunks = chunks.reshape(width, n_bx, ca, n_by, cb * rows)
        chunks = jnp.transpose(chunks, (1, 3, 0, 2, 4)).reshape(devices, width * ca * cb * rows)
        received = lax.all_to_all(chunks, AXES, 0, 0, tiled=True)
        flat = received.reshape(devices * width, ca * cb * rows).T
        flat = flat.reshape(ca, cb, rows, nz)
        return jnp.transpose(flat, (2, 0, 1, 3))[:count]

    def small_to_z(values):
        padded = jnp.pad(values, ((0, ROWS - count), (0, 0), (0, 0), (0, 0)))
        flat = jnp.transpose(padded, (1, 2, 0, 3)).reshape(ca * cb * ROWS, nz)
        chunks = flat.T.reshape(devices, width * ca * cb * ROWS)
        received = lax.all_to_all(chunks, AXES, 0, 0, tiled=True)
        shaped = received.reshape(n_bx, n_by, width, ca, cb * ROWS)
        shaped = jnp.transpose(shaped, (2, 0, 3, 1, 4)).reshape(width * nx, ny * ROWS)
        return skew(shaped.T.reshape(ny, ROWS, width * nx), steps, nx)

    span = count * count
    sweep_rows = to_z(
        jnp.concatenate(
            [
                jnp.swapaxes(inverses, 0, 1).reshape(span, ca, cb, nz),
                jnp.swapaxes(couplings[0::2][:2], 1, 2).astype(jnp.float32).reshape(2 * span, ca, cb, nz),
            ],
            axis=0,
        ),
        skew_big,
    )
    base = adjoint_source - interface(initial, *tables)
    below = jnp.concatenate([jnp.zeros_like(initial[..., :1]), initial[..., :-1]], axis=-1)
    above = jnp.concatenate([initial[..., 1:], jnp.zeros_like(initial[..., :1])], axis=-1)
    along_z = couplings[4].astype(jnp.float32) * below[None] + couplings[5].astype(jnp.float32) * above[None]
    lower_base = base - jnp.sum(along_z, axis=1)
    other_rows = to_z(
        jnp.concatenate(
            [
                jnp.swapaxes(couplings[jnp.array([1, 3, 4, 5])], 1, 2).astype(jnp.float32).reshape(4 * span, ca, cb, nz),
                base,
                lower_base,
                initial,
            ],
            axis=0,
        ),
        skew_big,
    )
    base_z = other_rows[:, 4 * span : 4 * span + count]
    lower_z = other_rows[:, 4 * span + count : 4 * span + 2 * count]
    iterate = other_rows[:, 4 * span + 2 * count : 4 * span + 3 * count]
    forward_places = ((0, span), (0, 2 * span), (0, 0))
    backward_places = ((0, 0), (0, span), (1, 0))

    for number in range(ITERS):
        if number > 0:
            inter = interface(to_xy(iterate), *tables)
            base_z = small_to_z(adjoint_source - inter)[:, :count]
        if number > 0:
            lower_z = base_z - (
                matvec(other_rows, 2 * span, shift_z(iterate, -1, nx, devices, count))
                + matvec(other_rows, 3 * span, shift_z(iterate, 1, nx, devices, count))
            )
        lower_terms = lower_z - (
            matvec(other_rows, 0, shift_x(shift_t(iterate, 1), 1, nx))
            + matvec(other_rows, span, shift_t(iterate, 1))
        )
        half = sweep(lower_terms, (sweep_rows,), forward_places, True, nx)
        upper_terms = base_z - (
            matvec(sweep_rows, span, shift_x(shift_t(half, -1), -1, nx))
            + matvec(sweep_rows, 2 * span, shift_t(half, -1))
            + matvec(other_rows, 2 * span, shift_z(half, -1, nx, devices, count))
            + matvec(other_rows, 3 * span, shift_z(half, 1, nx, devices, count))
        )
        iterate = sweep(upper_terms, (other_rows, sweep_rows), backward_places, False, nx)
    return to_xy(iterate)


def solution(mesh):
    return jax.shard_map(
        per_device,
        mesh=mesh,
        in_specs=(
            P(None, "bx", "by", None),
            P(None, "bx", "by", None),
            P(None, None, "bx", "by", None),
            P(None, None, None, "bx", "by", None),
            P(AXES, None, None, None),
            P(AXES, None),
            P(AXES, None),
            P(AXES, None),
        ),
        out_specs=P(None, "bx", "by", None),
        check_vma=False,
    )
```

```python
import functools

import jax
import jax.numpy as jnp
from jax import lax
from jax.experimental import pallas as pl
from jax.experimental.pallas import tpu as pltpu
from jax.sharding import PartitionSpec as P

ITERS = 2
AXES = ("bx", "by")
ROWS = 8


def interface(iterate, interface_tiles, source_cells, target_cells, tile_counts):
    var_count = iterate.shape[0]
    flat_cells = iterate.reshape(var_count, -1)
    block_count = lax.axis_size("bx") * lax.axis_size("by")
    slot_count = source_cells.shape[1]
    per_pair = slot_count // block_count
    picked = jnp.take(flat_cells, source_cells[0], axis=1)
    products = jnp.sum(interface_tiles[0] * picked[None], axis=1)
    slot_ids = jnp.arange(slot_count, dtype=jnp.int32)
    limits = jnp.repeat(tile_counts[0], per_pair)
    products = jnp.where((slot_ids % per_pair)[None] < limits[None], products, 0.0)
    arrived = lax.all_to_all(products, AXES, split_axis=1, concat_axis=1, tiled=True)
    summed = jnp.zeros_like(flat_cells).at[:, target_cells[0]].add(arrived)
    return summed.reshape(iterate.shape)


def to_slices(values, devices):
    count, ca, cb, nz = values.shape
    shaped = jnp.transpose(values, (3, 1, 2, 0))
    return shaped.reshape(devices, (nz // devices) * ca * cb, count)


def gather_grid(received, n_bx, n_by, ca, cb, width):
    count = received.shape[2]
    shaped = received.reshape(n_bx, n_by, width, ca, cb, count)
    shaped = jnp.transpose(shaped, (1, 4, 5, 2, 0, 3))
    return shaped.reshape(n_by * cb, count, width * n_bx * ca)


def scatter_grid(grid, n_bx, n_by, ca, cb, width):
    ny, count, lanes = grid.shape
    shaped = grid.reshape(n_by, cb, count, width, n_bx, ca)
    shaped = jnp.transpose(shaped, (4, 0, 3, 5, 1, 2))
    return shaped.reshape(n_bx * n_by, width * ca * cb, count)


def from_slices(received, ca, cb):
    src, rows, count = received.shape
    width = rows // (ca * cb)
    shaped = received.reshape(src * width, ca, cb, count)
    return jnp.transpose(shaped, (3, 1, 2, 0))


def lane_x(shape, nx):
    return lax.broadcasted_iota(jnp.int32, shape, len(shape) - 1) % nx


def skew(grid, steps, nx):
    ny = grid.shape[0]
    values = jnp.pad(grid, ((0, steps - ny), (0, 0), (0, 0)))
    x = lane_x(values.shape, nx)
    bit = 1
    while bit < nx:
        values = lax.optimization_barrier(values)
        moved = jnp.concatenate([jnp.zeros_like(values[:bit]), values[:-bit]], axis=0)
        values = jnp.where((x & bit) != 0, moved, values)
        bit *= 2
    return values


def skew_kernel(grid_ref, out_ref, *, nx):
    ny = grid_ref.shape[0]
    steps = out_ref.shape[0]
    out_ref[:ny] = grid_ref[...]
    out_ref[ny:] = jnp.zeros((steps - ny,) + out_ref.shape[1:], jnp.float32)
    x = lax.broadcasted_iota(jnp.int32, out_ref.shape[1:], 1) % nx
    bit = 1
    while bit < nx:
        moves = (x & bit) != 0

        def body(i, carry, bit=bit, moves=moves):
            t = steps - 1 - i
            out_ref[t] = jnp.where(moves, out_ref[t - bit], out_ref[t])
            return carry

        lax.fori_loop(0, steps - bit, body, 0)
        for t in range(bit):
            out_ref[t] = jnp.where(moves, 0.0, out_ref[t])
        bit *= 2


def skew_big(grid, steps, nx):
    ny, count, lanes = grid.shape
    return pl.pallas_call(
        functools.partial(skew_kernel, nx=nx),
        out_shape=jax.ShapeDtypeStruct((steps, count, lanes), jnp.float32),
    )(grid)


def unskew(values, ny, nx):
    x = lane_x(values.shape, nx)
    bit = 1
    while bit < nx:
        values = lax.optimization_barrier(values)
        moved = jnp.concatenate([values[bit:], jnp.zeros_like(values[:bit])], axis=0)
        values = jnp.where((x & bit) != 0, moved, values)
        bit *= 2
    return values[:ny]


def as_vectors(rows):
    return jnp.pad(rows, ((0, 0), (0, ROWS - rows.shape[1]), (0, 0)))


def as_matrices(rows, count):
    steps, _, lanes = rows.shape
    shaped = rows.reshape(steps, count, count, lanes)
    return jnp.pad(shaped, ((0, 0), (0, 0), (0, ROWS - count), (0, 0)))


def matvec(source, off, vector):
    count = vector.shape[1]
    return tree_sum([source[:, off + count * j : off + count * (j + 1), :] * vector[:, j : j + 1, :] for j in range(count)])


def shift_t(values, offset):
    zero = jnp.zeros_like(values[:1])
    if offset > 0:
        return jnp.concatenate([values[1:], zero], axis=0)
    return jnp.concatenate([zero, values[:-1]], axis=0)


def shift_x(values, offset, nx):
    x = lane_x(values.shape, nx)
    zero = jnp.zeros_like(values[..., :1])
    if offset > 0:
        moved = jnp.concatenate([values[..., 1:], zero], axis=-1)
        return jnp.where(x == nx - 1, 0.0, moved)
    moved = jnp.concatenate([zero, values[..., :-1]], axis=-1)
    return jnp.where(x == 0, 0.0, moved)


def shift_z(values, offset, nx, devices, count):
    rows = values.shape[1]
    if offset > 0:
        halo = lax.ppermute(values[:, :count, :nx], AXES, [(i + 1, i) for i in range(devices - 1)])
        halo = jnp.pad(halo, ((0, 0), (0, rows - count), (0, 0)))
        return jnp.concatenate([values[..., nx:], halo], axis=-1)
    halo = lax.ppermute(values[:, :count, -nx:], AXES, [(i, i + 1) for i in range(devices - 1)])
    halo = jnp.pad(halo, ((0, 0), (0, rows - count), (0, 0)))
    return jnp.concatenate([halo, values[..., :-nx]], axis=-1)


def tree_sum(terms):
    while len(terms) > 1:
        paired = [terms[i] + terms[i + 1] for i in range(0, len(terms) - 1, 2)]
        terms = paired + terms[len(paired) * 2 :]
    return terms[0]


def sweep_kernel(rhs_ref, *refs, forward, nx, count, places):
    out_ref = refs[-2]
    carry_ref = refs[-1]
    steps = rhs_ref.shape[0]
    lanes = rhs_ref.shape[2]
    x = lax.broadcasted_iota(jnp.int32, (count, lanes), 1) % nx
    if forward:
        keep = x > 0
        shift = 1
    else:
        keep = x < nx - 1
        shift = lanes - 1
    (kx_at, kx_off), (ky_at, ky_off), (inv_at, inv_off) = places

    @pl.when(pl.program_id(0) == 0)
    def _():
        carry_ref[...] = jnp.zeros((count, lanes), jnp.float32)

    def column(at, off, t, j):
        return refs[at][t, pl.ds(off + count * j, count), :]

    def step(s, fresh):
        t = s if forward else steps - 1 - s
        from_x = jnp.where(keep, pltpu.roll(fresh, shift, 1), 0.0)
        terms = [column(kx_at, kx_off, t, j) * from_x[j : j + 1, :] for j in range(count)]
        terms += [column(ky_at, ky_off, t, j) * fresh[j : j + 1, :] for j in range(count)]
        right = rhs_ref[t] - tree_sum(terms)
        result = tree_sum([column(inv_at, inv_off, t, j) * right[j : j + 1, :] for j in range(count)])
        out_ref[t] = result
        return result

    carry_ref[...] = lax.fori_loop(0, steps, step, carry_ref[...], unroll=2)


def sweep(rhs, sources, places, forward, nx, chunks=4):
    steps, count, lanes = rhs.shape
    size = steps // chunks
    if forward:
        where = lambda i: (i, 0, 0)
    else:
        where = lambda i: (chunks - 1 - i, 0, 0)
    kernel = functools.partial(sweep_kernel, forward=forward, nx=nx, count=count, places=places)
    specs = [pl.BlockSpec((size, count, lanes), where)]
    for source in sources:
        needed = max(off + count * count for at, off in places if sources[at] is source)
        rows = min(source.shape[1], -(-needed // ROWS) * ROWS)
        specs.append(pl.BlockSpec((size, rows, source.shape[2]), where))
    return pl.pallas_call(
        kernel,
        grid=(chunks,),
        in_specs=specs,
        out_specs=pl.BlockSpec((size, count, lanes), where),
        out_shape=jax.ShapeDtypeStruct(rhs.shape, jnp.float32),
        scratch_shapes=[pltpu.VMEM((count, lanes), jnp.float32)],
    )(rhs, *sources)


def per_device(
    adjoint_source,
    initial,
    inverses,
    couplings,
    interface_tiles,
    source_cells,
    target_cells,
    tile_counts,
):
    n_bx = lax.axis_size("bx")
    n_by = lax.axis_size("by")
    devices = n_bx * n_by
    count, ca, cb, nz = adjoint_source.shape
    nx, ny = n_bx * ca, n_by * cb
    width = nz // devices
    steps = nx + ny
    tables = (interface_tiles, source_cells, target_cells, tile_counts)

    def to_z(values, skewer=skew):
        received = lax.all_to_all(to_slices(values, devices), AXES, 0, 0, tiled=True)
        return skewer(gather_grid(received, n_bx, n_by, ca, cb, width), steps, nx)

    def to_xy(skewed):
        rows = ROWS
        grid = unskew(jnp.pad(skewed, ((0, 0), (0, rows - skewed.shape[1]), (0, 0))), ny, nx)
        lanes = grid.shape[2]
        chunks = grid.reshape(ny * rows, lanes).T
        chunks = chunks.reshape(width, n_bx, ca, n_by, cb * rows)
        chunks = jnp.transpose(chunks, (1, 3, 0, 2, 4)).reshape(devices, width * ca * cb * rows)
        received = lax.all_to_all(chunks, AXES, 0, 0, tiled=True)
        flat = received.reshape(devices * width, ca * cb * rows).T
        flat = flat.reshape(ca, cb, rows, nz)
        return jnp.transpose(flat, (2, 0, 1, 3))[:count]

    def small_to_z(values):
        padded = jnp.pad(values, ((0, ROWS - count), (0, 0), (0, 0), (0, 0)))
        flat = jnp.transpose(padded, (1, 2, 0, 3)).reshape(ca * cb * ROWS, nz)
        chunks = flat.T.reshape(devices, width * ca * cb * ROWS)
        received = lax.all_to_all(chunks, AXES, 0, 0, tiled=True)
        shaped = received.reshape(n_bx, n_by, width, ca, cb * ROWS)
        shaped = jnp.transpose(shaped, (2, 0, 3, 1, 4)).reshape(width * nx, ny * ROWS)
        return skew(shaped.T.reshape(ny, ROWS, width * nx), steps, nx)

    span = count * count
    sweep_rows = to_z(
        jnp.concatenate(
            [
                jnp.swapaxes(inverses, 0, 1).reshape(span, ca, cb, nz),
                jnp.swapaxes(couplings[0::2][:2], 1, 2).astype(jnp.float32).reshape(2 * span, ca, cb, nz),
            ],
            axis=0,
        ),
        skew_big,
    )
    base = adjoint_source - interface(initial, *tables)
    below = jnp.concatenate([jnp.zeros_like(initial[..., :1]), initial[..., :-1]], axis=-1)
    above = jnp.concatenate([initial[..., 1:], jnp.zeros_like(initial[..., :1])], axis=-1)
    along_z = couplings[4].astype(jnp.float32) * below[None] + couplings[5].astype(jnp.float32) * above[None]
    lower_base = base - jnp.sum(along_z, axis=1)
    other_rows = to_z(
        jnp.concatenate(
            [
                jnp.swapaxes(couplings[jnp.array([1, 3, 4, 5])], 1, 2).astype(jnp.float32).reshape(4 * span, ca, cb, nz),
                base,
                lower_base,
                initial,
            ],
            axis=0,
        ),
        skew_big,
    )
    base_z = other_rows[:, 4 * span : 4 * span + count]
    lower_z = other_rows[:, 4 * span + count : 4 * span + 2 * count]
    iterate = other_rows[:, 4 * span + 2 * count : 4 * span + 3 * count]
    forward_places = ((0, span), (0, 2 * span), (0, 0))
    backward_places = ((0, 0), (0, span), (1, 0))

    for number in range(ITERS):
        if number > 0:
            inter = interface(to_xy(iterate), *tables)
            base_z = small_to_z(adjoint_source - inter)[:, :count]
        if number > 0:
            lower_z = base_z - (
                matvec(other_rows, 2 * span, shift_z(iterate, -1, nx, devices, count))
                + matvec(other_rows, 3 * span, shift_z(iterate, 1, nx, devices, count))
            )
        lower_terms = lower_z - (
            matvec(other_rows, 0, shift_x(shift_t(iterate, 1), 1, nx))
            + matvec(other_rows, span, shift_t(iterate, 1))
        )
        half = sweep(lower_terms, (sweep_rows,), forward_places, True, nx)
        upper_terms = base_z - (
            matvec(sweep_rows, span, shift_x(shift_t(half, -1), -1, nx))
            + matvec(sweep_rows, 2 * span, shift_t(half, -1))
            + matvec(other_rows, 2 * span, shift_z(half, -1, nx, devices, count))
            + matvec(other_rows, 3 * span, shift_z(half, 1, nx, devices, count))
        )
        iterate = sweep(upper_terms, (other_rows, sweep_rows), backward_places, False, nx)
    return to_xy(iterate)


def solution(mesh):
    return jax.shard_map(
        per_device,
        mesh=mesh,
        in_specs=(
            P(None, "bx", "by", None),
            P(None, "bx", "by", None),
            P(None, None, "bx", "by", None),
            P(None, None, None, "bx", "by", None),
            P(AXES, None, None, None),
            P(AXES, None),
            P(AXES, None),
            P(AXES, None),
        ),
        out_specs=P(None, "bx", "by", None),
        check_vma=False,
    )
```

```python
import functools

import jax
import jax.numpy as jnp
from jax import lax
from jax.experimental import pallas as pl
from jax.experimental.pallas import tpu as pltpu
from jax.sharding import PartitionSpec as P

ITERS = 2
AXES = ("bx", "by")
ROWS = 8


def interface(iterate, interface_tiles, source_cells, target_cells, tile_counts):
    var_count = iterate.shape[0]
    flat_cells = iterate.reshape(var_count, -1)
    block_count = lax.axis_size("bx") * lax.axis_size("by")
    slot_count = source_cells.shape[1]
    per_pair = slot_count // block_count
    picked = jnp.take(flat_cells, source_cells[0], axis=1)
    products = jnp.sum(interface_tiles[0] * picked[None], axis=1)
    slot_ids = jnp.arange(slot_count, dtype=jnp.int32)
    limits = jnp.repeat(tile_counts[0], per_pair)
    products = jnp.where((slot_ids % per_pair)[None] < limits[None], products, 0.0)
    arrived = lax.all_to_all(products, AXES, split_axis=1, concat_axis=1, tiled=True)
    summed = jnp.zeros_like(flat_cells).at[:, target_cells[0]].add(arrived)
    return summed.reshape(iterate.shape)


def to_slices(values, devices):
    count, ca, cb, nz = values.shape
    shaped = jnp.transpose(values, (3, 1, 2, 0))
    return shaped.reshape(devices, (nz // devices) * ca * cb, count)


def gather_grid(received, n_bx, n_by, ca, cb, width):
    count = received.shape[2]
    shaped = received.reshape(n_bx, n_by, width, ca, cb, count)
    shaped = jnp.transpose(shaped, (1, 4, 5, 2, 0, 3))
    return shaped.reshape(n_by * cb, count, width * n_bx * ca)


def scatter_grid(grid, n_bx, n_by, ca, cb, width):
    ny, count, lanes = grid.shape
    shaped = grid.reshape(n_by, cb, count, width, n_bx, ca)
    shaped = jnp.transpose(shaped, (4, 0, 3, 5, 1, 2))
    return shaped.reshape(n_bx * n_by, width * ca * cb, count)


def from_slices(received, ca, cb):
    src, rows, count = received.shape
    width = rows // (ca * cb)
    shaped = received.reshape(src * width, ca, cb, count)
    return jnp.transpose(shaped, (3, 1, 2, 0))


def lane_x(shape, nx):
    return lax.broadcasted_iota(jnp.int32, shape, len(shape) - 1) % nx


def skew(grid, steps, nx):
    ny = grid.shape[0]
    values = jnp.pad(grid, ((0, steps - ny), (0, 0), (0, 0)))
    x = lane_x(values.shape, nx)
    bit = 1
    while bit < nx:
        values = lax.optimization_barrier(values)
        moved = jnp.concatenate([jnp.zeros_like(values[:bit]), values[:-bit]], axis=0)
        values = jnp.where((x & bit) != 0, moved, values)
        bit *= 2
    return values


def skew_kernel(grid_ref, out_ref, *, nx):
    ny = grid_ref.shape[0]
    steps = out_ref.shape[0]
    out_ref[:ny] = grid_ref[...]
    out_ref[ny:] = jnp.zeros((steps - ny,) + out_ref.shape[1:], jnp.float32)
    x = lax.broadcasted_iota(jnp.int32, out_ref.shape[1:], 1) % nx
    bit = 1
    while bit < nx:
        moves = (x & bit) != 0

        def body(i, carry, bit=bit, moves=moves):
            t = steps - 1 - i
            out_ref[t] = jnp.where(moves, out_ref[t - bit], out_ref[t])
            return carry

        lax.fori_loop(0, steps - bit, body, 0)
        for t in range(bit):
            out_ref[t] = jnp.where(moves, 0.0, out_ref[t])
        bit *= 2


def skew_big(grid, steps, nx):
    ny, count, lanes = grid.shape
    return pl.pallas_call(
        functools.partial(skew_kernel, nx=nx),
        out_shape=jax.ShapeDtypeStruct((steps, count, lanes), jnp.float32),
    )(grid)


def unskew(values, ny, nx):
    x = lane_x(values.shape, nx)
    bit = 1
    while bit < nx:
        values = lax.optimization_barrier(values)
        moved = jnp.concatenate([values[bit:], jnp.zeros_like(values[:bit])], axis=0)
        values = jnp.where((x & bit) != 0, moved, values)
        bit *= 2
    return values[:ny]


def as_vectors(rows):
    return jnp.pad(rows, ((0, 0), (0, ROWS - rows.shape[1]), (0, 0)))


def as_matrices(rows, count):
    steps, _, lanes = rows.shape
    shaped = rows.reshape(steps, count, count, lanes)
    return jnp.pad(shaped, ((0, 0), (0, 0), (0, ROWS - count), (0, 0)))


def matvec(source, off, vector):
    count = vector.shape[1]
    return tree_sum([source[:, off + count * j : off + count * (j + 1), :] * vector[:, j : j + 1, :] for j in range(count)])


def shift_t(values, offset):
    zero = jnp.zeros_like(values[:1])
    if offset > 0:
        return jnp.concatenate([values[1:], zero], axis=0)
    return jnp.concatenate([zero, values[:-1]], axis=0)


def shift_x(values, offset, nx):
    x = lane_x(values.shape, nx)
    zero = jnp.zeros_like(values[..., :1])
    if offset > 0:
        moved = jnp.concatenate([values[..., 1:], zero], axis=-1)
        return jnp.where(x == nx - 1, 0.0, moved)
    moved = jnp.concatenate([zero, values[..., :-1]], axis=-1)
    return jnp.where(x == 0, 0.0, moved)


def shift_z(values, offset, nx, devices, count):
    rows = values.shape[1]
    if offset > 0:
        halo = lax.ppermute(values[:, :count, :nx], AXES, [(i + 1, i) for i in range(devices - 1)])
        halo = jnp.pad(halo, ((0, 0), (0, rows - count), (0, 0)))
        return jnp.concatenate([values[..., nx:], halo], axis=-1)
    halo = lax.ppermute(values[:, :count, -nx:], AXES, [(i, i + 1) for i in range(devices - 1)])
    halo = jnp.pad(halo, ((0, 0), (0, rows - count), (0, 0)))
    return jnp.concatenate([halo, values[..., :-nx]], axis=-1)


def tree_sum(terms):
    while len(terms) > 1:
        paired = [terms[i] + terms[i + 1] for i in range(0, len(terms) - 1, 2)]
        terms = paired + terms[len(paired) * 2 :]
    return terms[0]


def sweep_kernel(rhs_ref, *refs, forward, nx, count, places):
    out_ref = refs[-2]
    carry_ref = refs[-1]
    steps = rhs_ref.shape[0]
    lanes = rhs_ref.shape[2]
    x = lax.broadcasted_iota(jnp.int32, (count, lanes), 1) % nx
    if forward:
        keep = x > 0
        shift = 1
    else:
        keep = x < nx - 1
        shift = lanes - 1
    (kx_at, kx_off), (ky_at, ky_off), (inv_at, inv_off) = places

    @pl.when(pl.program_id(0) == 0)
    def _():
        carry_ref[...] = jnp.zeros((count, lanes), jnp.float32)

    def column(at, off, t, j):
        return refs[at][t, pl.ds(off + count * j, count), :]

    def step(s, fresh):
        t = s if forward else steps - 1 - s
        from_x = jnp.where(keep, pltpu.roll(fresh, shift, 1), 0.0)
        terms = [column(kx_at, kx_off, t, j) * from_x[j : j + 1, :] for j in range(count)]
        terms += [column(ky_at, ky_off, t, j) * fresh[j : j + 1, :] for j in range(count)]
        right = rhs_ref[t] - tree_sum(terms)
        result = tree_sum([column(inv_at, inv_off, t, j) * right[j : j + 1, :] for j in range(count)])
        out_ref[t] = result
        return result

    carry_ref[...] = lax.fori_loop(0, steps, step, carry_ref[...], unroll=2)


def sweep(rhs, sources, places, forward, nx, chunks=4):
    steps, count, lanes = rhs.shape
    size = steps // chunks
    if forward:
        where = lambda i: (i, 0, 0)
    else:
        where = lambda i: (chunks - 1 - i, 0, 0)
    kernel = functools.partial(sweep_kernel, forward=forward, nx=nx, count=count, places=places)
    specs = [pl.BlockSpec((size, count, lanes), where)]
    for source in sources:
        needed = max(off + count * count for at, off in places if sources[at] is source)
        rows = min(source.shape[1], -(-needed // ROWS) * ROWS)
        specs.append(pl.BlockSpec((size, rows, source.shape[2]), where))
    return pl.pallas_call(
        kernel,
        grid=(chunks,),
        in_specs=specs,
        out_specs=pl.BlockSpec((size, count, lanes), where),
        out_shape=jax.ShapeDtypeStruct(rhs.shape, jnp.float32),
        scratch_shapes=[pltpu.VMEM((count, lanes), jnp.float32)],
    )(rhs, *sources)


def per_device(
    adjoint_source,
    initial,
    inverses,
    couplings,
    interface_tiles,
    source_cells,
    target_cells,
    tile_counts,
):
    n_bx = lax.axis_size("bx")
    n_by = lax.axis_size("by")
    devices = n_bx * n_by
    count, ca, cb, nz = adjoint_source.shape
    nx, ny = n_bx * ca, n_by * cb
    width = nz // devices
    steps = nx + ny
    tables = (interface_tiles, source_cells, target_cells, tile_counts)

    def to_z(values, skewer=skew):
        received = lax.all_to_all(to_slices(values, devices), AXES, 0, 0, tiled=True)
        return skewer(gather_grid(received, n_bx, n_by, ca, cb, width), steps, nx)

    def to_xy(skewed):
        rows = ROWS
        grid = unskew(jnp.pad(skewed, ((0, 0), (0, rows - skewed.shape[1]), (0, 0))), ny, nx)
        lanes = grid.shape[2]
        chunks = grid.reshape(ny * rows, lanes).T
        chunks = chunks.reshape(width, n_bx, ca, n_by, cb * rows)
        chunks = jnp.transpose(chunks, (1, 3, 0, 2, 4)).reshape(devices, width * ca * cb * rows)
        received = lax.all_to_all(chunks, AXES, 0, 0, tiled=True)
        flat = received.reshape(devices * width, ca * cb * rows).T
        flat = flat.reshape(ca, cb, rows, nz)
        return jnp.transpose(flat, (2, 0, 1, 3))[:count]

    def small_to_z(values):
        rows = -(-values.shape[0] // ROWS) * ROWS
        padded = jnp.pad(values, ((0, rows - values.shape[0]), (0, 0), (0, 0), (0, 0)))
        flat = jnp.transpose(padded, (1, 2, 0, 3)).reshape(ca * cb * rows, nz)
        chunks = flat.T.reshape(devices, width * ca * cb * rows)
        received = lax.all_to_all(chunks, AXES, 0, 0, tiled=True)
        shaped = received.reshape(n_bx, n_by, width, ca, cb * rows)
        shaped = jnp.transpose(shaped, (2, 0, 3, 1, 4)).reshape(width * nx, ny * rows)
        return skew(shaped.T.reshape(ny, rows, width * nx), steps, nx)

    span = count * count
    sweep_rows = to_z(
        jnp.concatenate(
            [
                jnp.swapaxes(inverses, 0, 1).reshape(span, ca, cb, nz),
                jnp.swapaxes(couplings[0::2][:2], 1, 2).astype(jnp.float32).reshape(2 * span, ca, cb, nz),
            ],
            axis=0,
        ),
        skew_big,
    )
    base = adjoint_source - interface(initial, *tables)
    below = jnp.concatenate([jnp.zeros_like(initial[..., :1]), initial[..., :-1]], axis=-1)
    above = jnp.concatenate([initial[..., 1:], jnp.zeros_like(initial[..., :1])], axis=-1)
    along_z = couplings[4].astype(jnp.float32) * below[None] + couplings[5].astype(jnp.float32) * above[None]
    lower_base = base - jnp.sum(along_z, axis=1)
    other_sent = jnp.concatenate(
        [
            jnp.swapaxes(couplings[jnp.array([1, 3, 4, 5])], 1, 2).astype(jnp.float32).reshape(4 * span, ca, cb, nz),
            initial,
        ],
        axis=0,
    )
    other_received = lax.all_to_all(to_slices(other_sent, devices), AXES, 0, 0, tiled=True)
    pair = jnp.concatenate([base, lower_base], axis=0)
    pair, other_received = lax.optimization_barrier((pair, other_received))
    other_rows = skew_big(gather_grid(other_received, n_bx, n_by, ca, cb, width), steps, nx)
    iterate = other_rows[:, 4 * span : 4 * span + count]
    bases = small_to_z(pair)
    base_z = bases[:, :count]
    lower_z = bases[:, count : 2 * count]
    forward_places = ((0, span), (0, 2 * span), (0, 0))
    backward_places = ((0, 0), (0, span), (1, 0))

    for number in range(ITERS):
        if number > 0:
            inter = interface(to_xy(iterate), *tables)
            base_z = small_to_z(adjoint_source - inter)[:, :count]
        if number > 0:
            lower_z = base_z - (
                matvec(other_rows, 2 * span, shift_z(iterate, -1, nx, devices, count))
                + matvec(other_rows, 3 * span, shift_z(iterate, 1, nx, devices, count))
            )
        lower_terms = lower_z - (
            matvec(other_rows, 0, shift_x(shift_t(iterate, 1), 1, nx))
            + matvec(other_rows, span, shift_t(iterate, 1))
        )
        half = sweep(lower_terms, (sweep_rows,), forward_places, True, nx)
        upper_terms = base_z - (
            matvec(sweep_rows, span, shift_x(shift_t(half, -1), -1, nx))
            + matvec(sweep_rows, 2 * span, shift_t(half, -1))
            + matvec(other_rows, 2 * span, shift_z(half, -1, nx, devices, count))
            + matvec(other_rows, 3 * span, shift_z(half, 1, nx, devices, count))
        )
        iterate = sweep(upper_terms, (other_rows, sweep_rows), backward_places, False, nx)
    return to_xy(iterate)


def solution(mesh):
    return jax.shard_map(
        per_device,
        mesh=mesh,
        in_specs=(
            P(None, "bx", "by", None),
            P(None, "bx", "by", None),
            P(None, None, "bx", "by", None),
            P(None, None, None, "bx", "by", None),
            P(AXES, None, None, None),
            P(AXES, None),
            P(AXES, None),
            P(AXES, None),
        ),
        out_specs=P(None, "bx", "by", None),
        check_vma=False,
    )
```

```python
import functools

import jax
import jax.numpy as jnp
from jax import lax
from jax.experimental import pallas as pl
from jax.experimental.pallas import tpu as pltpu
from jax.sharding import PartitionSpec as P

ITERS = 2
AXES = ("bx", "by")
ROWS = 8


def interface(iterate, interface_tiles, source_cells, target_cells, tile_counts):
    var_count = iterate.shape[0]
    flat_cells = iterate.reshape(var_count, -1)
    block_count = lax.axis_size("bx") * lax.axis_size("by")
    slot_count = source_cells.shape[1]
    per_pair = slot_count // block_count
    picked = jnp.take(flat_cells, source_cells[0], axis=1)
    products = jnp.sum(interface_tiles[0] * picked[None], axis=1)
    slot_ids = jnp.arange(slot_count, dtype=jnp.int32)
    limits = jnp.repeat(tile_counts[0], per_pair)
    products = jnp.where((slot_ids % per_pair)[None] < limits[None], products, 0.0)
    arrived = lax.all_to_all(products, AXES, split_axis=1, concat_axis=1, tiled=True)
    summed = jnp.zeros_like(flat_cells).at[:, target_cells[0]].add(arrived)
    return summed.reshape(iterate.shape)


def to_slices(values, devices):
    count, ca, cb, nz = values.shape
    shaped = jnp.transpose(values, (3, 1, 2, 0))
    return shaped.reshape(devices, (nz // devices) * ca * cb, count)


def gather_grid(received, n_bx, n_by, ca, cb, width):
    count = received.shape[2]
    shaped = received.reshape(n_bx, n_by, width, ca, cb, count)
    shaped = jnp.transpose(shaped, (1, 4, 5, 2, 0, 3))
    return shaped.reshape(n_by * cb, count, width * n_bx * ca)


def scatter_grid(grid, n_bx, n_by, ca, cb, width):
    ny, count, lanes = grid.shape
    shaped = grid.reshape(n_by, cb, count, width, n_bx, ca)
    shaped = jnp.transpose(shaped, (4, 0, 3, 5, 1, 2))
    return shaped.reshape(n_bx * n_by, width * ca * cb, count)


def from_slices(received, ca, cb):
    src, rows, count = received.shape
    width = rows // (ca * cb)
    shaped = received.reshape(src * width, ca, cb, count)
    return jnp.transpose(shaped, (3, 1, 2, 0))


def lane_x(shape, nx):
    return lax.broadcasted_iota(jnp.int32, shape, len(shape) - 1) % nx


def skew(grid, steps, nx):
    ny = grid.shape[0]
    values = jnp.pad(grid, ((0, steps - ny), (0, 0), (0, 0)))
    x = lane_x(values.shape, nx)
    bit = 1
    while bit < nx:
        values = lax.optimization_barrier(values)
        moved = jnp.concatenate([jnp.zeros_like(values[:bit]), values[:-bit]], axis=0)
        values = jnp.where((x & bit) != 0, moved, values)
        bit *= 2
    return values


def skew_kernel(grid_ref, out_ref, *, nx):
    ny = grid_ref.shape[0]
    steps = out_ref.shape[0]
    out_ref[:ny] = grid_ref[...]
    out_ref[ny:] = jnp.zeros((steps - ny,) + out_ref.shape[1:], jnp.float32)
    x = lax.broadcasted_iota(jnp.int32, out_ref.shape[1:], 1) % nx
    bit = 1
    while bit < nx:
        moves = (x & bit) != 0

        def body(i, carry, bit=bit, moves=moves):
            t = steps - 1 - i
            out_ref[t] = jnp.where(moves, out_ref[t - bit], out_ref[t])
            return carry

        lax.fori_loop(0, steps - bit, body, 0)
        for t in range(bit):
            out_ref[t] = jnp.where(moves, 0.0, out_ref[t])
        bit *= 2


def skew_big(grid, steps, nx):
    ny, count, lanes = grid.shape
    return pl.pallas_call(
        functools.partial(skew_kernel, nx=nx),
        out_shape=jax.ShapeDtypeStruct((steps, count, lanes), jnp.float32),
    )(grid)


def unskew(values, ny, nx):
    x = lane_x(values.shape, nx)
    bit = 1
    while bit < nx:
        values = lax.optimization_barrier(values)
        moved = jnp.concatenate([values[bit:], jnp.zeros_like(values[:bit])], axis=0)
        values = jnp.where((x & bit) != 0, moved, values)
        bit *= 2
    return values[:ny]


def as_vectors(rows):
    return jnp.pad(rows, ((0, 0), (0, ROWS - rows.shape[1]), (0, 0)))


def as_matrices(rows, count):
    steps, _, lanes = rows.shape
    shaped = rows.reshape(steps, count, count, lanes)
    return jnp.pad(shaped, ((0, 0), (0, 0), (0, ROWS - count), (0, 0)))


def matvec(source, off, vector):
    count = vector.shape[1]
    return tree_sum([source[:, off + count * j : off + count * (j + 1), :] * vector[:, j : j + 1, :] for j in range(count)])


def shift_t(values, offset):
    zero = jnp.zeros_like(values[:1])
    if offset > 0:
        return jnp.concatenate([values[1:], zero], axis=0)
    return jnp.concatenate([zero, values[:-1]], axis=0)


def shift_x(values, offset, nx):
    x = lane_x(values.shape, nx)
    zero = jnp.zeros_like(values[..., :1])
    if offset > 0:
        moved = jnp.concatenate([values[..., 1:], zero], axis=-1)
        return jnp.where(x == nx - 1, 0.0, moved)
    moved = jnp.concatenate([zero, values[..., :-1]], axis=-1)
    return jnp.where(x == 0, 0.0, moved)


def shift_z(values, offset, nx, devices, count):
    rows = values.shape[1]
    if offset > 0:
        halo = lax.ppermute(values[:, :count, :nx], AXES, [(i + 1, i) for i in range(devices - 1)])
        halo = jnp.pad(halo, ((0, 0), (0, rows - count), (0, 0)))
        return jnp.concatenate([values[..., nx:], halo], axis=-1)
    halo = lax.ppermute(values[:, :count, -nx:], AXES, [(i, i + 1) for i in range(devices - 1)])
    halo = jnp.pad(halo, ((0, 0), (0, rows - count), (0, 0)))
    return jnp.concatenate([halo, values[..., :-nx]], axis=-1)


def tree_sum(terms):
    while len(terms) > 1:
        paired = [terms[i] + terms[i + 1] for i in range(0, len(terms) - 1, 2)]
        terms = paired + terms[len(paired) * 2 :]
    return terms[0]


def sweep_kernel(rhs_ref, *refs, forward, nx, count, places):
    out_ref = refs[-2]
    carry_ref = refs[-1]
    steps = rhs_ref.shape[0]
    lanes = rhs_ref.shape[2]
    x = lax.broadcasted_iota(jnp.int32, (count, lanes), 1) % nx
    if forward:
        keep = x > 0
        shift = 1
    else:
        keep = x < nx - 1
        shift = lanes - 1
    (kx_at, kx_off), (ky_at, ky_off), (inv_at, inv_off) = places

    @pl.when(pl.program_id(0) == 0)
    def _():
        carry_ref[...] = jnp.zeros((count, lanes), jnp.float32)

    def column(at, off, t, j):
        return refs[at][t, pl.ds(off + count * j, count), :]

    def step(s, fresh):
        t = s if forward else steps - 1 - s
        from_x = jnp.where(keep, pltpu.roll(fresh, shift, 1), 0.0)
        terms = [column(kx_at, kx_off, t, j) * from_x[j : j + 1, :] for j in range(count)]
        terms += [column(ky_at, ky_off, t, j) * fresh[j : j + 1, :] for j in range(count)]
        right = rhs_ref[t] - tree_sum(terms)
        result = tree_sum([column(inv_at, inv_off, t, j) * right[j : j + 1, :] for j in range(count)])
        out_ref[t] = result
        return result

    carry_ref[...] = lax.fori_loop(0, steps, step, carry_ref[...], unroll=2)


def sweep(rhs, sources, places, forward, nx, chunks=4):
    steps, count, lanes = rhs.shape
    size = steps // chunks
    if forward:
        where = lambda i: (i, 0, 0)
    else:
        where = lambda i: (chunks - 1 - i, 0, 0)
    kernel = functools.partial(sweep_kernel, forward=forward, nx=nx, count=count, places=places)
    specs = [pl.BlockSpec((size, count, lanes), where)]
    for source in sources:
        needed = max(off + count * count for at, off in places if sources[at] is source)
        rows = min(source.shape[1], -(-needed // ROWS) * ROWS)
        specs.append(pl.BlockSpec((size, rows, source.shape[2]), where))
    return pl.pallas_call(
        kernel,
        grid=(chunks,),
        in_specs=specs,
        out_specs=pl.BlockSpec((size, count, lanes), where),
        out_shape=jax.ShapeDtypeStruct(rhs.shape, jnp.float32),
        scratch_shapes=[pltpu.VMEM((count, lanes), jnp.float32)],
    )(rhs, *sources)


def per_device(
    adjoint_source,
    initial,
    inverses,
    couplings,
    interface_tiles,
    source_cells,
    target_cells,
    tile_counts,
):
    n_bx = lax.axis_size("bx")
    n_by = lax.axis_size("by")
    devices = n_bx * n_by
    count, ca, cb, nz = adjoint_source.shape
    nx, ny = n_bx * ca, n_by * cb
    width = nz // devices
    steps = nx + ny
    tables = (interface_tiles, source_cells, target_cells, tile_counts)

    def to_z(values, skewer=skew):
        received = lax.all_to_all(to_slices(values, devices), AXES, 0, 0, tiled=True)
        return skewer(gather_grid(received, n_bx, n_by, ca, cb, width), steps, nx)

    def to_xy(skewed):
        rows = ROWS
        grid = unskew(jnp.pad(skewed, ((0, 0), (0, rows - skewed.shape[1]), (0, 0))), ny, nx)
        lanes = grid.shape[2]
        chunks = grid.reshape(ny * rows, lanes).T
        chunks = chunks.reshape(width, n_bx, ca, n_by, cb * rows)
        chunks = jnp.transpose(chunks, (1, 3, 0, 2, 4)).reshape(devices, width * ca * cb * rows)
        received = lax.all_to_all(chunks, AXES, 0, 0, tiled=True)
        flat = received.reshape(devices * width, ca * cb * rows).T
        flat = flat.reshape(ca, cb, rows, nz)
        return jnp.transpose(flat, (2, 0, 1, 3))[:count]

    def small_to_z(values):
        padded = jnp.pad(values, ((0, ROWS - count), (0, 0), (0, 0), (0, 0)))
        flat = jnp.transpose(padded, (1, 2, 0, 3)).reshape(ca * cb * ROWS, nz)
        chunks = flat.T.reshape(devices, width * ca * cb * ROWS)
        received = lax.all_to_all(chunks, AXES, 0, 0, tiled=True)
        shaped = received.reshape(n_bx, n_by, width, ca, cb * ROWS)
        shaped = jnp.transpose(shaped, (2, 0, 3, 1, 4)).reshape(width * nx, ny * ROWS)
        return skew(shaped.T.reshape(ny, ROWS, width * nx), steps, nx)

    span = count * count
    sweep_rows = to_z(
        jnp.concatenate(
            [
                jnp.swapaxes(inverses, 0, 1).reshape(span, ca, cb, nz),
                jnp.swapaxes(couplings[0::2][:2], 1, 2).astype(jnp.float32).reshape(2 * span, ca, cb, nz),
            ],
            axis=0,
        ),
        skew_big,
    )
    base = adjoint_source - interface(initial, *tables)
    below = jnp.concatenate([jnp.zeros_like(initial[..., :1]), initial[..., :-1]], axis=-1)
    above = jnp.concatenate([initial[..., 1:], jnp.zeros_like(initial[..., :1])], axis=-1)
    along_z = couplings[4].astype(jnp.float32) * below[None] + couplings[5].astype(jnp.float32) * above[None]
    lower_base = base - jnp.sum(along_z, axis=1)
    other_rows = to_z(
        jnp.concatenate(
            [
                jnp.swapaxes(couplings[jnp.array([1, 3, 4, 5])], 1, 2).astype(jnp.float32).reshape(4 * span, ca, cb, nz),
                base,
                lower_base,
                initial,
            ],
            axis=0,
        ),
        skew_big,
    )
    base_z = other_rows[:, 4 * span : 4 * span + count]
    lower_z = other_rows[:, 4 * span + count : 4 * span + 2 * count]
    iterate = other_rows[:, 4 * span + 2 * count : 4 * span + 3 * count]
    forward_places = ((0, span), (0, 2 * span), (0, 0))
    backward_places = ((0, 0), (0, span), (1, 0))

    for number in range(ITERS):
        if number > 0:
            inter = interface(to_xy(iterate), *tables)
            base_z = small_to_z(adjoint_source - inter)[:, :count]
        in_plane = lax.optimization_barrier(
            matvec(other_rows, 0, shift_x(shift_t(iterate, 1), 1, nx))
            + matvec(other_rows, span, shift_t(iterate, 1))
        )
        if number > 0:
            lower_z = base_z - (
                matvec(other_rows, 2 * span, shift_z(iterate, -1, nx, devices, count))
                + matvec(other_rows, 3 * span, shift_z(iterate, 1, nx, devices, count))
            )
        lower_terms = lower_z - in_plane
        half = sweep(lower_terms, (sweep_rows,), forward_places, True, nx)
        in_plane = lax.optimization_barrier(
            matvec(sweep_rows, span, shift_x(shift_t(half, -1), -1, nx))
            + matvec(sweep_rows, 2 * span, shift_t(half, -1))
        )
        upper_terms = (base_z - in_plane) - (
            matvec(other_rows, 2 * span, shift_z(half, -1, nx, devices, count))
            + matvec(other_rows, 3 * span, shift_z(half, 1, nx, devices, count))
        )
        iterate = sweep(upper_terms, (other_rows, sweep_rows), backward_places, False, nx)
    return to_xy(iterate)


def solution(mesh):
    return jax.shard_map(
        per_device,
        mesh=mesh,
        in_specs=(
            P(None, "bx", "by", None),
            P(None, "bx", "by", None),
            P(None, None, "bx", "by", None),
            P(None, None, None, "bx", "by", None),
            P(AXES, None, None, None),
            P(AXES, None),
            P(AXES, None),
            P(AXES, None),
        ),
        out_specs=P(None, "bx", "by", None),
        check_vma=False,
    )
```

```python
import functools

import jax
import jax.numpy as jnp
from jax import lax
from jax.experimental import pallas as pl
from jax.experimental.pallas import tpu as pltpu
from jax.sharding import PartitionSpec as P

ITERS = 2
AXES = ("bx", "by")
ROWS = 8


def interface(iterate, interface_tiles, source_cells, target_cells, tile_counts):
    var_count = iterate.shape[0]
    flat_cells = iterate.reshape(var_count, -1)
    block_count = lax.axis_size("bx") * lax.axis_size("by")
    slot_count = source_cells.shape[1]
    per_pair = slot_count // block_count
    picked = jnp.take(flat_cells, source_cells[0], axis=1)
    products = jnp.sum(interface_tiles[0] * picked[None], axis=1)
    slot_ids = jnp.arange(slot_count, dtype=jnp.int32)
    limits = jnp.repeat(tile_counts[0], per_pair)
    products = jnp.where((slot_ids % per_pair)[None] < limits[None], products, 0.0)
    arrived = lax.all_to_all(products, AXES, split_axis=1, concat_axis=1, tiled=True)
    summed = jnp.zeros_like(flat_cells).at[:, target_cells[0]].add(arrived)
    return summed.reshape(iterate.shape)


def to_slices(values, devices):
    count, ca, cb, nz = values.shape
    shaped = jnp.transpose(values, (3, 1, 2, 0))
    return shaped.reshape(devices, (nz // devices) * ca * cb, count)


def gather_grid(received, n_bx, n_by, ca, cb, width):
    count = received.shape[2]
    shaped = received.reshape(n_bx, n_by, width, ca, cb, count)
    shaped = jnp.transpose(shaped, (1, 4, 5, 2, 0, 3))
    return shaped.reshape(n_by * cb, count, width * n_bx * ca)


def scatter_grid(grid, n_bx, n_by, ca, cb, width):
    ny, count, lanes = grid.shape
    shaped = grid.reshape(n_by, cb, count, width, n_bx, ca)
    shaped = jnp.transpose(shaped, (4, 0, 3, 5, 1, 2))
    return shaped.reshape(n_bx * n_by, width * ca * cb, count)


def from_slices(received, ca, cb):
    src, rows, count = received.shape
    width = rows // (ca * cb)
    shaped = received.reshape(src * width, ca, cb, count)
    return jnp.transpose(shaped, (3, 1, 2, 0))


def lane_x(shape, nx):
    return lax.broadcasted_iota(jnp.int32, shape, len(shape) - 1) % nx


def skew(grid, steps, nx):
    ny = grid.shape[0]
    values = jnp.pad(grid, ((0, steps - ny), (0, 0), (0, 0)))
    x = lane_x(values.shape, nx)
    bit = 1
    while bit < nx:
        values = lax.optimization_barrier(values)
        moved = jnp.concatenate([jnp.zeros_like(values[:bit]), values[:-bit]], axis=0)
        values = jnp.where((x & bit) != 0, moved, values)
        bit *= 2
    return values


def skew_kernel(grid_ref, out_ref, *, nx):
    ny = grid_ref.shape[0]
    steps = out_ref.shape[0]
    out_ref[:ny] = grid_ref[...]
    out_ref[ny:] = jnp.zeros((steps - ny,) + out_ref.shape[1:], jnp.float32)
    x = lax.broadcasted_iota(jnp.int32, out_ref.shape[1:], 1) % nx
    bit = 1
    while bit < nx:
        moves = (x & bit) != 0

        def body(i, carry, bit=bit, moves=moves):
            t = steps - 1 - i
            out_ref[t] = jnp.where(moves, out_ref[t - bit], out_ref[t])
            return carry

        lax.fori_loop(0, steps - bit, body, 0)
        for t in range(bit):
            out_ref[t] = jnp.where(moves, 0.0, out_ref[t])
        bit *= 2


def skew_big(grid, steps, nx):
    ny, count, lanes = grid.shape
    return pl.pallas_call(
        functools.partial(skew_kernel, nx=nx),
        out_shape=jax.ShapeDtypeStruct((steps, count, lanes), jnp.float32),
    )(grid)


def unskew(values, ny, nx):
    x = lane_x(values.shape, nx)
    bit = 1
    while bit < nx:
        values = lax.optimization_barrier(values)
        moved = jnp.concatenate([values[bit:], jnp.zeros_like(values[:bit])], axis=0)
        values = jnp.where((x & bit) != 0, moved, values)
        bit *= 2
    return values[:ny]


def as_vectors(rows):
    return jnp.pad(rows, ((0, 0), (0, ROWS - rows.shape[1]), (0, 0)))


def as_matrices(rows, count):
    steps, _, lanes = rows.shape
    shaped = rows.reshape(steps, count, count, lanes)
    return jnp.pad(shaped, ((0, 0), (0, 0), (0, ROWS - count), (0, 0)))


def matvec(source, off, vector):
    count = vector.shape[1]
    return tree_sum([source[:, off + count * j : off + count * (j + 1), :] * vector[:, j : j + 1, :] for j in range(count)])


def shift_t(values, offset):
    zero = jnp.zeros_like(values[:1])
    if offset > 0:
        return jnp.concatenate([values[1:], zero], axis=0)
    return jnp.concatenate([zero, values[:-1]], axis=0)


def shift_x(values, offset, nx):
    x = lane_x(values.shape, nx)
    zero = jnp.zeros_like(values[..., :1])
    if offset > 0:
        moved = jnp.concatenate([values[..., 1:], zero], axis=-1)
        return jnp.where(x == nx - 1, 0.0, moved)
    moved = jnp.concatenate([zero, values[..., :-1]], axis=-1)
    return jnp.where(x == 0, 0.0, moved)


def shift_z(values, offset, nx, devices, count):
    rows = values.shape[1]
    if offset > 0:
        halo = lax.ppermute(values[:, :count, :nx], AXES, [(i + 1, i) for i in range(devices - 1)])
        halo = jnp.pad(halo, ((0, 0), (0, rows - count), (0, 0)))
        return jnp.concatenate([values[..., nx:], halo], axis=-1)
    halo = lax.ppermute(values[:, :count, -nx:], AXES, [(i, i + 1) for i in range(devices - 1)])
    halo = jnp.pad(halo, ((0, 0), (0, rows - count), (0, 0)))
    return jnp.concatenate([halo, values[..., :-nx]], axis=-1)


def tree_sum(terms):
    while len(terms) > 1:
        paired = [terms[i] + terms[i + 1] for i in range(0, len(terms) - 1, 2)]
        terms = paired + terms[len(paired) * 2 :]
    return terms[0]


def sweep_kernel(rhs_ref, *refs, forward, nx, count, places):
    out_ref = refs[-2]
    carry_ref = refs[-1]
    steps = rhs_ref.shape[0]
    lanes = rhs_ref.shape[2]
    x = lax.broadcasted_iota(jnp.int32, (count, lanes), 1) % nx
    if forward:
        keep = x > 0
        shift = 1
    else:
        keep = x < nx - 1
        shift = lanes - 1
    (kx_at, kx_off), (ky_at, ky_off), (inv_at, inv_off) = places

    @pl.when(pl.program_id(0) == 0)
    def _():
        carry_ref[...] = jnp.zeros((count, lanes), jnp.float32)

    def column(at, off, t, j):
        return refs[at][t, pl.ds(off + count * j, count), :]

    def step(s, fresh):
        t = s if forward else steps - 1 - s
        from_x = jnp.where(keep, pltpu.roll(fresh, shift, 1), 0.0)
        terms = [column(kx_at, kx_off, t, j) * from_x[j : j + 1, :] for j in range(count)]
        terms += [column(ky_at, ky_off, t, j) * fresh[j : j + 1, :] for j in range(count)]
        right = rhs_ref[t] - tree_sum(terms)
        result = tree_sum([column(inv_at, inv_off, t, j) * right[j : j + 1, :] for j in range(count)])
        out_ref[t] = result
        return result

    carry_ref[...] = lax.fori_loop(0, steps, step, carry_ref[...], unroll=8)


def sweep(rhs, sources, places, forward, nx, chunks=4):
    steps, count, lanes = rhs.shape
    size = steps // chunks
    if forward:
        where = lambda i: (i, 0, 0)
    else:
        where = lambda i: (chunks - 1 - i, 0, 0)
    kernel = functools.partial(sweep_kernel, forward=forward, nx=nx, count=count, places=places)
    specs = [pl.BlockSpec((size, count, lanes), where)]
    for source in sources:
        needed = max(off + count * count for at, off in places if sources[at] is source)
        rows = min(source.shape[1], -(-needed // ROWS) * ROWS)
        specs.append(pl.BlockSpec((size, rows, source.shape[2]), where))
    return pl.pallas_call(
        kernel,
        grid=(chunks,),
        in_specs=specs,
        out_specs=pl.BlockSpec((size, count, lanes), where),
        out_shape=jax.ShapeDtypeStruct(rhs.shape, jnp.float32),
        scratch_shapes=[pltpu.VMEM((count, lanes), jnp.float32)],
    )(rhs, *sources)


def per_device(
    adjoint_source,
    initial,
    inverses,
    couplings,
    interface_tiles,
    source_cells,
    target_cells,
    tile_counts,
):
    n_bx = lax.axis_size("bx")
    n_by = lax.axis_size("by")
    devices = n_bx * n_by
    count, ca, cb, nz = adjoint_source.shape
    nx, ny = n_bx * ca, n_by * cb
    width = nz // devices
    steps = nx + ny
    tables = (interface_tiles, source_cells, target_cells, tile_counts)

    def to_z(values, skewer=skew):
        received = lax.all_to_all(to_slices(values, devices), AXES, 0, 0, tiled=True)
        return skewer(gather_grid(received, n_bx, n_by, ca, cb, width), steps, nx)

    def to_xy(skewed):
        rows = ROWS
        grid = unskew(jnp.pad(skewed, ((0, 0), (0, rows - skewed.shape[1]), (0, 0))), ny, nx)
        lanes = grid.shape[2]
        chunks = grid.reshape(ny * rows, lanes).T
        chunks = chunks.reshape(width, n_bx, ca, n_by, cb * rows)
        chunks = jnp.transpose(chunks, (1, 3, 0, 2, 4)).reshape(devices, width * ca * cb * rows)
        received = lax.all_to_all(chunks, AXES, 0, 0, tiled=True)
        flat = received.reshape(devices * width, ca * cb * rows).T
        flat = flat.reshape(ca, cb, rows, nz)
        return jnp.transpose(flat, (2, 0, 1, 3))[:count]

    def small_to_z(values):
        padded = jnp.pad(values, ((0, ROWS - count), (0, 0), (0, 0), (0, 0)))
        flat = jnp.transpose(padded, (1, 2, 0, 3)).reshape(ca * cb * ROWS, nz)
        chunks = flat.T.reshape(devices, width * ca * cb * ROWS)
        received = lax.all_to_all(chunks, AXES, 0, 0, tiled=True)
        shaped = received.reshape(n_bx, n_by, width, ca, cb * ROWS)
        shaped = jnp.transpose(shaped, (2, 0, 3, 1, 4)).reshape(width * nx, ny * ROWS)
        return skew(shaped.T.reshape(ny, ROWS, width * nx), steps, nx)

    span = count * count
    sweep_rows = to_z(
        jnp.concatenate(
            [
                jnp.swapaxes(inverses, 0, 1).reshape(span, ca, cb, nz),
                jnp.swapaxes(couplings[0::2][:2], 1, 2).astype(jnp.float32).reshape(2 * span, ca, cb, nz),
            ],
            axis=0,
        ),
        skew_big,
    )
    base = adjoint_source - interface(initial, *tables)
    below = jnp.concatenate([jnp.zeros_like(initial[..., :1]), initial[..., :-1]], axis=-1)
    above = jnp.concatenate([initial[..., 1:], jnp.zeros_like(initial[..., :1])], axis=-1)
    along_z = couplings[4].astype(jnp.float32) * below[None] + couplings[5].astype(jnp.float32) * above[None]
    lower_base = base - jnp.sum(along_z, axis=1)
    other_rows = to_z(
        jnp.concatenate(
            [
                jnp.swapaxes(couplings[jnp.array([1, 3, 4, 5])], 1, 2).astype(jnp.float32).reshape(4 * span, ca, cb, nz),
                base,
                lower_base,
                initial,
            ],
            axis=0,
        ),
        skew_big,
    )
    base_z = other_rows[:, 4 * span : 4 * span + count]
    lower_z = other_rows[:, 4 * span + count : 4 * span + 2 * count]
    iterate = other_rows[:, 4 * span + 2 * count : 4 * span + 3 * count]
    forward_places = ((0, span), (0, 2 * span), (0, 0))
    backward_places = ((0, 0), (0, span), (1, 0))

    for number in range(ITERS):
        if number > 0:
            inter = interface(to_xy(iterate), *tables)
            base_z = small_to_z(adjoint_source - inter)[:, :count]
        in_plane = lax.optimization_barrier(
            matvec(other_rows, 0, shift_x(shift_t(iterate, 1), 1, nx))
            + matvec(other_rows, span, shift_t(iterate, 1))
        )
        if number > 0:
            lower_z = base_z - (
                matvec(other_rows, 2 * span, shift_z(iterate, -1, nx, devices, count))
                + matvec(other_rows, 3 * span, shift_z(iterate, 1, nx, devices, count))
            )
        lower_terms = lower_z - in_plane
        half = sweep(lower_terms, (sweep_rows,), forward_places, True, nx)
        in_plane = lax.optimization_barrier(
            matvec(sweep_rows, span, shift_x(shift_t(half, -1), -1, nx))
            + matvec(sweep_rows, 2 * span, shift_t(half, -1))
        )
        upper_terms = (base_z - in_plane) - (
            matvec(other_rows, 2 * span, shift_z(half, -1, nx, devices, count))
            + matvec(other_rows, 3 * span, shift_z(half, 1, nx, devices, count))
        )
        iterate = sweep(upper_terms, (other_rows, sweep_rows), backward_places, False, nx)
    return to_xy(iterate)


def solution(mesh):
    return jax.shard_map(
        per_device,
        mesh=mesh,
        in_specs=(
            P(None, "bx", "by", None),
            P(None, "bx", "by", None),
            P(None, None, "bx", "by", None),
            P(None, None, None, "bx", "by", None),
            P(AXES, None, None, None),
            P(AXES, None),
            P(AXES, None),
            P(AXES, None),
        ),
        out_specs=P(None, "bx", "by", None),
        check_vma=False,
    )
```

```python
import functools

import jax
import jax.numpy as jnp
from jax import lax
from jax.experimental import pallas as pl
from jax.experimental.pallas import tpu as pltpu
from jax.sharding import PartitionSpec as P

ITERS = 2
AXES = ("bx", "by")
ROWS = 8


def interface(iterate, interface_tiles, source_cells, target_cells, tile_counts):
    var_count = iterate.shape[0]
    flat_cells = iterate.reshape(var_count, -1)
    block_count = lax.axis_size("bx") * lax.axis_size("by")
    slot_count = source_cells.shape[1]
    per_pair = slot_count // block_count
    picked = jnp.take(flat_cells, source_cells[0], axis=1)
    products = jnp.sum(interface_tiles[0] * picked[None], axis=1)
    slot_ids = jnp.arange(slot_count, dtype=jnp.int32)
    limits = jnp.repeat(tile_counts[0], per_pair)
    products = jnp.where((slot_ids % per_pair)[None] < limits[None], products, 0.0)
    arrived = lax.all_to_all(products, AXES, split_axis=1, concat_axis=1, tiled=True)
    summed = jnp.zeros_like(flat_cells).at[:, target_cells[0]].add(arrived)
    return summed.reshape(iterate.shape)


def to_slices(values, devices):
    count, ca, cb, nz = values.shape
    shaped = jnp.transpose(values, (3, 1, 2, 0))
    return shaped.reshape(devices, (nz // devices) * ca * cb, count)


def gather_grid(received, n_bx, n_by, ca, cb, width):
    count = received.shape[2]
    shaped = received.reshape(n_bx, n_by, width, ca, cb, count)
    shaped = jnp.transpose(shaped, (1, 4, 5, 2, 0, 3))
    return shaped.reshape(n_by * cb, count, width * n_bx * ca)


def scatter_grid(grid, n_bx, n_by, ca, cb, width):
    ny, count, lanes = grid.shape
    shaped = grid.reshape(n_by, cb, count, width, n_bx, ca)
    shaped = jnp.transpose(shaped, (4, 0, 3, 5, 1, 2))
    return shaped.reshape(n_bx * n_by, width * ca * cb, count)


def from_slices(received, ca, cb):
    src, rows, count = received.shape
    width = rows // (ca * cb)
    shaped = received.reshape(src * width, ca, cb, count)
    return jnp.transpose(shaped, (3, 1, 2, 0))


def lane_x(shape, nx):
    return lax.broadcasted_iota(jnp.int32, shape, len(shape) - 1) % nx


def skew(grid, steps, nx):
    ny = grid.shape[0]
    values = jnp.pad(grid, ((0, steps - ny), (0, 0), (0, 0)))
    x = lane_x(values.shape, nx)
    bit = 1
    while bit < nx:
        values = lax.optimization_barrier(values)
        moved = jnp.concatenate([jnp.zeros_like(values[:bit]), values[:-bit]], axis=0)
        values = jnp.where((x & bit) != 0, moved, values)
        bit *= 2
    return values


def skew_kernel(grid_ref, out_ref, *, nx):
    ny = grid_ref.shape[0]
    steps = out_ref.shape[0]
    out_ref[:ny] = grid_ref[...]
    out_ref[ny:] = jnp.zeros((steps - ny,) + out_ref.shape[1:], jnp.float32)
    x = lax.broadcasted_iota(jnp.int32, out_ref.shape[1:], 1) % nx
    unit = 1
    while unit < nx:
        ways = 4 if unit * 4 <= nx else 2
        part = (x // unit) % ways
        masks = [part == k for k in range(1, ways)]

        def pick(t, masks=masks, unit=unit, ways=ways):
            value = out_ref[t]
            for k in range(1, ways):
                if isinstance(t, int) and t < k * unit:
                    moved = jnp.zeros_like(value)
                else:
                    moved = out_ref[t - k * unit]
                value = jnp.where(masks[k - 1], moved, value)
            return value

        def body(i, carry, pick=pick):
            t = steps - 1 - i
            out_ref[t] = pick(t)
            return carry

        reach = (ways - 1) * unit
        lax.fori_loop(0, steps - reach, body, 0)
        for t in reversed(range(reach)):
            out_ref[t] = pick(t)
        unit *= ways


def skew_big(grid, steps, nx):
    ny, count, lanes = grid.shape
    return pl.pallas_call(
        functools.partial(skew_kernel, nx=nx),
        out_shape=jax.ShapeDtypeStruct((steps, count, lanes), jnp.float32),
    )(grid)


def unskew(values, ny, nx):
    x = lane_x(values.shape, nx)
    bit = 1
    while bit < nx:
        values = lax.optimization_barrier(values)
        moved = jnp.concatenate([values[bit:], jnp.zeros_like(values[:bit])], axis=0)
        values = jnp.where((x & bit) != 0, moved, values)
        bit *= 2
    return values[:ny]


def as_vectors(rows):
    return jnp.pad(rows, ((0, 0), (0, ROWS - rows.shape[1]), (0, 0)))


def as_matrices(rows, count):
    steps, _, lanes = rows.shape
    shaped = rows.reshape(steps, count, count, lanes)
    return jnp.pad(shaped, ((0, 0), (0, 0), (0, ROWS - count), (0, 0)))


def matvec(source, off, vector):
    count = vector.shape[1]
    return tree_sum([source[:, off + count * j : off + count * (j + 1), :] * vector[:, j : j + 1, :] for j in range(count)])


def shift_t(values, offset):
    zero = jnp.zeros_like(values[:1])
    if offset > 0:
        return jnp.concatenate([values[1:], zero], axis=0)
    return jnp.concatenate([zero, values[:-1]], axis=0)


def shift_x(values, offset, nx):
    x = lane_x(values.shape, nx)
    zero = jnp.zeros_like(values[..., :1])
    if offset > 0:
        moved = jnp.concatenate([values[..., 1:], zero], axis=-1)
        return jnp.where(x == nx - 1, 0.0, moved)
    moved = jnp.concatenate([zero, values[..., :-1]], axis=-1)
    return jnp.where(x == 0, 0.0, moved)


def shift_z(values, offset, nx, devices, count):
    rows = values.shape[1]
    if offset > 0:
        halo = lax.ppermute(values[:, :count, :nx], AXES, [(i + 1, i) for i in range(devices - 1)])
        halo = jnp.pad(halo, ((0, 0), (0, rows - count), (0, 0)))
        return jnp.concatenate([values[..., nx:], halo], axis=-1)
    halo = lax.ppermute(values[:, :count, -nx:], AXES, [(i, i + 1) for i in range(devices - 1)])
    halo = jnp.pad(halo, ((0, 0), (0, rows - count), (0, 0)))
    return jnp.concatenate([halo, values[..., :-nx]], axis=-1)


def tree_sum(terms):
    while len(terms) > 1:
        paired = [terms[i] + terms[i + 1] for i in range(0, len(terms) - 1, 2)]
        terms = paired + terms[len(paired) * 2 :]
    return terms[0]


def sweep_kernel(rhs_ref, *refs, forward, nx, count, places):
    out_ref = refs[-2]
    carry_ref = refs[-1]
    steps = rhs_ref.shape[0]
    lanes = rhs_ref.shape[2]
    x = lax.broadcasted_iota(jnp.int32, (count, lanes), 1) % nx
    if forward:
        keep = x > 0
        shift = 1
    else:
        keep = x < nx - 1
        shift = lanes - 1
    (kx_at, kx_off), (ky_at, ky_off), (inv_at, inv_off) = places

    @pl.when(pl.program_id(0) == 0)
    def _():
        carry_ref[...] = jnp.zeros((count, lanes), jnp.float32)

    def column(at, off, t, j):
        return refs[at][t, pl.ds(off + count * j, count), :]

    def step(s, fresh):
        t = s if forward else steps - 1 - s
        from_x = jnp.where(keep, pltpu.roll(fresh, shift, 1), 0.0)
        terms = [column(kx_at, kx_off, t, j) * from_x[j : j + 1, :] for j in range(count)]
        terms += [column(ky_at, ky_off, t, j) * fresh[j : j + 1, :] for j in range(count)]
        right = rhs_ref[t] - tree_sum(terms)
        result = tree_sum([column(inv_at, inv_off, t, j) * right[j : j + 1, :] for j in range(count)])
        out_ref[t] = result
        return result

    carry_ref[...] = lax.fori_loop(0, steps, step, carry_ref[...], unroll=2)


def sweep(rhs, sources, places, forward, nx, chunks=4):
    steps, count, lanes = rhs.shape
    size = steps // chunks
    if forward:
        where = lambda i: (i, 0, 0)
    else:
        where = lambda i: (chunks - 1 - i, 0, 0)
    kernel = functools.partial(sweep_kernel, forward=forward, nx=nx, count=count, places=places)
    specs = [pl.BlockSpec((size, count, lanes), where)]
    for source in sources:
        needed = max(off + count * count for at, off in places if sources[at] is source)
        rows = min(source.shape[1], -(-needed // ROWS) * ROWS)
        specs.append(pl.BlockSpec((size, rows, source.shape[2]), where))
    return pl.pallas_call(
        kernel,
        grid=(chunks,),
        in_specs=specs,
        out_specs=pl.BlockSpec((size, count, lanes), where),
        out_shape=jax.ShapeDtypeStruct(rhs.shape, jnp.float32),
        scratch_shapes=[pltpu.VMEM((count, lanes), jnp.float32)],
    )(rhs, *sources)


def per_device(
    adjoint_source,
    initial,
    inverses,
    couplings,
    interface_tiles,
    source_cells,
    target_cells,
    tile_counts,
):
    n_bx = lax.axis_size("bx")
    n_by = lax.axis_size("by")
    devices = n_bx * n_by
    count, ca, cb, nz = adjoint_source.shape
    nx, ny = n_bx * ca, n_by * cb
    width = nz // devices
    steps = nx + ny
    tables = (interface_tiles, source_cells, target_cells, tile_counts)

    def to_z(values, skewer=skew):
        received = lax.all_to_all(to_slices(values, devices), AXES, 0, 0, tiled=True)
        return skewer(gather_grid(received, n_bx, n_by, ca, cb, width), steps, nx)

    def to_xy(skewed):
        rows = ROWS
        grid = unskew(jnp.pad(skewed, ((0, 0), (0, rows - skewed.shape[1]), (0, 0))), ny, nx)
        lanes = grid.shape[2]
        chunks = grid.reshape(ny * rows, lanes).T
        chunks = chunks.reshape(width, n_bx, ca, n_by, cb * rows)
        chunks = jnp.transpose(chunks, (1, 3, 0, 2, 4)).reshape(devices, width * ca * cb * rows)
        received = lax.all_to_all(chunks, AXES, 0, 0, tiled=True)
        flat = received.reshape(devices * width, ca * cb * rows).T
        flat = flat.reshape(ca, cb, rows, nz)
        return jnp.transpose(flat, (2, 0, 1, 3))[:count]

    def small_to_z(values):
        padded = jnp.pad(values, ((0, ROWS - count), (0, 0), (0, 0), (0, 0)))
        flat = jnp.transpose(padded, (1, 2, 0, 3)).reshape(ca * cb * ROWS, nz)
        chunks = flat.T.reshape(devices, width * ca * cb * ROWS)
        received = lax.all_to_all(chunks, AXES, 0, 0, tiled=True)
        shaped = received.reshape(n_bx, n_by, width, ca, cb * ROWS)
        shaped = jnp.transpose(shaped, (2, 0, 3, 1, 4)).reshape(width * nx, ny * ROWS)
        return skew(shaped.T.reshape(ny, ROWS, width * nx), steps, nx)

    span = count * count
    sweep_rows = to_z(
        jnp.concatenate(
            [
                jnp.swapaxes(inverses, 0, 1).reshape(span, ca, cb, nz),
                jnp.swapaxes(couplings[0::2][:2], 1, 2).astype(jnp.float32).reshape(2 * span, ca, cb, nz),
            ],
            axis=0,
        ),
        skew_big,
    )
    base = adjoint_source - interface(initial, *tables)
    below = jnp.concatenate([jnp.zeros_like(initial[..., :1]), initial[..., :-1]], axis=-1)
    above = jnp.concatenate([initial[..., 1:], jnp.zeros_like(initial[..., :1])], axis=-1)
    along_z = couplings[4].astype(jnp.float32) * below[None] + couplings[5].astype(jnp.float32) * above[None]
    lower_base = base - jnp.sum(along_z, axis=1)
    other_rows = to_z(
        jnp.concatenate(
            [
                jnp.swapaxes(couplings[jnp.array([1, 3, 4, 5])], 1, 2).astype(jnp.float32).reshape(4 * span, ca, cb, nz),
                base,
                lower_base,
                initial,
            ],
            axis=0,
        ),
        skew_big,
    )
    base_z = other_rows[:, 4 * span : 4 * span + count]
    lower_z = other_rows[:, 4 * span + count : 4 * span + 2 * count]
    iterate = other_rows[:, 4 * span + 2 * count : 4 * span + 3 * count]
    forward_places = ((0, span), (0, 2 * span), (0, 0))
    backward_places = ((0, 0), (0, span), (1, 0))

    for number in range(ITERS):
        if number > 0:
            inter = interface(to_xy(iterate), *tables)
            base_z = small_to_z(adjoint_source - inter)[:, :count]
        in_plane = lax.optimization_barrier(
            matvec(other_rows, 0, shift_x(shift_t(iterate, 1), 1, nx))
            + matvec(other_rows, span, shift_t(iterate, 1))
        )
        if number > 0:
            lower_z = base_z - (
                matvec(other_rows, 2 * span, shift_z(iterate, -1, nx, devices, count))
                + matvec(other_rows, 3 * span, shift_z(iterate, 1, nx, devices, count))
            )
        lower_terms = lower_z - in_plane
        half = sweep(lower_terms, (sweep_rows,), forward_places, True, nx)
        in_plane = lax.optimization_barrier(
            matvec(sweep_rows, span, shift_x(shift_t(half, -1), -1, nx))
            + matvec(sweep_rows, 2 * span, shift_t(half, -1))
        )
        upper_terms = (base_z - in_plane) - (
            matvec(other_rows, 2 * span, shift_z(half, -1, nx, devices, count))
            + matvec(other_rows, 3 * span, shift_z(half, 1, nx, devices, count))
        )
        iterate = sweep(upper_terms, (other_rows, sweep_rows), backward_places, False, nx)
    return to_xy(iterate)


def solution(mesh):
    return jax.shard_map(
        per_device,
        mesh=mesh,
        in_specs=(
            P(None, "bx", "by", None),
            P(None, "bx", "by", None),
            P(None, None, "bx", "by", None),
            P(None, None, None, "bx", "by", None),
            P(AXES, None, None, None),
            P(AXES, None),
            P(AXES, None),
            P(AXES, None),
        ),
        out_specs=P(None, "bx", "by", None),
        check_vma=False,
    )
```

```python
import functools

import jax
import jax.numpy as jnp
from jax import lax
from jax.experimental import pallas as pl
from jax.experimental.pallas import tpu as pltpu
from jax.sharding import PartitionSpec as P

ITERS = 2
AXES = ("bx", "by")
ROWS = 8


def interface(iterate, interface_tiles, source_cells, target_cells, tile_counts):
    var_count = iterate.shape[0]
    flat_cells = iterate.reshape(var_count, -1)
    block_count = lax.axis_size("bx") * lax.axis_size("by")
    slot_count = source_cells.shape[1]
    per_pair = slot_count // block_count
    picked = jnp.take(flat_cells, source_cells[0], axis=1)
    products = jnp.sum(interface_tiles[0] * picked[None], axis=1)
    slot_ids = jnp.arange(slot_count, dtype=jnp.int32)
    limits = jnp.repeat(tile_counts[0], per_pair)
    products = jnp.where((slot_ids % per_pair)[None] < limits[None], products, 0.0)
    arrived = lax.all_to_all(products, AXES, split_axis=1, concat_axis=1, tiled=True)
    summed = jnp.zeros_like(flat_cells).at[:, target_cells[0]].add(arrived)
    return summed.reshape(iterate.shape)


def to_slices(values, devices):
    count, ca, cb, nz = values.shape
    shaped = jnp.transpose(values, (3, 1, 2, 0))
    return shaped.reshape(devices, (nz // devices) * ca * cb, count)


def gather_grid(received, n_bx, n_by, ca, cb, width):
    count = received.shape[2]
    shaped = received.reshape(n_bx, n_by, width, ca, cb, count)
    shaped = jnp.transpose(shaped, (1, 4, 5, 2, 0, 3))
    return shaped.reshape(n_by * cb, count, width * n_bx * ca)


def scatter_grid(grid, n_bx, n_by, ca, cb, width):
    ny, count, lanes = grid.shape
    shaped = grid.reshape(n_by, cb, count, width, n_bx, ca)
    shaped = jnp.transpose(shaped, (4, 0, 3, 5, 1, 2))
    return shaped.reshape(n_bx * n_by, width * ca * cb, count)


def from_slices(received, ca, cb):
    src, rows, count = received.shape
    width = rows // (ca * cb)
    shaped = received.reshape(src * width, ca, cb, count)
    return jnp.transpose(shaped, (3, 1, 2, 0))


def lane_x(shape, nx):
    return lax.broadcasted_iota(jnp.int32, shape, len(shape) - 1) % nx


def skew(grid, steps, nx):
    ny = grid.shape[0]
    values = jnp.pad(grid, ((0, steps - ny), (0, 0), (0, 0)))
    x = lane_x(values.shape, nx)
    bit = 1
    while bit < nx:
        values = lax.optimization_barrier(values)
        moved = jnp.concatenate([jnp.zeros_like(values[:bit]), values[:-bit]], axis=0)
        values = jnp.where((x & bit) != 0, moved, values)
        bit *= 2
    return values


def skew_kernel(grid_ref, out_ref, *, nx):
    ny = grid_ref.shape[0]
    steps = out_ref.shape[0]
    out_ref[:ny] = grid_ref[...]
    out_ref[ny:] = jnp.zeros((steps - ny,) + out_ref.shape[1:], jnp.float32)
    x = lax.broadcasted_iota(jnp.int32, out_ref.shape[1:], 1) % nx
    unit = 1
    while unit < nx:
        ways = 4 if unit * 4 <= nx else 2
        part = (x // unit) % ways
        masks = [part == k for k in range(1, ways)]

        def pick(t, masks=masks, unit=unit, ways=ways):
            value = out_ref[t]
            for k in range(1, ways):
                if isinstance(t, int) and t < k * unit:
                    moved = jnp.zeros_like(value)
                else:
                    moved = out_ref[t - k * unit]
                value = jnp.where(masks[k - 1], moved, value)
            return value

        def body(i, carry, pick=pick):
            t = steps - 1 - i
            out_ref[t] = pick(t)
            return carry

        reach = (ways - 1) * unit
        lax.fori_loop(0, steps - reach, body, 0)
        for t in reversed(range(reach)):
            out_ref[t] = pick(t)
        unit *= ways


def skew_big(grid, steps, nx):
    ny, count, lanes = grid.shape
    return pl.pallas_call(
        functools.partial(skew_kernel, nx=nx),
        out_shape=jax.ShapeDtypeStruct((steps, count, lanes), jnp.float32),
    )(grid)


def unskew(values, ny, nx):
    x = lane_x(values.shape, nx)
    bit = 1
    while bit < nx:
        values = lax.optimization_barrier(values)
        moved = jnp.concatenate([values[bit:], jnp.zeros_like(values[:bit])], axis=0)
        values = jnp.where((x & bit) != 0, moved, values)
        bit *= 2
    return values[:ny]


def as_vectors(rows):
    return jnp.pad(rows, ((0, 0), (0, ROWS - rows.shape[1]), (0, 0)))


def as_matrices(rows, count):
    steps, _, lanes = rows.shape
    shaped = rows.reshape(steps, count, count, lanes)
    return jnp.pad(shaped, ((0, 0), (0, 0), (0, ROWS - count), (0, 0)))


def matvec(source, off, vector):
    count = vector.shape[1]
    return tree_sum([source[:, off + count * j : off + count * (j + 1), :] * vector[:, j : j + 1, :] for j in range(count)])


def shift_t(values, offset):
    zero = jnp.zeros_like(values[:1])
    if offset > 0:
        return jnp.concatenate([values[1:], zero], axis=0)
    return jnp.concatenate([zero, values[:-1]], axis=0)


def shift_x(values, offset, nx):
    x = lane_x(values.shape, nx)
    zero = jnp.zeros_like(values[..., :1])
    if offset > 0:
        moved = jnp.concatenate([values[..., 1:], zero], axis=-1)
        return jnp.where(x == nx - 1, 0.0, moved)
    moved = jnp.concatenate([zero, values[..., :-1]], axis=-1)
    return jnp.where(x == 0, 0.0, moved)


def shift_z(values, offset, nx, devices, count):
    rows = values.shape[1]
    if offset > 0:
        halo = lax.ppermute(values[:, :count, :nx], AXES, [(i + 1, i) for i in range(devices - 1)])
        halo = jnp.pad(halo, ((0, 0), (0, rows - count), (0, 0)))
        return jnp.concatenate([values[..., nx:], halo], axis=-1)
    halo = lax.ppermute(values[:, :count, -nx:], AXES, [(i, i + 1) for i in range(devices - 1)])
    halo = jnp.pad(halo, ((0, 0), (0, rows - count), (0, 0)))
    return jnp.concatenate([halo, values[..., :-nx]], axis=-1)


def tree_sum(terms):
    while len(terms) > 1:
        paired = [terms[i] + terms[i + 1] for i in range(0, len(terms) - 1, 2)]
        terms = paired + terms[len(paired) * 2 :]
    return terms[0]


def sweep_kernel(rhs_ref, *refs, forward, nx, count, places):
    out_ref = refs[-2]
    carry_ref = refs[-1]
    steps = rhs_ref.shape[0]
    lanes = rhs_ref.shape[2]
    x = lax.broadcasted_iota(jnp.int32, (count, lanes), 1) % nx
    if forward:
        keep = x > 0
        shift = 1
    else:
        keep = x < nx - 1
        shift = lanes - 1
    (kx_at, kx_off), (ky_at, ky_off), (inv_at, inv_off) = places

    @pl.when(pl.program_id(0) == 0)
    def _():
        carry_ref[...] = jnp.zeros((count, lanes), jnp.float32)

    def column(at, off, t, j):
        return refs[at][t, pl.ds(off + count * j, count), :]

    def step(s, fresh):
        t = s if forward else steps - 1 - s
        from_x = jnp.where(keep, pltpu.roll(fresh, shift, 1), 0.0)
        terms = [column(kx_at, kx_off, t, j) * from_x[j : j + 1, :] for j in range(count)]
        terms += [column(ky_at, ky_off, t, j) * fresh[j : j + 1, :] for j in range(count)]
        right = rhs_ref[t] - tree_sum(terms)
        result = tree_sum([column(inv_at, inv_off, t, j) * right[j : j + 1, :] for j in range(count)])
        out_ref[t] = result
        return result

    carry_ref[...] = lax.fori_loop(0, steps, step, carry_ref[...], unroll=2)


def sweep(rhs, sources, places, forward, nx, chunks=4):
    steps, count, lanes = rhs.shape
    size = steps // chunks
    if forward:
        where = lambda i: (i, 0, 0)
    else:
        where = lambda i: (chunks - 1 - i, 0, 0)
    kernel = functools.partial(sweep_kernel, forward=forward, nx=nx, count=count, places=places)
    specs = [pl.BlockSpec((size, count, lanes), where)]
    for source in sources:
        needed = max(off + count * count for at, off in places if sources[at] is source)
        rows = min(source.shape[1], -(-needed // ROWS) * ROWS)
        specs.append(pl.BlockSpec((size, rows, source.shape[2]), where))
    return pl.pallas_call(
        kernel,
        grid=(chunks,),
        in_specs=specs,
        out_specs=pl.BlockSpec((size, count, lanes), where),
        out_shape=jax.ShapeDtypeStruct(rhs.shape, jnp.float32),
        scratch_shapes=[pltpu.VMEM((count, lanes), jnp.float32)],
    )(rhs, *sources)


def per_device(
    adjoint_source,
    initial,
    inverses,
    couplings,
    interface_tiles,
    source_cells,
    target_cells,
    tile_counts,
):
    n_bx = lax.axis_size("bx")
    n_by = lax.axis_size("by")
    devices = n_bx * n_by
    count, ca, cb, nz = adjoint_source.shape
    nx, ny = n_bx * ca, n_by * cb
    width = nz // devices
    steps = nx + ny
    tables = (interface_tiles, source_cells, target_cells, tile_counts)

    def to_z(values, skewer=skew):
        received = lax.all_to_all(to_slices(values, devices), AXES, 0, 0, tiled=True)
        return skewer(gather_grid(received, n_bx, n_by, ca, cb, width), steps, nx)

    def to_xy(skewed):
        rows = ROWS
        grid = unskew(jnp.pad(skewed, ((0, 0), (0, rows - skewed.shape[1]), (0, 0))), ny, nx)
        lanes = grid.shape[2]
        chunks = grid.reshape(ny * rows, lanes).T
        chunks = chunks.reshape(width, n_bx, ca, n_by, cb * rows)
        chunks = jnp.transpose(chunks, (1, 3, 0, 2, 4)).reshape(devices, width * ca * cb * rows)
        received = lax.all_to_all(chunks, AXES, 0, 0, tiled=True)
        flat = received.reshape(devices * width, ca * cb * rows).T
        flat = flat.reshape(ca, cb, rows, nz)
        return jnp.transpose(flat, (2, 0, 1, 3))[:count]

    def small_to_z(values):
        padded = jnp.pad(values, ((0, ROWS - count), (0, 0), (0, 0), (0, 0)))
        flat = jnp.transpose(padded, (1, 2, 0, 3)).reshape(ca * cb * ROWS, nz)
        chunks = flat.T.reshape(devices, width * ca * cb * ROWS)
        received = lax.all_to_all(chunks, AXES, 0, 0, tiled=True)
        shaped = received.reshape(n_bx, n_by, width, ca, cb * ROWS)
        shaped = jnp.transpose(shaped, (2, 0, 3, 1, 4)).reshape(width * nx, ny * ROWS)
        return skew(shaped.T.reshape(ny, ROWS, width * nx), steps, nx)

    span = count * count
    sweep_rows = to_z(
        jnp.concatenate(
            [
                jnp.swapaxes(inverses, 0, 1).reshape(span, ca, cb, nz),
                jnp.swapaxes(couplings[jnp.array([0, 2, 4, 5])], 1, 2).astype(jnp.float32).reshape(4 * span, ca, cb, nz),
            ],
            axis=0,
        ),
        skew_big,
    )
    base = adjoint_source - interface(initial, *tables)
    below = jnp.concatenate([jnp.zeros_like(initial[..., :1]), initial[..., :-1]], axis=-1)
    above = jnp.concatenate([initial[..., 1:], jnp.zeros_like(initial[..., :1])], axis=-1)
    along_z = couplings[4].astype(jnp.float32) * below[None] + couplings[5].astype(jnp.float32) * above[None]
    lower_base = base - jnp.sum(along_z, axis=1)
    other_rows = to_z(
        jnp.concatenate(
            [
                jnp.swapaxes(couplings[jnp.array([1, 3])], 1, 2).astype(jnp.float32).reshape(2 * span, ca, cb, nz),
                base,
                lower_base,
                initial,
            ],
            axis=0,
        ),
        skew_big,
    )
    base_z = other_rows[:, 2 * span : 2 * span + count]
    lower_z = other_rows[:, 2 * span + count : 2 * span + 2 * count]
    iterate = other_rows[:, 2 * span + 2 * count : 2 * span + 3 * count]
    forward_places = ((0, span), (0, 2 * span), (0, 0))
    backward_places = ((0, 0), (0, span), (1, 0))

    for number in range(ITERS):
        if number > 0:
            inter = interface(to_xy(iterate), *tables)
            base_z = small_to_z(adjoint_source - inter)[:, :count]
        in_plane = lax.optimization_barrier(
            matvec(other_rows, 0, shift_x(shift_t(iterate, 1), 1, nx))
            + matvec(other_rows, span, shift_t(iterate, 1))
        )
        if number > 0:
            lower_z = base_z - (
                matvec(sweep_rows, 3 * span, shift_z(iterate, -1, nx, devices, count))
                + matvec(sweep_rows, 4 * span, shift_z(iterate, 1, nx, devices, count))
            )
        lower_terms = lower_z - in_plane
        half = sweep(lower_terms, (sweep_rows,), forward_places, True, nx)
        in_plane = lax.optimization_barrier(
            matvec(sweep_rows, span, shift_x(shift_t(half, -1), -1, nx))
            + matvec(sweep_rows, 2 * span, shift_t(half, -1))
        )
        upper_terms = (base_z - in_plane) - (
            matvec(sweep_rows, 3 * span, shift_z(half, -1, nx, devices, count))
            + matvec(sweep_rows, 4 * span, shift_z(half, 1, nx, devices, count))
        )
        iterate = sweep(upper_terms, (other_rows, sweep_rows), backward_places, False, nx)
    return to_xy(iterate)


def solution(mesh):
    return jax.shard_map(
        per_device,
        mesh=mesh,
        in_specs=(
            P(None, "bx", "by", None),
            P(None, "bx", "by", None),
            P(None, None, "bx", "by", None),
            P(None, None, None, "bx", "by", None),
            P(AXES, None, None, None),
            P(AXES, None),
            P(AXES, None),
            P(AXES, None),
        ),
        out_specs=P(None, "bx", "by", None),
        check_vma=False,
    )
```

```python
import functools

import jax
import jax.numpy as jnp
from jax import lax
from jax.experimental import pallas as pl
from jax.experimental.pallas import tpu as pltpu
from jax.sharding import PartitionSpec as P

ITERS = 2
AXES = ("bx", "by")
ROWS = 8


def interface(iterate, interface_tiles, source_cells, target_cells, tile_counts):
    var_count = iterate.shape[0]
    flat_cells = iterate.reshape(var_count, -1)
    block_count = lax.axis_size("bx") * lax.axis_size("by")
    slot_count = source_cells.shape[1]
    per_pair = slot_count // block_count
    picked = jnp.take(flat_cells, source_cells[0], axis=1)
    products = jnp.sum(interface_tiles[0] * picked[None], axis=1)
    slot_ids = jnp.arange(slot_count, dtype=jnp.int32)
    limits = jnp.repeat(tile_counts[0], per_pair)
    products = jnp.where((slot_ids % per_pair)[None] < limits[None], products, 0.0)
    arrived = lax.all_to_all(products, AXES, split_axis=1, concat_axis=1, tiled=True)
    summed = jnp.zeros_like(flat_cells).at[:, target_cells[0]].add(arrived)
    return summed.reshape(iterate.shape)


def to_slices(values, devices):
    count, ca, cb, nz = values.shape
    shaped = jnp.transpose(values, (3, 1, 2, 0))
    return shaped.reshape(devices, (nz // devices) * ca * cb, count)


def gather_grid(received, n_bx, n_by, ca, cb, width):
    count = received.shape[2]
    shaped = received.reshape(n_bx, n_by, width, ca, cb, count)
    shaped = jnp.transpose(shaped, (1, 4, 5, 2, 0, 3))
    return shaped.reshape(n_by * cb, count, width * n_bx * ca)


def scatter_grid(grid, n_bx, n_by, ca, cb, width):
    ny, count, lanes = grid.shape
    shaped = grid.reshape(n_by, cb, count, width, n_bx, ca)
    shaped = jnp.transpose(shaped, (4, 0, 3, 5, 1, 2))
    return shaped.reshape(n_bx * n_by, width * ca * cb, count)


def from_slices(received, ca, cb):
    src, rows, count = received.shape
    width = rows // (ca * cb)
    shaped = received.reshape(src * width, ca, cb, count)
    return jnp.transpose(shaped, (3, 1, 2, 0))


def lane_x(shape, nx):
    return lax.broadcasted_iota(jnp.int32, shape, len(shape) - 1) % nx


def skew(grid, steps, nx):
    ny = grid.shape[0]
    values = jnp.pad(grid, ((0, steps - ny), (0, 0), (0, 0)))
    x = lane_x(values.shape, nx)
    bit = 1
    while bit < nx:
        values = lax.optimization_barrier(values)
        moved = jnp.concatenate([jnp.zeros_like(values[:bit]), values[:-bit]], axis=0)
        values = jnp.where((x & bit) != 0, moved, values)
        bit *= 2
    return values


def skew_kernel(grid_ref, out_ref, *, nx):
    ny = grid_ref.shape[0]
    steps = out_ref.shape[0]
    out_ref[:ny] = grid_ref[...]
    out_ref[ny:] = jnp.zeros((steps - ny,) + out_ref.shape[1:], jnp.float32)
    x = lax.broadcasted_iota(jnp.int32, out_ref.shape[1:], 1) % nx
    unit = 1
    while unit < nx:
        ways = 4 if unit * 4 <= nx else 2
        part = (x // unit) % ways
        masks = [part == k for k in range(1, ways)]

        def pick(t, masks=masks, unit=unit, ways=ways):
            value = out_ref[t]
            for k in range(1, ways):
                if isinstance(t, int) and t < k * unit:
                    moved = jnp.zeros_like(value)
                else:
                    moved = out_ref[t - k * unit]
                value = jnp.where(masks[k - 1], moved, value)
            return value

        def body(i, carry, pick=pick):
            t = steps - 1 - i
            out_ref[t] = pick(t)
            return carry

        reach = (ways - 1) * unit
        lax.fori_loop(0, steps - reach, body, 0)
        for t in reversed(range(reach)):
            out_ref[t] = pick(t)
        unit *= ways


def skew_big(grid, steps, nx):
    ny, count, lanes = grid.shape
    return pl.pallas_call(
        functools.partial(skew_kernel, nx=nx),
        out_shape=jax.ShapeDtypeStruct((steps, count, lanes), jnp.float32),
    )(grid)


def unskew(values, ny, nx):
    x = lane_x(values.shape, nx)
    bit = 1
    while bit < nx:
        values = lax.optimization_barrier(values)
        moved = jnp.concatenate([values[bit:], jnp.zeros_like(values[:bit])], axis=0)
        values = jnp.where((x & bit) != 0, moved, values)
        bit *= 2
    return values[:ny]


def as_vectors(rows):
    return jnp.pad(rows, ((0, 0), (0, ROWS - rows.shape[1]), (0, 0)))


def as_matrices(rows, count):
    steps, _, lanes = rows.shape
    shaped = rows.reshape(steps, count, count, lanes)
    return jnp.pad(shaped, ((0, 0), (0, 0), (0, ROWS - count), (0, 0)))


def matvec(source, off, vector):
    count = vector.shape[1]
    return tree_sum([source[:, off + count * j : off + count * (j + 1), :] * vector[:, j : j + 1, :] for j in range(count)])


def shift_t(values, offset):
    zero = jnp.zeros_like(values[:1])
    if offset > 0:
        return jnp.concatenate([values[1:], zero], axis=0)
    return jnp.concatenate([zero, values[:-1]], axis=0)


def shift_x(values, offset, nx):
    x = lane_x(values.shape, nx)
    zero = jnp.zeros_like(values[..., :1])
    if offset > 0:
        moved = jnp.concatenate([values[..., 1:], zero], axis=-1)
        return jnp.where(x == nx - 1, 0.0, moved)
    moved = jnp.concatenate([zero, values[..., :-1]], axis=-1)
    return jnp.where(x == 0, 0.0, moved)


def shift_z(values, offset, nx, devices, count):
    rows = values.shape[1]
    if offset > 0:
        halo = lax.ppermute(values[:, :count, :nx], AXES, [(i + 1, i) for i in range(devices - 1)])
        halo = jnp.pad(halo, ((0, 0), (0, rows - count), (0, 0)))
        return jnp.concatenate([values[..., nx:], halo], axis=-1)
    halo = lax.ppermute(values[:, :count, -nx:], AXES, [(i, i + 1) for i in range(devices - 1)])
    halo = jnp.pad(halo, ((0, 0), (0, rows - count), (0, 0)))
    return jnp.concatenate([halo, values[..., :-nx]], axis=-1)


def tree_sum(terms):
    while len(terms) > 1:
        paired = [terms[i] + terms[i + 1] for i in range(0, len(terms) - 1, 2)]
        terms = paired + terms[len(paired) * 2 :]
    return terms[0]


def sweep_kernel(rhs_ref, *refs, forward, nx, count, places):
    out_ref = refs[-2]
    carry_ref = refs[-1]
    steps = rhs_ref.shape[0]
    lanes = rhs_ref.shape[2]
    x = lax.broadcasted_iota(jnp.int32, (count, lanes), 1) % nx
    if forward:
        keep = x > 0
        shift = 1
    else:
        keep = x < nx - 1
        shift = lanes - 1
    (kx_at, kx_off), (ky_at, ky_off), (inv_at, inv_off) = places

    @pl.when(pl.program_id(0) == 0)
    def _():
        carry_ref[...] = jnp.zeros((count, lanes), jnp.float32)

    def column(at, off, t, j):
        return refs[at][t, pl.ds(off + count * j, count), :]

    def step(s, fresh):
        t = s if forward else steps - 1 - s
        from_x = jnp.where(keep, pltpu.roll(fresh, shift, 1), 0.0)
        terms = [column(kx_at, kx_off, t, j) * from_x[j : j + 1, :] for j in range(count)]
        terms += [column(ky_at, ky_off, t, j) * fresh[j : j + 1, :] for j in range(count)]
        right = rhs_ref[t] - tree_sum(terms)
        result = tree_sum([column(inv_at, inv_off, t, j) * right[j : j + 1, :] for j in range(count)])
        out_ref[t] = result
        return result

    carry_ref[...] = lax.fori_loop(0, steps, step, carry_ref[...], unroll=2)


def sweep(rhs, sources, places, forward, nx, chunks=8):
    steps, count, lanes = rhs.shape
    size = steps // chunks
    if forward:
        where = lambda i: (i, 0, 0)
    else:
        where = lambda i: (chunks - 1 - i, 0, 0)
    kernel = functools.partial(sweep_kernel, forward=forward, nx=nx, count=count, places=places)
    specs = [pl.BlockSpec((size, count, lanes), where)]
    for source in sources:
        needed = max(off + count * count for at, off in places if sources[at] is source)
        rows = min(source.shape[1], -(-needed // ROWS) * ROWS)
        specs.append(pl.BlockSpec((size, rows, source.shape[2]), where))
    return pl.pallas_call(
        kernel,
        grid=(chunks,),
        in_specs=specs,
        out_specs=pl.BlockSpec((size, count, lanes), where),
        out_shape=jax.ShapeDtypeStruct(rhs.shape, jnp.float32),
        scratch_shapes=[pltpu.VMEM((count, lanes), jnp.float32)],
    )(rhs, *sources)


def per_device(
    adjoint_source,
    initial,
    inverses,
    couplings,
    interface_tiles,
    source_cells,
    target_cells,
    tile_counts,
):
    n_bx = lax.axis_size("bx")
    n_by = lax.axis_size("by")
    devices = n_bx * n_by
    count, ca, cb, nz = adjoint_source.shape
    nx, ny = n_bx * ca, n_by * cb
    width = nz // devices
    steps = nx + ny
    tables = (interface_tiles, source_cells, target_cells, tile_counts)

    def to_z(values, skewer=skew):
        received = lax.all_to_all(to_slices(values, devices), AXES, 0, 0, tiled=True)
        return skewer(gather_grid(received, n_bx, n_by, ca, cb, width), steps, nx)

    def to_xy(skewed):
        rows = ROWS
        grid = unskew(jnp.pad(skewed, ((0, 0), (0, rows - skewed.shape[1]), (0, 0))), ny, nx)
        lanes = grid.shape[2]
        chunks = grid.reshape(ny * rows, lanes).T
        chunks = chunks.reshape(width, n_bx, ca, n_by, cb * rows)
        chunks = jnp.transpose(chunks, (1, 3, 0, 2, 4)).reshape(devices, width * ca * cb * rows)
        received = lax.all_to_all(chunks, AXES, 0, 0, tiled=True)
        flat = received.reshape(devices * width, ca * cb * rows).T
        flat = flat.reshape(ca, cb, rows, nz)
        return jnp.transpose(flat, (2, 0, 1, 3))[:count]

    def small_to_z(values):
        padded = jnp.pad(values, ((0, ROWS - count), (0, 0), (0, 0), (0, 0)))
        flat = jnp.transpose(padded, (1, 2, 0, 3)).reshape(ca * cb * ROWS, nz)
        chunks = flat.T.reshape(devices, width * ca * cb * ROWS)
        received = lax.all_to_all(chunks, AXES, 0, 0, tiled=True)
        shaped = received.reshape(n_bx, n_by, width, ca, cb * ROWS)
        shaped = jnp.transpose(shaped, (2, 0, 3, 1, 4)).reshape(width * nx, ny * ROWS)
        return skew(shaped.T.reshape(ny, ROWS, width * nx), steps, nx)

    span = count * count
    sweep_rows = to_z(
        jnp.concatenate(
            [
                jnp.swapaxes(inverses, 0, 1).reshape(span, ca, cb, nz),
                jnp.swapaxes(couplings[0::2][:2], 1, 2).astype(jnp.float32).reshape(2 * span, ca, cb, nz),
            ],
            axis=0,
        ),
        skew_big,
    )
    base = adjoint_source - interface(initial, *tables)
    below = jnp.concatenate([jnp.zeros_like(initial[..., :1]), initial[..., :-1]], axis=-1)
    above = jnp.concatenate([initial[..., 1:], jnp.zeros_like(initial[..., :1])], axis=-1)
    along_z = couplings[4].astype(jnp.float32) * below[None] + couplings[5].astype(jnp.float32) * above[None]
    lower_base = base - jnp.sum(along_z, axis=1)
    other_rows = to_z(
        jnp.concatenate(
            [
                jnp.swapaxes(couplings[jnp.array([1, 3, 4, 5])], 1, 2).astype(jnp.float32).reshape(4 * span, ca, cb, nz),
                base,
                lower_base,
                initial,
            ],
            axis=0,
        ),
        skew_big,
    )
    base_z = other_rows[:, 4 * span : 4 * span + count]
    lower_z = other_rows[:, 4 * span + count : 4 * span + 2 * count]
    iterate = other_rows[:, 4 * span + 2 * count : 4 * span + 3 * count]
    forward_places = ((0, span), (0, 2 * span), (0, 0))
    backward_places = ((0, 0), (0, span), (1, 0))

    for number in range(ITERS):
        if number > 0:
            inter = interface(to_xy(iterate), *tables)
            base_z = small_to_z(adjoint_source - inter)[:, :count]
        in_plane = lax.optimization_barrier(
            matvec(other_rows, 0, shift_x(shift_t(iterate, 1), 1, nx))
            + matvec(other_rows, span, shift_t(iterate, 1))
        )
        if number > 0:
            lower_z = base_z - (
                matvec(other_rows, 2 * span, shift_z(iterate, -1, nx, devices, count))
                + matvec(other_rows, 3 * span, shift_z(iterate, 1, nx, devices, count))
            )
        lower_terms = lower_z - in_plane
        half = sweep(lower_terms, (sweep_rows,), forward_places, True, nx)
        in_plane = lax.optimization_barrier(
            matvec(sweep_rows, span, shift_x(shift_t(half, -1), -1, nx))
            + matvec(sweep_rows, 2 * span, shift_t(half, -1))
        )
        upper_terms = (base_z - in_plane) - (
            matvec(other_rows, 2 * span, shift_z(half, -1, nx, devices, count))
            + matvec(other_rows, 3 * span, shift_z(half, 1, nx, devices, count))
        )
        iterate = sweep(upper_terms, (other_rows, sweep_rows), backward_places, False, nx)
    return to_xy(iterate)


def solution(mesh):
    return jax.shard_map(
        per_device,
        mesh=mesh,
        in_specs=(
            P(None, "bx", "by", None),
            P(None, "bx", "by", None),
            P(None, None, "bx", "by", None),
            P(None, None, None, "bx", "by", None),
            P(AXES, None, None, None),
            P(AXES, None),
            P(AXES, None),
            P(AXES, None),
        ),
        out_specs=P(None, "bx", "by", None),
        check_vma=False,
    )
```

```python
import functools

import jax
import jax.numpy as jnp
from jax import lax
from jax.experimental import pallas as pl
from jax.experimental.pallas import tpu as pltpu
from jax.sharding import PartitionSpec as P

ITERS = 2
AXES = ("bx", "by")
ROWS = 8


def interface(iterate, interface_tiles, source_cells, target_cells, tile_counts):
    var_count = iterate.shape[0]
    flat_cells = iterate.reshape(var_count, -1)
    block_count = lax.axis_size("bx") * lax.axis_size("by")
    slot_count = source_cells.shape[1]
    per_pair = slot_count // block_count
    picked = jnp.take(flat_cells, source_cells[0], axis=1)
    products = jnp.sum(interface_tiles[0] * picked[None], axis=1)
    slot_ids = jnp.arange(slot_count, dtype=jnp.int32)
    limits = jnp.repeat(tile_counts[0], per_pair)
    products = jnp.where((slot_ids % per_pair)[None] < limits[None], products, 0.0)
    arrived = lax.all_to_all(products, AXES, split_axis=1, concat_axis=1, tiled=True)
    summed = jnp.zeros_like(flat_cells).at[:, target_cells[0]].add(arrived)
    return summed.reshape(iterate.shape)


def to_slices(values, devices):
    count, ca, cb, nz = values.shape
    shaped = jnp.transpose(values, (3, 1, 2, 0))
    return shaped.reshape(devices, (nz // devices) * ca * cb, count)


def gather_grid(received, n_bx, n_by, ca, cb, width):
    count = received.shape[2]
    shaped = received.reshape(n_bx, n_by, width, ca, cb, count)
    shaped = jnp.transpose(shaped, (1, 4, 5, 2, 0, 3))
    return shaped.reshape(n_by * cb, count, width * n_bx * ca)


def scatter_grid(grid, n_bx, n_by, ca, cb, width):
    ny, count, lanes = grid.shape
    shaped = grid.reshape(n_by, cb, count, width, n_bx, ca)
    shaped = jnp.transpose(shaped, (4, 0, 3, 5, 1, 2))
    return shaped.reshape(n_bx * n_by, width * ca * cb, count)


def from_slices(received, ca, cb):
    src, rows, count = received.shape
    width = rows // (ca * cb)
    shaped = received.reshape(src * width, ca, cb, count)
    return jnp.transpose(shaped, (3, 1, 2, 0))


def lane_x(shape, nx):
    return lax.broadcasted_iota(jnp.int32, shape, len(shape) - 1) % nx


def skew(grid, steps, nx):
    ny = grid.shape[0]
    values = jnp.pad(grid, ((0, steps - ny), (0, 0), (0, 0)))
    x = lane_x(values.shape, nx)
    bit = 1
    while bit < nx:
        values = lax.optimization_barrier(values)
        moved = jnp.concatenate([jnp.zeros_like(values[:bit]), values[:-bit]], axis=0)
        values = jnp.where((x & bit) != 0, moved, values)
        bit *= 2
    return values


def skew_kernel(grid_ref, out_ref, *, nx):
    ny = grid_ref.shape[0]
    steps = out_ref.shape[0]
    out_ref[:ny] = grid_ref[...]
    out_ref[ny:] = jnp.zeros((steps - ny,) + out_ref.shape[1:], jnp.float32)
    x = lax.broadcasted_iota(jnp.int32, out_ref.shape[1:], 1) % nx
    unit = 1
    while unit < nx:
        ways = 4 if unit * 4 <= nx else 2
        part = (x // unit) % ways
        masks = [part == k for k in range(1, ways)]

        def pick(t, masks=masks, unit=unit, ways=ways):
            value = out_ref[t]
            for k in range(1, ways):
                if isinstance(t, int) and t < k * unit:
                    moved = jnp.zeros_like(value)
                else:
                    moved = out_ref[t - k * unit]
                value = jnp.where(masks[k - 1], moved, value)
            return value

        def body(i, carry, pick=pick):
            t = steps - 1 - i
            out_ref[t] = pick(t)
            return carry

        reach = (ways - 1) * unit
        lax.fori_loop(0, steps - reach, body, 0)
        for t in reversed(range(reach)):
            out_ref[t] = pick(t)
        unit *= ways


def skew_big(grid, steps, nx):
    ny, count, lanes = grid.shape
    return pl.pallas_call(
        functools.partial(skew_kernel, nx=nx),
        out_shape=jax.ShapeDtypeStruct((steps, count, lanes), jnp.float32),
    )(grid)


def unskew(values, ny, nx):
    x = lane_x(values.shape, nx)
    bit = 1
    while bit < nx:
        values = lax.optimization_barrier(values)
        moved = jnp.concatenate([values[bit:], jnp.zeros_like(values[:bit])], axis=0)
        values = jnp.where((x & bit) != 0, moved, values)
        bit *= 2
    return values[:ny]


def as_vectors(rows):
    return jnp.pad(rows, ((0, 0), (0, ROWS - rows.shape[1]), (0, 0)))


def as_matrices(rows, count):
    steps, _, lanes = rows.shape
    shaped = rows.reshape(steps, count, count, lanes)
    return jnp.pad(shaped, ((0, 0), (0, 0), (0, ROWS - count), (0, 0)))


def matvec(source, off, vector):
    count = vector.shape[1]
    return tree_sum([source[:, off + count * j : off + count * (j + 1), :] * vector[:, j : j + 1, :] for j in range(count)])


def shift_t(values, offset):
    zero = jnp.zeros_like(values[:1])
    if offset > 0:
        return jnp.concatenate([values[1:], zero], axis=0)
    return jnp.concatenate([zero, values[:-1]], axis=0)


def shift_x(values, offset, nx):
    x = lane_x(values.shape, nx)
    zero = jnp.zeros_like(values[..., :1])
    if offset > 0:
        moved = jnp.concatenate([values[..., 1:], zero], axis=-1)
        return jnp.where(x == nx - 1, 0.0, moved)
    moved = jnp.concatenate([zero, values[..., :-1]], axis=-1)
    return jnp.where(x == 0, 0.0, moved)


def shift_z(values, offset, nx, devices, count):
    rows = values.shape[1]
    if offset > 0:
        halo = lax.ppermute(values[:, :count, :nx], AXES, [(i + 1, i) for i in range(devices - 1)])
        halo = jnp.pad(halo, ((0, 0), (0, rows - count), (0, 0)))
        return jnp.concatenate([values[..., nx:], halo], axis=-1)
    halo = lax.ppermute(values[:, :count, -nx:], AXES, [(i, i + 1) for i in range(devices - 1)])
    halo = jnp.pad(halo, ((0, 0), (0, rows - count), (0, 0)))
    return jnp.concatenate([halo, values[..., :-nx]], axis=-1)


def tree_sum(terms):
    while len(terms) > 1:
        paired = [terms[i] + terms[i + 1] for i in range(0, len(terms) - 1, 2)]
        terms = paired + terms[len(paired) * 2 :]
    return terms[0]


def sweep_kernel(rhs_ref, *refs, forward, nx, count, places):
    out_ref = refs[-2]
    carry_ref = refs[-1]
    steps = rhs_ref.shape[0]
    lanes = rhs_ref.shape[2]
    x = lax.broadcasted_iota(jnp.int32, (count, lanes), 1) % nx
    if forward:
        keep = x > 0
        shift = 1
    else:
        keep = x < nx - 1
        shift = lanes - 1
    (kx_at, kx_off), (ky_at, ky_off), (inv_at, inv_off) = places

    @pl.when(pl.program_id(0) == 0)
    def _():
        carry_ref[...] = jnp.zeros((count, lanes), jnp.float32)

    def column(at, off, t, j):
        return refs[at][t, pl.ds(off + count * j, count), :]

    def step(s, fresh):
        t = s if forward else steps - 1 - s
        from_x = jnp.where(keep, pltpu.roll(fresh, shift, 1), 0.0)
        terms = [column(kx_at, kx_off, t, j) * from_x[j : j + 1, :] for j in range(count)]
        terms += [column(ky_at, ky_off, t, j) * fresh[j : j + 1, :] for j in range(count)]
        right = rhs_ref[t] - tree_sum(terms)
        result = tree_sum([column(inv_at, inv_off, t, j) * right[j : j + 1, :] for j in range(count)])
        out_ref[t] = result
        return result

    carry_ref[...] = lax.fori_loop(0, steps, step, carry_ref[...], unroll=2)


def sweep(rhs, sources, places, forward, nx, chunks=4):
    steps, count, lanes = rhs.shape
    size = steps // chunks
    if forward:
        where = lambda i: (i, 0, 0)
    else:
        where = lambda i: (chunks - 1 - i, 0, 0)
    kernel = functools.partial(sweep_kernel, forward=forward, nx=nx, count=count, places=places)
    specs = [pl.BlockSpec((size, count, lanes), where)]
    for source in sources:
        needed = max(off + count * count for at, off in places if sources[at] is source)
        rows = min(source.shape[1], -(-needed // ROWS) * ROWS)
        specs.append(pl.BlockSpec((size, rows, source.shape[2]), where))
    return pl.pallas_call(
        kernel,
        grid=(chunks,),
        in_specs=specs,
        out_specs=pl.BlockSpec((size, count, lanes), where),
        out_shape=jax.ShapeDtypeStruct(rhs.shape, jnp.float32),
        scratch_shapes=[pltpu.VMEM((count, lanes), jnp.float32)],
    )(rhs, *sources)


def per_device(
    adjoint_source,
    initial,
    inverses,
    couplings,
    interface_tiles,
    source_cells,
    target_cells,
    tile_counts,
):
    n_bx = lax.axis_size("bx")
    n_by = lax.axis_size("by")
    devices = n_bx * n_by
    count, ca, cb, nz = adjoint_source.shape
    nx, ny = n_bx * ca, n_by * cb
    width = nz // devices
    steps = nx + ny
    tables = (interface_tiles, source_cells, target_cells, tile_counts)

    def to_z(values, skewer=skew):
        received = lax.all_to_all(to_slices(values, devices), AXES, 0, 0, tiled=True)
        return skewer(gather_grid(received, n_bx, n_by, ca, cb, width), steps, nx)

    def to_xy(skewed):
        rows = ROWS
        grid = unskew(jnp.pad(skewed, ((0, 0), (0, rows - skewed.shape[1]), (0, 0))), ny, nx)
        lanes = grid.shape[2]
        chunks = grid.reshape(ny * rows, lanes).T
        chunks = chunks.reshape(width, n_bx, ca, n_by, cb * rows)
        chunks = jnp.transpose(chunks, (1, 3, 0, 2, 4)).reshape(devices, width * ca * cb * rows)
        received = lax.all_to_all(chunks, AXES, 0, 0, tiled=True)
        flat = received.reshape(devices * width, ca * cb * rows).T
        flat = flat.reshape(ca, cb, rows, nz)
        return jnp.transpose(flat, (2, 0, 1, 3))[:count]

    def small_to_z(values):
        padded = jnp.pad(values, ((0, ROWS - count), (0, 0), (0, 0), (0, 0)))
        flat = jnp.transpose(padded, (1, 2, 0, 3)).reshape(ca * cb * ROWS, nz)
        chunks = flat.T.reshape(devices, width * ca * cb * ROWS)
        received = lax.all_to_all(chunks, AXES, 0, 0, tiled=True)
        shaped = received.reshape(n_bx, n_by, width, ca, cb * ROWS)
        shaped = jnp.transpose(shaped, (2, 0, 3, 1, 4)).reshape(width * nx, ny * ROWS)
        return skew(shaped.T.reshape(ny, ROWS, width * nx), steps, nx)

    span = count * count
    sweep_rows = to_z(
        jnp.concatenate(
            [
                jnp.swapaxes(inverses, 0, 1).reshape(span, ca, cb, nz),
                jnp.swapaxes(couplings[0::2][:2], 1, 2).astype(jnp.float32).reshape(2 * span, ca, cb, nz),
            ],
            axis=0,
        ),
        skew_big,
    )
    base = adjoint_source - interface(initial, *tables)
    below = jnp.concatenate([jnp.zeros_like(initial[..., :1]), initial[..., :-1]], axis=-1)
    above = jnp.concatenate([initial[..., 1:], jnp.zeros_like(initial[..., :1])], axis=-1)
    along_z = couplings[4].astype(jnp.float32) * below[None] + couplings[5].astype(jnp.float32) * above[None]
    lower_base = base - jnp.sum(along_z, axis=1)
    other_rows = to_z(
        jnp.concatenate(
            [
                jnp.swapaxes(couplings[jnp.array([1, 3, 4, 5])], 1, 2).astype(jnp.float32).reshape(4 * span, ca, cb, nz),
                base,
                lower_base,
                initial,
            ],
            axis=0,
        ),
        skew_big,
    )
    base_z = other_rows[:, 4 * span : 4 * span + count]
    lower_z = other_rows[:, 4 * span + count : 4 * span + 2 * count]
    iterate = other_rows[:, 4 * span + 2 * count : 4 * span + 3 * count]
    forward_places = ((0, span), (0, 2 * span), (0, 0))
    backward_places = ((0, 0), (0, span), (1, 0))

    for number in range(ITERS):
        if number > 0:
            inter = interface(to_xy(iterate), *tables)
            base_z = small_to_z(adjoint_source - inter)[:, :count]
        in_plane = (
            matvec(other_rows, 0, shift_x(shift_t(iterate, 1), 1, nx))
            + matvec(other_rows, span, shift_t(iterate, 1))
        )
        if number > 0:
            in_plane = lax.optimization_barrier(in_plane)
        if number > 0:
            lower_z = base_z - (
                matvec(other_rows, 2 * span, shift_z(iterate, -1, nx, devices, count))
                + matvec(other_rows, 3 * span, shift_z(iterate, 1, nx, devices, count))
            )
        lower_terms = lower_z - in_plane
        half = sweep(lower_terms, (sweep_rows,), forward_places, True, nx)
        in_plane = lax.optimization_barrier(
            matvec(sweep_rows, span, shift_x(shift_t(half, -1), -1, nx))
            + matvec(sweep_rows, 2 * span, shift_t(half, -1))
        )
        upper_terms = (base_z - in_plane) - (
            matvec(other_rows, 2 * span, shift_z(half, -1, nx, devices, count))
            + matvec(other_rows, 3 * span, shift_z(half, 1, nx, devices, count))
        )
        iterate = sweep(upper_terms, (other_rows, sweep_rows), backward_places, False, nx)
    return to_xy(iterate)


def solution(mesh):
    return jax.shard_map(
        per_device,
        mesh=mesh,
        in_specs=(
            P(None, "bx", "by", None),
            P(None, "bx", "by", None),
            P(None, None, "bx", "by", None),
            P(None, None, None, "bx", "by", None),
            P(AXES, None, None, None),
            P(AXES, None),
            P(AXES, None),
            P(AXES, None),
        ),
        out_specs=P(None, "bx", "by", None),
        check_vma=False,
    )
```
